256 devices in a mesh: seg: 8 (over z), blk: 32 (over x, y, core).
Axes of the slice: x: 4, y: 4, z: 8, core: 2. Of those that a mesh axis runs over, the one named last changes fastest.
Arguments:
- sampled_data: float32 [4, 256, 65536], P(None, None, ('seg', 'blk')), may hold values from -6 to 6
- update_weights: float32 [4, 256, 256], replicated, may hold values from -0.375 to 0.375
- eigenbasis_columns: float32 [4, 256, 256], replicated, may hold values from -0.375 to 0.375
- measuring_operator: float32 [4, 256, 256], replicated, may hold values from -0.375 to 0.375
- eigen_damping: float32 [256, 4, 128], P(('seg', 'blk')), may hold values from 0 to 1, as said below
- backward_damping: float32 [256, 4, 128], P(('seg', 'blk')), may hold values from 0 to 1, as said below
- rotation_angle: float32 [256, 4, 128], P(('seg', 'blk')), may hold values from 0.0105 to 0.21
- switch_flags: int32 [65536], P(('seg', 'blk')), may hold values 0 or 1
- prior_expectation: float32 [2, 4, 128], replicated, may hold values from -6 to 6
Outputs:
- states: bfloat16 [4, 256, 65536], P(None, None, ('seg', 'blk'))
- fitted: bfloat16 [4, 256, 65536], P(None, None, ('seg', 'blk'))
The draws below stay inside these ranges and needn't reach their ends.
Inputs may be any that keep to these rules, and one draw needn't show every extreme that they name: `eigen_damping`: positive decay rates per step. `backward_damping`: positive decay rates per step.
All inputs are finite; a program needn't handle non-finite values. No bound on the sum of `switch_flags` on one device may be relied on, other than what follows from the above.
Results may differ from the reference program's by a relative error of at most 0.0055.
Values sent between devices are 32-bit elements; how exact they have to be, the bound alone decides.
No kernel may reach another device: no remote copies, remote signals or barrier semaphores. Data moves between devices by JAX's collectives and lax.ppermute only.
A program may use at most 64 MiB of HBM per device.

```python
import math
import jax
import jax.numpy as jnp
from jax import lax

GRID_AREAS = 4
AREA_STATES = 256
SENSOR_CHANNELS = 256
PIECE_LENGTH = 256
MODES = 128
PIECE_COUNT = 256
SERIES_LENGTH = 65536


def rate_law(key):
    pick_key, slow_key, fast_key = jax.random.split(key, 3)
    grid_shape = (PIECE_COUNT, GRID_AREAS, MODES)
    fast_share = 0.5
    slow_rate = jnp.exp(jax.random.uniform(slow_key, grid_shape, minval=math.log(0.3), maxval=0.0)) / SERIES_LENGTH
    fast_rate = jnp.exp(jax.random.uniform(fast_key, grid_shape, minval=math.log(0.04), maxval=math.log(0.09)))
    chosen = jax.random.uniform(pick_key, (1, GRID_AREAS, MODES)) < fast_share
    return jnp.where(chosen, fast_rate, slow_rate).astype(jnp.float32)


def draw_eigen_damping(key, part):
    return rate_law(jax.random.fold_in(key, 11))


def draw_backward_damping(key, part):
    return rate_law(jax.random.fold_in(key, 23))


def set_ends(array, key, least, high):
    spot = [jax.random.randint(jax.random.fold_in(key, axis), (), 0, length) for axis, length in enumerate(array.shape)]
    widest = array.shape.index(max(array.shape))
    next_to = spot[:widest] + [(spot[widest] + 1) % array.shape[widest]] + spot[widest + 1:]
    return array.at[tuple(spot)].set(least).at[tuple(next_to)].set(high)


def steps_of(rng, dims, shards, smallest, high):
    loudness, own = 1.0, jax.random.fold_in(rng, 6)
    for dim, parts in shards:
        draws = jnp.exp(jax.random.uniform(jax.random.fold_in(own, dim), (parts,), jnp.float32, smallest / len(shards), high / len(shards)))
        loudness = loudness * jnp.repeat(draws, dims[dim] // parts).reshape([-1 if axis == dim else 1 for axis in range(len(dims))])
    return loudness


def normal_values(rng, extent, scale, limit, pieces=(), held_as=jnp.bfloat16):
    entries = jax.random.normal(rng, extent, jnp.float32) * scale
    if len(pieces) > 0:
        entries = steps_of(rng, extent, pieces, -0.22, 0.18) * entries
    return jnp.clip(entries, min=-limit, max=limit).astype(held_as)


def setup_inputs(seed: int = 0) -> dict:
    streams_of = jax.random.split(jax.random.key(seed), 10)
    sampled_data = normal_values(streams_of[0], (GRID_AREAS, SENSOR_CHANNELS, SERIES_LENGTH), 1.0, 6.0, ((2, 256),), jnp.float32)
    update_weights = normal_values(streams_of[1], (GRID_AREAS, AREA_STATES, SENSOR_CHANNELS), SENSOR_CHANNELS ** -0.5, 0.375, (), jnp.float32)
    eigenbasis_columns = normal_values(streams_of[2], (GRID_AREAS, AREA_STATES, AREA_STATES), AREA_STATES ** -0.5, 0.375, (), jnp.float32)
    measuring_operator = normal_values(streams_of[3], (GRID_AREAS, SENSOR_CHANNELS, AREA_STATES), AREA_STATES ** -0.5, 0.375, (), jnp.float32)
    eigen_damping = draw_eigen_damping(jax.random.fold_in(streams_of[9], 71), 0)
    backward_damping = draw_backward_damping(jax.random.fold_in(streams_of[9], 71), 0)
    rotation_angle = jnp.clip(0.0105 + 0.1995 * jax.random.uniform(streams_of[6], (PIECE_COUNT, GRID_AREAS, MODES), jnp.float32) ** steps_of(streams_of[6], (PIECE_COUNT, GRID_AREAS, MODES), ((0, 256),), -0.2, 0.2), 0.0105, 0.21)
    switch_flags = set_ends((jax.random.randint(streams_of[7], (SERIES_LENGTH,), 0, SERIES_LENGTH // 3) < 1).astype(jnp.int32), jax.random.fold_in(streams_of[7], 1), 0, 1)
    prior_expectation = normal_values(streams_of[8], (2, GRID_AREAS, MODES), 1.0, 6.0, (), jnp.float32)
    return dict(sampled_data=sampled_data, update_weights=update_weights, eigenbasis_columns=eigenbasis_columns, measuring_operator=measuring_operator, eigen_damping=eigen_damping, backward_damping=backward_damping, rotation_angle=rotation_angle, switch_flags=switch_flags, prior_expectation=prior_expectation)


spike_multiplier = 0.7

def compose(earlier, latter):
    growth_real, growth_imag, offset_real, offset_imag = earlier
    factor_real, factor_imag, addend_real, addend_imag = latter
    return (factor_real * growth_real - factor_imag * growth_imag, factor_real * growth_imag + factor_imag * growth_real, factor_real * offset_real - factor_imag * offset_imag + addend_real, factor_real * offset_imag + factor_imag * offset_real + addend_imag)

def reference(sampled_data, update_weights, eigenbasis_columns, measuring_operator, eigen_damping, backward_damping, rotation_angle, switch_flags, prior_expectation):
    highest = lax.Precision.HIGHEST
    noise_lines = switch_flags.reshape(PIECE_COUNT, PIECE_LENGTH)
    block_list = jnp.arange(PIECE_COUNT, dtype=jnp.int32)
    columns = jnp.arange(PIECE_LENGTH, dtype=jnp.int32)

    def block_inputs(block_number):
        local_readings = lax.dynamic_slice_in_dim(sampled_data, block_number * PIECE_LENGTH, PIECE_LENGTH, 2)
        jolt_moment = lax.dynamic_index_in_dim(noise_lines, block_number, 0, keepdims=False) == 1
        multiplier = jnp.where(jolt_moment, spike_multiplier, 1.0).astype(jnp.float32)
        logarithm_multiplier = jnp.where(jolt_moment, math.log(spike_multiplier), 0.0).astype(jnp.float32)
        forward_rate = lax.dynamic_index_in_dim(eigen_damping, block_number, 0, keepdims=False)
        backward_rate = lax.dynamic_index_in_dim(backward_damping, block_number, 0, keepdims=False)
        angle = lax.dynamic_index_in_dim(rotation_angle, block_number, 0, keepdims=False)
        return (local_readings, multiplier, logarithm_multiplier, forward_rate, backward_rate, angle)

    def forward(carried, block_number):
        local_readings, multiplier, logarithm_multiplier, forward_rate, backward_rate, angle = block_inputs(block_number)
        drive = jnp.einsum('asm,amt->ast', update_weights, local_readings, precision=highest)
        scaling = jnp.sqrt(-jnp.expm1(-2.0 * forward_rate))[:, :, None]
        magnitude = jnp.exp(-forward_rate)
        growth_real = (magnitude * jnp.cos(angle))[:, :, None] * multiplier
        growth_imag = (magnitude * jnp.sin(angle))[:, :, None] * multiplier
        local_scan = lax.associative_scan(compose, (growth_real, growth_imag, scaling * drive[:, :MODES], scaling * drive[:, MODES:]), axis=2)
        carry_real, carry_imag = carried
        mean_real = local_scan[0] * carry_real[:, :, None] - local_scan[1] * carry_imag[:, :, None] + local_scan[2]
        mean_imag = local_scan[0] * carry_imag[:, :, None] + local_scan[1] * carry_real[:, :, None] + local_scan[3]
        return ((mean_real[:, :, -1], mean_imag[:, :, -1]), jnp.stack([mean_real, mean_imag]))
    final_carry, means = lax.scan(forward, (prior_expectation[0], prior_expectation[1]), block_list)

    def backward(carried, block_number):
        local_readings, multiplier, logarithm_multiplier, forward_rate, backward_rate, angle = block_inputs(block_number)
        final_step = block_number * PIECE_LENGTH + columns == SERIES_LENGTH - 1
        magnitude = jnp.exp(-backward_rate)
        back_real = jnp.where(final_step, 0.0, (magnitude * jnp.cos(angle))[:, :, None] * multiplier)
        back_imag = jnp.where(final_step, 0.0, -(magnitude * jnp.sin(angle))[:, :, None] * multiplier)
        weight = jnp.where(final_step, 1.0, -jnp.expm1(2.0 * logarithm_multiplier - (forward_rate + backward_rate)[:, :, None]))
        block_means = lax.dynamic_index_in_dim(means, block_number, 0, keepdims=False)
        local_scan = lax.associative_scan(compose, (back_real, back_imag, weight * block_means[0], weight * block_means[1]), reverse=True, axis=2)
        entry_real, entry_imag = carried
        smooth_real = local_scan[0] * entry_real[:, :, None] - local_scan[1] * entry_imag[:, :, None] + local_scan[2]
        smooth_imag = local_scan[0] * entry_imag[:, :, None] + local_scan[1] * entry_real[:, :, None] + local_scan[3]
        stacked = jnp.concatenate([smooth_real, smooth_imag], axis=1)
        states = jnp.einsum('ars,ast->art', eigenbasis_columns, stacked, precision=highest).astype(jnp.bfloat16)
        fitted = (local_readings - jnp.einsum('ams,ast->amt', measuring_operator, stacked, precision=highest)).astype(jnp.bfloat16)
        return ((smooth_real[:, :, 0], smooth_imag[:, :, 0]), (states, fitted))
    empty = jnp.zeros((GRID_AREAS, MODES), jnp.float32)
    first_carry, output_values = lax.scan(backward, (empty, empty), block_list, reverse=True)
    states = jnp.transpose(output_values[0], (1, 2, 0, 3)).reshape(GRID_AREAS, AREA_STATES, SERIES_LENGTH)
    fitted = jnp.transpose(output_values[1], (1, 2, 0, 3)).reshape(GRID_AREAS, SENSOR_CHANNELS, SERIES_LENGTH)
    return (states, fitted)
```

```python
import math

import jax
import jax.numpy as jnp
from jax import lax
from jax.experimental import pallas as pl
from jax.experimental.pallas import tpu as pltpu
from jax.sharding import PartitionSpec as P

spike_multiplier = 0.7

VMEM = pltpu.VMEM
SMEM = pltpu.SMEM


def cmul(ar, ai, br, bi):
    return ar * br - ai * bi, ar * bi + ai * br


def factor_of(flag):
    return jnp.where(flag == 1, jnp.float32(spike_multiplier), jnp.float32(1.0))


def summary_kernel(flags_ref, last_ref, u_ref, par_ref, out_ref):
    steps = u_ref.shape[0]
    half = u_ref.shape[2] // 2
    lam_r, lam_i = par_ref[0], par_ref[1]
    bk_r, bk_i = par_ref[2], par_ref[3]
    w_plain, w_spike = par_ref[4], par_ref[5]
    zero = jnp.zeros_like(lam_r)
    one = jnp.ones_like(lam_r)

    def step(t, carry, final):
        mr, mi, ar, ai, pr, pi, qr, qi, hr, hi = carry
        flag = flags_ref[t]
        f = factor_of(flag)
        lr, li = f * lam_r, f * lam_i
        u = u_ref[t]
        mr, mi = lr * mr - li * mi + u[:, :half], lr * mi + li * mr + u[:, half:]
        ar, ai = cmul(lr, li, ar, ai)
        w = jnp.where(flag == 1, w_spike, w_plain)
        br, bi = f * bk_r, f * bk_i
        if final:
            last = last_ref[0] == 1
            w = jnp.where(last, one, w)
            br = jnp.where(last, zero, br)
            bi = jnp.where(last, zero, bi)
        wmr, wmi = w * mr, w * mi
        war, wai = w * ar, w * ai
        tr, ti = cmul(hr, hi, wmr, wmi)
        pr, pi = pr + tr, pi + ti
        tr, ti = cmul(hr, hi, war, wai)
        qr, qi = qr + tr, qi + ti
        hr, hi = cmul(br, bi, hr, hi)
        return (mr, mi, ar, ai, pr, pi, qr, qi, hr, hi)

    carry = (zero, zero, one, zero, zero, zero, zero, zero, one, zero)
    carry = lax.fori_loop(0, steps - 1, lambda t, c: step(t, c, False), carry, unroll=8)
    carry = step(steps - 1, carry, True)
    mr, mi, ar, ai, pr, pi, qr, qi, hr, hi = carry
    for idx, v in enumerate((ar, ai, mr, mi, hr, hi, pr, pi, qr, qi)):
        out_ref[idx] = v


def segment_kernel(me_ref, g_ref, tot_ref, mine_ref, al_r, al_i, be_r, be_i):
    count = g_ref.shape[0]
    me = me_ref[0]
    zero = jnp.zeros(g_ref.shape[2:], jnp.float32)
    one = jnp.ones_like(zero)

    ar, ai, br, bi = one, zero, zero, zero
    rec = [one, zero, zero, zero]
    for k in range(count):
        sel = me == k
        rec = [jnp.where(sel, v, r) for v, r in zip((ar, ai, br, bi), rec)]
        al_r[k], al_i[k], be_r[k], be_i[k] = ar, ai, br, bi
        Ar, Ai, Br, Bi = g_ref[k, 0], g_ref[k, 1], g_ref[k, 2], g_ref[k, 3]
        ar, ai = cmul(Ar, Ai, ar, ai)
        nr, ni = cmul(Ar, Ai, br, bi)
        br, bi = nr + Br, ni + Bi
    fwd_tot = (ar, ai, br, bi)
    fwd_me = rec

    gr, gi, pr, pi, kr, ki = one, zero, zero, zero, zero, zero
    rec = [one, zero, zero, zero, zero, zero]
    for k in reversed(range(count)):
        sel = me == k
        rec = [jnp.where(sel, v, r) for v, r in zip((gr, gi, pr, pi, kr, ki), rec)]
        Gr, Gi = g_ref[k, 4], g_ref[k, 5]
        Pr, Pi = g_ref[k, 6], g_ref[k, 7]
        Qr, Qi = g_ref[k, 8], g_ref[k, 9]
        xr, xi = cmul(Qr, Qi, be_r[k], be_i[k])
        yr, yi = cmul(Qr, Qi, al_r[k], al_i[k])
        gr, gi = cmul(Gr, Gi, gr, gi)
        nr, ni = cmul(Gr, Gi, pr, pi)
        pr, pi = nr + Pr + xr, ni + Pi + xi
        nr, ni = cmul(Gr, Gi, kr, ki)
        kr, ki = nr + yr, ni + yi
    bwd_tot = (gr, gi, pr, pi, kr, ki)
    bwd_me = rec
    for idx, v in enumerate(fwd_tot + bwd_tot):
        tot_ref[idx] = v
    for idx, v in enumerate(list(fwd_me) + list(bwd_me)):
        mine_ref[idx] = v


def final_kernel(flags_ref, last_ref, myseg_ref, tot_ref, mine_ref, prior_ref, u_ref, par_ref,
                 out_ref, m_r, m_i):
    steps = u_ref.shape[0]
    half = u_ref.shape[2] // 2
    segs = tot_ref.shape[0]
    myseg = myseg_ref[0]
    zero = jnp.zeros(par_ref.shape[1:], jnp.float32)
    one = jnp.ones_like(zero)

    cr, ci = prior_ref[0], prior_ref[1]
    c_in = []
    c_my = [zero, zero]
    for s in range(segs):
        c_in.append((cr, ci))
        sel = myseg == s
        c_my = [jnp.where(sel, cr, c_my[0]), jnp.where(sel, ci, c_my[1])]
        Ar, Ai, Br, Bi = tot_ref[s, 0], tot_ref[s, 1], tot_ref[s, 2], tot_ref[s, 3]
        nr, ni = cmul(Ar, Ai, cr, ci)
        cr, ci = nr + Br, ni + Bi
    er, ei = zero, zero
    e_my = [zero, zero]
    for s in reversed(range(segs)):
        sel = myseg == s
        e_my = [jnp.where(sel, er, e_my[0]), jnp.where(sel, ei, e_my[1])]
        Gr, Gi = tot_ref[s, 4], tot_ref[s, 5]
        Pr, Pi = tot_ref[s, 6], tot_ref[s, 7]
        Kr, Ki = tot_ref[s, 8], tot_ref[s, 9]
        nr, ni = cmul(Gr, Gi, er, ei)
        xr, xi = cmul(Kr, Ki, c_in[s][0], c_in[s][1])
        er, ei = nr + Pr + xr, ni + Pi + xi
    nr, ni = cmul(mine_ref[0], mine_ref[1], c_my[0], c_my[1])
    cr, ci = nr + mine_ref[2], ni + mine_ref[3]
    nr, ni = cmul(mine_ref[4], mine_ref[5], e_my[0], e_my[1])
    xr, xi = cmul(mine_ref[8], mine_ref[9], c_my[0], c_my[1])
    er, ei = nr + mine_ref[6] + xr, ni + mine_ref[7] + xi

    lam_r, lam_i = par_ref[0], par_ref[1]
    bk_r, bk_i = par_ref[2], par_ref[3]
    w_plain, w_spike = par_ref[4], par_ref[5]

    def fwd(t, carry):
        mr, mi = carry
        f = factor_of(flags_ref[t])
        lr, li = f * lam_r, f * lam_i
        u = u_ref[t]
        mr, mi = lr * mr - li * mi + u[:, :half], lr * mi + li * mr + u[:, half:]
        m_r[t] = mr
        m_i[t] = mi
        return (mr, mi)

    lax.fori_loop(0, steps, fwd, (cr, ci), unroll=8)

    def bwd_step(t, carry, final):
        sr, si = carry
        flag = flags_ref[t]
        f = factor_of(flag)
        w = jnp.where(flag == 1, w_spike, w_plain)
        br, bi = f * bk_r, f * bk_i
        if final:
            last = last_ref[0] == 1
            w = jnp.where(last, one, w)
            br = jnp.where(last, zero, br)
            bi = jnp.where(last, zero, bi)
        nr, ni = cmul(br, bi, sr, si)
        sr, si = nr + w * m_r[t], ni + w * m_i[t]
        out_ref[t, :, :half] = sr
        out_ref[t, :, half:] = si
        return (sr, si)

    carry = bwd_step(steps - 1, (er, ei), True)
    lax.fori_loop(0, steps - 1, lambda j, c: bwd_step(steps - 2 - j, c, False), carry, unroll=8)


def on_device(
    sampled_data,
    update_weights,
    eigenbasis_columns,
    measuring_operator,
    eigen_damping,
    backward_damping,
    rotation_angle,
    switch_flags,
    prior_expectation,
):
    highest = lax.Precision.HIGHEST
    steps = sampled_data.shape[2]
    seg_index = lax.axis_index("seg")
    blk_index = lax.axis_index("blk")
    last = ((seg_index == lax.axis_size("seg") - 1) & (blk_index == lax.axis_size("blk") - 1))
    last = last.astype(jnp.int32).reshape(1)
    flags = switch_flags.astype(jnp.int32)

    forward_rate = eigen_damping[0]
    backward_rate = backward_damping[0]
    angle = rotation_angle[0]
    magnitude = jnp.exp(-forward_rate)
    smooth_magnitude = jnp.exp(-backward_rate)
    both = forward_rate + backward_rate
    params = jnp.stack(
        [
            magnitude * jnp.cos(angle),
            magnitude * jnp.sin(angle),
            smooth_magnitude * jnp.cos(angle),
            -(smooth_magnitude * jnp.sin(angle)),
            -jnp.expm1(-both),
            -jnp.expm1(jnp.float32(2.0 * math.log(spike_multiplier)) - both),
        ]
    )
    scaling = jnp.sqrt(-jnp.expm1(-2.0 * forward_rate))
    scaling2 = jnp.concatenate([scaling, scaling], axis=1)
    drive = jnp.einsum("asm,amt->tas", update_weights, sampled_data, precision=highest)
    u = drive * scaling2[None]

    mode_shape = forward_rate.shape
    summary = pl.pallas_call(
        summary_kernel,
        out_shape=jax.ShapeDtypeStruct((10,) + mode_shape, jnp.float32),
        in_specs=[
            pl.BlockSpec(memory_space=SMEM),
            pl.BlockSpec(memory_space=SMEM),
            pl.BlockSpec(memory_space=VMEM),
            pl.BlockSpec(memory_space=VMEM),
        ],
        out_specs=pl.BlockSpec(memory_space=VMEM),
    )(flags, last, u, params)

    gathered = lax.all_gather(summary, "blk")
    count = gathered.shape[0]
    tot, mine = pl.pallas_call(
        segment_kernel,
        out_shape=(
            jax.ShapeDtypeStruct((10,) + mode_shape, jnp.float32),
            jax.ShapeDtypeStruct((10,) + mode_shape, jnp.float32),
        ),
        in_specs=[pl.BlockSpec(memory_space=SMEM), pl.BlockSpec(memory_space=VMEM)],
        out_specs=(pl.BlockSpec(memory_space=VMEM), pl.BlockSpec(memory_space=VMEM)),
        scratch_shapes=[pltpu.VMEM((count,) + mode_shape, jnp.float32) for _ in range(4)],
    )(blk_index.astype(jnp.int32).reshape(1), gathered)

    seg_tot = lax.all_gather(tot, "seg")
    stacked = pl.pallas_call(
        final_kernel,
        out_shape=jax.ShapeDtypeStruct(u.shape, jnp.float32),
        in_specs=[pl.BlockSpec(memory_space=SMEM)] * 3 + [pl.BlockSpec(memory_space=VMEM)] * 5,
        out_specs=pl.BlockSpec(memory_space=VMEM),
        scratch_shapes=[pltpu.VMEM((steps,) + mode_shape, jnp.float32) for _ in range(2)],
    )(flags, last, seg_index.astype(jnp.int32).reshape(1), seg_tot, mine, prior_expectation, u, params)

    states = jnp.einsum("ars,tas->art", eigenbasis_columns, stacked, precision=highest).astype(
        jnp.bfloat16
    )
    fitted = (
        sampled_data - jnp.einsum("ams,tas->amt", measuring_operator, stacked, precision=highest)
    ).astype(jnp.bfloat16)
    return (states, fitted)


def solution(mesh):
    placed = (
        P(None, None, ("seg", "blk")),
        P(),
        P(),
        P(),
        P(("seg", "blk"), None, None),
        P(("seg", "blk"), None, None),
        P(("seg", "blk"), None, None),
        P(("seg", "blk")),
        P(),
    )
    return jax.shard_map(
        on_device,
        mesh=mesh,
        in_specs=placed,
        out_specs=(P(None, None, ("seg", "blk")), P(None, None, ("seg", "blk"))),
        check_vma=False,
    )
```

```python
import math

import jax
import jax.numpy as jnp
from jax import lax
from jax.experimental import pallas as pl
from jax.experimental.pallas import tpu as pltpu
from jax.sharding import PartitionSpec as P

spike_multiplier = 0.7

VMEM = pltpu.VMEM
SMEM = pltpu.SMEM


def cmul(ar, ai, br, bi):
    return ar * br - ai * bi, ar * bi + ai * br


def factor_of(flag):
    return jnp.where(flag == 1, jnp.float32(spike_multiplier), jnp.float32(1.0))


def summary_kernel(flags_ref, last_ref, u_ref, par_ref, out_ref):
    steps = u_ref.shape[0]
    half = u_ref.shape[2] // 2
    lam_r, lam_i = par_ref[0], par_ref[1]
    bk_r, bk_i = par_ref[2], par_ref[3]
    w_plain, w_spike = par_ref[4], par_ref[5]
    scale = par_ref[6]
    zero = jnp.zeros_like(lam_r)
    one = jnp.ones_like(lam_r)

    def step(t, carry, final):
        mr, mi, ar, ai, pr, pi, qr, qi, hr, hi = carry
        flag = flags_ref[t]
        f = factor_of(flag)
        lr, li = f * lam_r, f * lam_i
        u = u_ref[t]
        mr, mi = lr * mr - li * mi + scale * u[:, :half], lr * mi + li * mr + scale * u[:, half:]
        ar, ai = cmul(lr, li, ar, ai)
        w = jnp.where(flag == 1, w_spike, w_plain)
        br, bi = f * bk_r, f * bk_i
        if final:
            last = last_ref[0] == 1
            w = jnp.where(last, one, w)
            br = jnp.where(last, zero, br)
            bi = jnp.where(last, zero, bi)
        wmr, wmi = w * mr, w * mi
        war, wai = w * ar, w * ai
        tr, ti = cmul(hr, hi, wmr, wmi)
        pr, pi = pr + tr, pi + ti
        tr, ti = cmul(hr, hi, war, wai)
        qr, qi = qr + tr, qi + ti
        hr, hi = cmul(br, bi, hr, hi)
        return (mr, mi, ar, ai, pr, pi, qr, qi, hr, hi)

    carry = (zero, zero, one, zero, zero, zero, zero, zero, one, zero)
    carry = lax.fori_loop(0, steps - 1, lambda t, c: step(t, c, False), carry, unroll=8)
    carry = step(steps - 1, carry, True)
    mr, mi, ar, ai, pr, pi, qr, qi, hr, hi = carry
    for idx, v in enumerate((ar, ai, mr, mi, hr, hi, pr, pi, qr, qi)):
        out_ref[idx] = v


def segment_kernel(me_ref, g_ref, tot_ref, mine_ref, al_r, al_i, be_r, be_i):
    count = g_ref.shape[0]
    me = me_ref[0]
    zero = jnp.zeros(g_ref.shape[2:], jnp.float32)
    one = jnp.ones_like(zero)

    ar, ai, br, bi = one, zero, zero, zero
    rec = [one, zero, zero, zero]
    for k in range(count):
        sel = me == k
        rec = [jnp.where(sel, v, r) for v, r in zip((ar, ai, br, bi), rec)]
        al_r[k], al_i[k], be_r[k], be_i[k] = ar, ai, br, bi
        Ar, Ai, Br, Bi = g_ref[k, 0], g_ref[k, 1], g_ref[k, 2], g_ref[k, 3]
        ar, ai = cmul(Ar, Ai, ar, ai)
        nr, ni = cmul(Ar, Ai, br, bi)
        br, bi = nr + Br, ni + Bi
    fwd_tot = (ar, ai, br, bi)
    fwd_me = rec

    gr, gi, pr, pi, kr, ki = one, zero, zero, zero, zero, zero
    rec = [one, zero, zero, zero, zero, zero]
    for k in reversed(range(count)):
        sel = me == k
        rec = [jnp.where(sel, v, r) for v, r in zip((gr, gi, pr, pi, kr, ki), rec)]
        Gr, Gi = g_ref[k, 4], g_ref[k, 5]
        Pr, Pi = g_ref[k, 6], g_ref[k, 7]
        Qr, Qi = g_ref[k, 8], g_ref[k, 9]
        xr, xi = cmul(Qr, Qi, be_r[k], be_i[k])
        yr, yi = cmul(Qr, Qi, al_r[k], al_i[k])
        gr, gi = cmul(Gr, Gi, gr, gi)
        nr, ni = cmul(Gr, Gi, pr, pi)
        pr, pi = nr + Pr + xr, ni + Pi + xi
        nr, ni = cmul(Gr, Gi, kr, ki)
        kr, ki = nr + yr, ni + yi
    bwd_tot = (gr, gi, pr, pi, kr, ki)
    bwd_me = rec
    for idx, v in enumerate(fwd_tot + bwd_tot):
        tot_ref[idx] = v
    for idx, v in enumerate(list(fwd_me) + list(bwd_me)):
        mine_ref[idx] = v


def final_kernel(flags_ref, last_ref, myseg_ref, tot_ref, mine_ref, prior_ref, u_ref, par_ref,
                 out_ref, m_r, m_i):
    steps = u_ref.shape[0]
    half = u_ref.shape[2] // 2
    segs = tot_ref.shape[0]
    myseg = myseg_ref[0]
    zero = jnp.zeros(par_ref.shape[1:], jnp.float32)
    one = jnp.ones_like(zero)

    cr, ci = prior_ref[0], prior_ref[1]
    c_in = []
    c_my = [zero, zero]
    for s in range(segs):
        c_in.append((cr, ci))
        sel = myseg == s
        c_my = [jnp.where(sel, cr, c_my[0]), jnp.where(sel, ci, c_my[1])]
        Ar, Ai, Br, Bi = tot_ref[s, 0], tot_ref[s, 1], tot_ref[s, 2], tot_ref[s, 3]
        nr, ni = cmul(Ar, Ai, cr, ci)
        cr, ci = nr + Br, ni + Bi
    er, ei = zero, zero
    e_my = [zero, zero]
    for s in reversed(range(segs)):
        sel = myseg == s
        e_my = [jnp.where(sel, er, e_my[0]), jnp.where(sel, ei, e_my[1])]
        Gr, Gi = tot_ref[s, 4], tot_ref[s, 5]
        Pr, Pi = tot_ref[s, 6], tot_ref[s, 7]
        Kr, Ki = tot_ref[s, 8], tot_ref[s, 9]
        nr, ni = cmul(Gr, Gi, er, ei)
        xr, xi = cmul(Kr, Ki, c_in[s][0], c_in[s][1])
        er, ei = nr + Pr + xr, ni + Pi + xi
    nr, ni = cmul(mine_ref[0], mine_ref[1], c_my[0], c_my[1])
    cr, ci = nr + mine_ref[2], ni + mine_ref[3]
    nr, ni = cmul(mine_ref[4], mine_ref[5], e_my[0], e_my[1])
    xr, xi = cmul(mine_ref[8], mine_ref[9], c_my[0], c_my[1])
    er, ei = nr + mine_ref[6] + xr, ni + mine_ref[7] + xi

    lam_r, lam_i = par_ref[0], par_ref[1]
    bk_r, bk_i = par_ref[2], par_ref[3]
    w_plain, w_spike = par_ref[4], par_ref[5]
    scale = par_ref[6]

    def fwd(t, carry):
        mr, mi = carry
        f = factor_of(flags_ref[t])
        lr, li = f * lam_r, f * lam_i
        u = u_ref[t]
        mr, mi = lr * mr - li * mi + scale * u[:, :half], lr * mi + li * mr + scale * u[:, half:]
        m_r[t] = mr
        m_i[t] = mi
        return (mr, mi)

    lax.fori_loop(0, steps, fwd, (cr, ci), unroll=8)

    def bwd_step(t, carry, final):
        sr, si = carry
        flag = flags_ref[t]
        f = factor_of(flag)
        w = jnp.where(flag == 1, w_spike, w_plain)
        br, bi = f * bk_r, f * bk_i
        if final:
            last = last_ref[0] == 1
            w = jnp.where(last, one, w)
            br = jnp.where(last, zero, br)
            bi = jnp.where(last, zero, bi)
        nr, ni = cmul(br, bi, sr, si)
        sr, si = nr + w * m_r[t], ni + w * m_i[t]
        out_ref[t, :, :half] = sr
        out_ref[t, :, half:] = si
        return (sr, si)

    carry = bwd_step(steps - 1, (er, ei), True)
    lax.fori_loop(0, steps - 1, lambda j, c: bwd_step(steps - 2 - j, c, False), carry, unroll=8)


def gathered_over(block, axis):
    count = lax.axis_size(axis)
    spread = jnp.broadcast_to(block[None], (count,) + block.shape)
    return lax.all_to_all(spread, axis, 0, 0, tiled=False)


def on_device(
    sampled_data,
    update_weights,
    eigenbasis_columns,
    measuring_operator,
    eigen_damping,
    backward_damping,
    rotation_angle,
    switch_flags,
    prior_expectation,
):
    highest = lax.Precision.HIGHEST
    steps = sampled_data.shape[2]
    seg_index = lax.axis_index("seg")
    blk_index = lax.axis_index("blk")
    last = ((seg_index == lax.axis_size("seg") - 1) & (blk_index == lax.axis_size("blk") - 1))
    last = last.astype(jnp.int32).reshape(1)
    flags = switch_flags.astype(jnp.int32)

    forward_rate = eigen_damping[0]
    backward_rate = backward_damping[0]
    angle = rotation_angle[0]
    magnitude = jnp.exp(-forward_rate)
    smooth_magnitude = jnp.exp(-backward_rate)
    both = forward_rate + backward_rate
    params = jnp.stack(
        [
            magnitude * jnp.cos(angle),
            magnitude * jnp.sin(angle),
            smooth_magnitude * jnp.cos(angle),
            -(smooth_magnitude * jnp.sin(angle)),
            -jnp.expm1(-both),
            -jnp.expm1(jnp.float32(2.0 * math.log(spike_multiplier)) - both),
        ]
    )
    scaling = jnp.sqrt(-jnp.expm1(-2.0 * forward_rate))
    u = jnp.einsum("asm,amt->tas", update_weights, sampled_data, precision=highest)
    params = jnp.concatenate([params, scaling[None]], axis=0)

    mode_shape = forward_rate.shape
    summary = pl.pallas_call(
        summary_kernel,
        out_shape=jax.ShapeDtypeStruct((10,) + mode_shape, jnp.float32),
        in_specs=[
            pl.BlockSpec(memory_space=SMEM),
            pl.BlockSpec(memory_space=SMEM),
            pl.BlockSpec(memory_space=VMEM),
            pl.BlockSpec(memory_space=VMEM),
        ],
        out_specs=pl.BlockSpec(memory_space=VMEM),
    )(flags, last, u, params)

    gathered = gathered_over(summary, "blk")
    count = gathered.shape[0]
    tot, mine = pl.pallas_call(
        segment_kernel,
        out_shape=(
            jax.ShapeDtypeStruct((10,) + mode_shape, jnp.float32),
            jax.ShapeDtypeStruct((10,) + mode_shape, jnp.float32),
        ),
        in_specs=[pl.BlockSpec(memory_space=SMEM), pl.BlockSpec(memory_space=VMEM)],
        out_specs=(pl.BlockSpec(memory_space=VMEM), pl.BlockSpec(memory_space=VMEM)),
        scratch_shapes=[pltpu.VMEM((count,) + mode_shape, jnp.float32) for _ in range(4)],
    )(blk_index.astype(jnp.int32).reshape(1), gathered)

    seg_tot = gathered_over(tot, "seg")
    stacked = pl.pallas_call(
        final_kernel,
        out_shape=jax.ShapeDtypeStruct(u.shape, jnp.float32),
        in_specs=[pl.BlockSpec(memory_space=SMEM)] * 3 + [pl.BlockSpec(memory_space=VMEM)] * 5,
        out_specs=pl.BlockSpec(memory_space=VMEM),
        scratch_shapes=[pltpu.VMEM((steps,) + mode_shape, jnp.float32) for _ in range(2)],
    )(flags, last, seg_index.astype(jnp.int32).reshape(1), seg_tot, mine, prior_expectation, u, params)

    states = jnp.einsum("ars,tas->art", eigenbasis_columns, stacked, precision=highest).astype(
        jnp.bfloat16
    )
    fitted = (
        sampled_data - jnp.einsum("ams,tas->amt", measuring_operator, stacked, precision=highest)
    ).astype(jnp.bfloat16)
    return (states, fitted)


def solution(mesh):
    placed = (
        P(None, None, ("seg", "blk")),
        P(),
        P(),
        P(),
        P(("seg", "blk"), None, None),
        P(("seg", "blk"), None, None),
        P(("seg", "blk"), None, None),
        P(("seg", "blk")),
        P(),
    )
    return jax.shard_map(
        on_device,
        mesh=mesh,
        in_specs=placed,
        out_specs=(P(None, None, ("seg", "blk")), P(None, None, ("seg", "blk"))),
        check_vma=False,
    )
```

```python
import math

import jax
import jax.numpy as jnp
from jax import lax
from jax.experimental import pallas as pl
from jax.experimental.pallas import tpu as pltpu
from jax.sharding import PartitionSpec as P

spike_multiplier = 0.7

VMEM = pltpu.VMEM
SMEM = pltpu.SMEM


def cmul(ar, ai, br, bi):
    return ar * br - ai * bi, ar * bi + ai * br


def factor_of(flag):
    return jnp.where(flag == 1, jnp.float32(spike_multiplier), jnp.float32(1.0))


def summary_kernel(flags_ref, last_ref, u_ref, par_ref, out_ref):
    steps = u_ref.shape[0]
    half = u_ref.shape[2] // 2
    lam_r, lam_i = par_ref[0], par_ref[1]
    bk_r, bk_i = par_ref[2], par_ref[3]
    w_plain, w_spike = par_ref[4], par_ref[5]
    scale = par_ref[6]
    zero = jnp.zeros_like(lam_r)
    one = jnp.ones_like(lam_r)

    def step(t, carry, final):
        mr, mi, ar, ai, pr, pi, qr, qi, hr, hi = carry
        flag = flags_ref[t]
        f = factor_of(flag)
        lr, li = f * lam_r, f * lam_i
        u = u_ref[t]
        mr, mi = lr * mr - li * mi + scale * u[:, :half], lr * mi + li * mr + scale * u[:, half:]
        ar, ai = cmul(lr, li, ar, ai)
        w = jnp.where(flag == 1, w_spike, w_plain)
        br, bi = f * bk_r, f * bk_i
        if final:
            last = last_ref[0] == 1
            w = jnp.where(last, one, w)
            br = jnp.where(last, zero, br)
            bi = jnp.where(last, zero, bi)
        wmr, wmi = w * mr, w * mi
        war, wai = w * ar, w * ai
        tr, ti = cmul(hr, hi, wmr, wmi)
        pr, pi = pr + tr, pi + ti
        tr, ti = cmul(hr, hi, war, wai)
        qr, qi = qr + tr, qi + ti
        hr, hi = cmul(br, bi, hr, hi)
        return (mr, mi, ar, ai, pr, pi, qr, qi, hr, hi)

    carry = (zero, zero, one, zero, zero, zero, zero, zero, one, zero)
    carry = lax.fori_loop(0, steps - 1, lambda t, c: step(t, c, False), carry, unroll=8)
    carry = step(steps - 1, carry, True)
    mr, mi, ar, ai, pr, pi, qr, qi, hr, hi = carry
    for idx, v in enumerate((ar, ai, mr, mi, hr, hi, pr, pi, qr, qi)):
        for k in range(out_ref.shape[0]):
            out_ref[k, idx] = v


def segment_kernel(me_ref, g_ref, tot_ref, mine_ref, al_r, al_i, be_r, be_i):
    count = g_ref.shape[0]
    me = me_ref[0]
    zero = jnp.zeros(g_ref.shape[2:], jnp.float32)
    one = jnp.ones_like(zero)

    ar, ai, br, bi = one, zero, zero, zero
    rec = [one, zero, zero, zero]
    for k in range(count):
        sel = me == k
        rec = [jnp.where(sel, v, r) for v, r in zip((ar, ai, br, bi), rec)]
        al_r[k], al_i[k], be_r[k], be_i[k] = ar, ai, br, bi
        Ar, Ai, Br, Bi = g_ref[k, 0], g_ref[k, 1], g_ref[k, 2], g_ref[k, 3]
        ar, ai = cmul(Ar, Ai, ar, ai)
        nr, ni = cmul(Ar, Ai, br, bi)
        br, bi = nr + Br, ni + Bi
    fwd_tot = (ar, ai, br, bi)
    fwd_me = rec

    gr, gi, pr, pi, kr, ki = one, zero, zero, zero, zero, zero
    rec = [one, zero, zero, zero, zero, zero]
    for k in reversed(range(count)):
        sel = me == k
        rec = [jnp.where(sel, v, r) for v, r in zip((gr, gi, pr, pi, kr, ki), rec)]
        Gr, Gi = g_ref[k, 4], g_ref[k, 5]
        Pr, Pi = g_ref[k, 6], g_ref[k, 7]
        Qr, Qi = g_ref[k, 8], g_ref[k, 9]
        xr, xi = cmul(Qr, Qi, be_r[k], be_i[k])
        yr, yi = cmul(Qr, Qi, al_r[k], al_i[k])
        gr, gi = cmul(Gr, Gi, gr, gi)
        nr, ni = cmul(Gr, Gi, pr, pi)
        pr, pi = nr + Pr + xr, ni + Pi + xi
        nr, ni = cmul(Gr, Gi, kr, ki)
        kr, ki = nr + yr, ni + yi
    bwd_tot = (gr, gi, pr, pi, kr, ki)
    bwd_me = rec
    for idx, v in enumerate(fwd_tot + bwd_tot):
        for s in range(tot_ref.shape[0]):
            tot_ref[s, idx] = v
    for idx, v in enumerate(list(fwd_me) + list(bwd_me)):
        mine_ref[idx] = v


def final_kernel(flags_ref, last_ref, myseg_ref, tot_ref, mine_ref, prior_ref, u_ref, par_ref,
                 out_ref, m_r, m_i):
    steps = u_ref.shape[0]
    half = u_ref.shape[2] // 2
    segs = tot_ref.shape[0]
    myseg = myseg_ref[0]
    zero = jnp.zeros(par_ref.shape[1:], jnp.float32)
    one = jnp.ones_like(zero)

    cr, ci = prior_ref[0], prior_ref[1]
    c_in = []
    c_my = [zero, zero]
    for s in range(segs):
        c_in.append((cr, ci))
        sel = myseg == s
        c_my = [jnp.where(sel, cr, c_my[0]), jnp.where(sel, ci, c_my[1])]
        Ar, Ai, Br, Bi = tot_ref[s, 0], tot_ref[s, 1], tot_ref[s, 2], tot_ref[s, 3]
        nr, ni = cmul(Ar, Ai, cr, ci)
        cr, ci = nr + Br, ni + Bi
    er, ei = zero, zero
    e_my = [zero, zero]
    for s in reversed(range(segs)):
        sel = myseg == s
        e_my = [jnp.where(sel, er, e_my[0]), jnp.where(sel, ei, e_my[1])]
        Gr, Gi = tot_ref[s, 4], tot_ref[s, 5]
        Pr, Pi = tot_ref[s, 6], tot_ref[s, 7]
        Kr, Ki = tot_ref[s, 8], tot_ref[s, 9]
        nr, ni = cmul(Gr, Gi, er, ei)
        xr, xi = cmul(Kr, Ki, c_in[s][0], c_in[s][1])
        er, ei = nr + Pr + xr, ni + Pi + xi
    nr, ni = cmul(mine_ref[0], mine_ref[1], c_my[0], c_my[1])
    cr, ci = nr + mine_ref[2], ni + mine_ref[3]
    nr, ni = cmul(mine_ref[4], mine_ref[5], e_my[0], e_my[1])
    xr, xi = cmul(mine_ref[8], mine_ref[9], c_my[0], c_my[1])
    er, ei = nr + mine_ref[6] + xr, ni + mine_ref[7] + xi

    lam_r, lam_i = par_ref[0], par_ref[1]
    bk_r, bk_i = par_ref[2], par_ref[3]
    w_plain, w_spike = par_ref[4], par_ref[5]
    scale = par_ref[6]

    def fwd(t, carry):
        mr, mi = carry
        f = factor_of(flags_ref[t])
        lr, li = f * lam_r, f * lam_i
        u = u_ref[t]
        mr, mi = lr * mr - li * mi + scale * u[:, :half], lr * mi + li * mr + scale * u[:, half:]
        m_r[t] = mr
        m_i[t] = mi
        return (mr, mi)

    lax.fori_loop(0, steps, fwd, (cr, ci), unroll=8)

    def bwd_step(t, carry, final):
        sr, si = carry
        flag = flags_ref[t]
        f = factor_of(flag)
        w = jnp.where(flag == 1, w_spike, w_plain)
        br, bi = f * bk_r, f * bk_i
        if final:
            last = last_ref[0] == 1
            w = jnp.where(last, one, w)
            br = jnp.where(last, zero, br)
            bi = jnp.where(last, zero, bi)
        nr, ni = cmul(br, bi, sr, si)
        sr, si = nr + w * m_r[t], ni + w * m_i[t]
        out_ref[t, :, :half] = sr
        out_ref[t, :, half:] = si
        return (sr, si)

    carry = bwd_step(steps - 1, (er, ei), True)
    lax.fori_loop(0, steps - 1, lambda j, c: bwd_step(steps - 2 - j, c, False), carry, unroll=8)


def gathered_over(spread, axis):
    return lax.all_to_all(spread, axis, 0, 0, tiled=False)


def on_device(
    sampled_data,
    update_weights,
    eigenbasis_columns,
    measuring_operator,
    eigen_damping,
    backward_damping,
    rotation_angle,
    switch_flags,
    prior_expectation,
):
    highest = lax.Precision.HIGH
    steps = sampled_data.shape[2]
    seg_index = lax.axis_index("seg")
    blk_index = lax.axis_index("blk")
    last = ((seg_index == lax.axis_size("seg") - 1) & (blk_index == lax.axis_size("blk") - 1))
    last = last.astype(jnp.int32).reshape(1)
    flags = switch_flags.astype(jnp.int32)

    forward_rate = eigen_damping[0]
    backward_rate = backward_damping[0]
    angle = rotation_angle[0]
    magnitude = jnp.exp(-forward_rate)
    smooth_magnitude = jnp.exp(-backward_rate)
    both = forward_rate + backward_rate
    params = jnp.stack(
        [
            magnitude * jnp.cos(angle),
            magnitude * jnp.sin(angle),
            smooth_magnitude * jnp.cos(angle),
            -(smooth_magnitude * jnp.sin(angle)),
            -jnp.expm1(-both),
            -jnp.expm1(jnp.float32(2.0 * math.log(spike_multiplier)) - both),
        ]
    )
    scaling = jnp.sqrt(-jnp.expm1(-2.0 * forward_rate))
    u = jnp.einsum("asm,amt->tas", update_weights, sampled_data, precision=highest)
    params = jnp.concatenate([params, scaling[None]], axis=0)

    mode_shape = forward_rate.shape
    summary = pl.pallas_call(
        summary_kernel,
        out_shape=jax.ShapeDtypeStruct((lax.axis_size("blk"), 10) + mode_shape, jnp.float32),
        in_specs=[
            pl.BlockSpec(memory_space=SMEM),
            pl.BlockSpec(memory_space=SMEM),
            pl.BlockSpec(memory_space=VMEM),
            pl.BlockSpec(memory_space=VMEM),
        ],
        out_specs=pl.BlockSpec(memory_space=VMEM),
    )(flags, last, u, params)

    gathered = gathered_over(summary, "blk")
    count = gathered.shape[0]
    tot, mine = pl.pallas_call(
        segment_kernel,
        out_shape=(
            jax.ShapeDtypeStruct((lax.axis_size("seg"), 10) + mode_shape, jnp.float32),
            jax.ShapeDtypeStruct((10,) + mode_shape, jnp.float32),
        ),
        in_specs=[pl.BlockSpec(memory_space=SMEM), pl.BlockSpec(memory_space=VMEM)],
        out_specs=(pl.BlockSpec(memory_space=VMEM), pl.BlockSpec(memory_space=VMEM)),
        scratch_shapes=[pltpu.VMEM((count,) + mode_shape, jnp.float32) for _ in range(4)],
    )(blk_index.astype(jnp.int32).reshape(1), gathered)

    seg_tot = gathered_over(tot, "seg")
    stacked = pl.pallas_call(
        final_kernel,
        out_shape=jax.ShapeDtypeStruct(u.shape, jnp.float32),
        in_specs=[pl.BlockSpec(memory_space=SMEM)] * 3 + [pl.BlockSpec(memory_space=VMEM)] * 5,
        out_specs=pl.BlockSpec(memory_space=VMEM),
        scratch_shapes=[pltpu.VMEM((steps,) + mode_shape, jnp.float32) for _ in range(2)],
    )(flags, last, seg_index.astype(jnp.int32).reshape(1), seg_tot, mine, prior_expectation, u, params)

    states = jnp.einsum("ars,tas->art", eigenbasis_columns, stacked, precision=highest).astype(
        jnp.bfloat16
    )
    fitted = (
        sampled_data - jnp.einsum("ams,tas->amt", measuring_operator, stacked, precision=highest)
    ).astype(jnp.bfloat16)
    return (states, fitted)


def solution(mesh):
    placed = (
        P(None, None, ("seg", "blk")),
        P(),
        P(),
        P(),
        P(("seg", "blk"), None, None),
        P(("seg", "blk"), None, None),
        P(("seg", "blk"), None, None),
        P(("seg", "blk")),
        P(),
    )
    return jax.shard_map(
        on_device,
        mesh=mesh,
        in_specs=placed,
        out_specs=(P(None, None, ("seg", "blk")), P(None, None, ("seg", "blk"))),
        check_vma=False,
    )
```

```python
import math

import jax
import jax.numpy as jnp
from jax import lax
from jax.experimental import pallas as pl
from jax.experimental.pallas import tpu as pltpu
from jax.sharding import PartitionSpec as P

spike_multiplier = 0.7

VMEM = pltpu.VMEM
SMEM = pltpu.SMEM


def cmul(ar, ai, br, bi):
    return ar * br - ai * bi, ar * bi + ai * br


def factor_of(flag):
    return jnp.where(flag == 1, jnp.float32(spike_multiplier), jnp.float32(1.0))


def fill_drive(w_ref, d_ref, u_ref):
    for a in range(w_ref.shape[0]):
        u_ref[:, a, :] = lax.dot_general(
            d_ref[a], w_ref[a], (((0,), (1,)), ((), ())),
            precision=lax.Precision.HIGHEST, preferred_element_type=jnp.float32)


def summary_kernel(flags_ref, last_ref, w_ref, d_ref, par_ref, out_ref, u_ref):
    fill_drive(w_ref, d_ref, u_ref)
    steps = u_ref.shape[0]
    half = u_ref.shape[2] // 2
    lam_r, lam_i = par_ref[0], par_ref[1]
    bk_r, bk_i = par_ref[2], par_ref[3]
    w_plain, w_spike = par_ref[4], par_ref[5]
    scale = par_ref[6]
    zero = jnp.zeros_like(lam_r)
    one = jnp.ones_like(lam_r)

    def step(t, carry, final):
        mr, mi, ar, ai, pr, pi, qr, qi, hr, hi = carry
        flag = flags_ref[t]
        f = factor_of(flag)
        lr, li = f * lam_r, f * lam_i
        u = u_ref[t]
        mr, mi = lr * mr - li * mi + scale * u[:, :half], lr * mi + li * mr + scale * u[:, half:]
        ar, ai = cmul(lr, li, ar, ai)
        w = jnp.where(flag == 1, w_spike, w_plain)
        br, bi = f * bk_r, f * bk_i
        if final:
            last = last_ref[0] == 1
            w = jnp.where(last, one, w)
            br = jnp.where(last, zero, br)
            bi = jnp.where(last, zero, bi)
        wmr, wmi = w * mr, w * mi
        war, wai = w * ar, w * ai
        tr, ti = cmul(hr, hi, wmr, wmi)
        pr, pi = pr + tr, pi + ti
        tr, ti = cmul(hr, hi, war, wai)
        qr, qi = qr + tr, qi + ti
        hr, hi = cmul(br, bi, hr, hi)
        return (mr, mi, ar, ai, pr, pi, qr, qi, hr, hi)

    carry = (zero, zero, one, zero, zero, zero, zero, zero, one, zero)
    carry = lax.fori_loop(0, steps - 1, lambda t, c: step(t, c, False), carry, unroll=8)
    carry = step(steps - 1, carry, True)
    mr, mi, ar, ai, pr, pi, qr, qi, hr, hi = carry
    for idx, v in enumerate((ar, ai, mr, mi, hr, hi, pr, pi, qr, qi)):
        for k in range(out_ref.shape[0]):
            out_ref[k, idx] = v


def segment_kernel(me_ref, g_ref, tot_ref, mine_ref, al_r, al_i, be_r, be_i):
    count = g_ref.shape[0]
    me = me_ref[0]
    zero = jnp.zeros(g_ref.shape[2:], jnp.float32)
    one = jnp.ones_like(zero)

    ar, ai, br, bi = one, zero, zero, zero
    rec = [one, zero, zero, zero]
    for k in range(count):
        sel = me == k
        rec = [jnp.where(sel, v, r) for v, r in zip((ar, ai, br, bi), rec)]
        al_r[k], al_i[k], be_r[k], be_i[k] = ar, ai, br, bi
        Ar, Ai, Br, Bi = g_ref[k, 0], g_ref[k, 1], g_ref[k, 2], g_ref[k, 3]
        ar, ai = cmul(Ar, Ai, ar, ai)
        nr, ni = cmul(Ar, Ai, br, bi)
        br, bi = nr + Br, ni + Bi
    fwd_tot = (ar, ai, br, bi)
    fwd_me = rec

    gr, gi, pr, pi, kr, ki = one, zero, zero, zero, zero, zero
    rec = [one, zero, zero, zero, zero, zero]
    for k in reversed(range(count)):
        sel = me == k
        rec = [jnp.where(sel, v, r) for v, r in zip((gr, gi, pr, pi, kr, ki), rec)]
        Gr, Gi = g_ref[k, 4], g_ref[k, 5]
        Pr, Pi = g_ref[k, 6], g_ref[k, 7]
        Qr, Qi = g_ref[k, 8], g_ref[k, 9]
        xr, xi = cmul(Qr, Qi, be_r[k], be_i[k])
        yr, yi = cmul(Qr, Qi, al_r[k], al_i[k])
        gr, gi = cmul(Gr, Gi, gr, gi)
        nr, ni = cmul(Gr, Gi, pr, pi)
        pr, pi = nr + Pr + xr, ni + Pi + xi
        nr, ni = cmul(Gr, Gi, kr, ki)
        kr, ki = nr + yr, ni + yi
    bwd_tot = (gr, gi, pr, pi, kr, ki)
    bwd_me = rec
    for idx, v in enumerate(fwd_tot + bwd_tot):
        for s in range(tot_ref.shape[0]):
            tot_ref[s, idx] = v
    for idx, v in enumerate(list(fwd_me) + list(bwd_me)):
        mine_ref[idx] = v


def final_kernel(flags_ref, last_ref, myseg_ref, tot_ref, mine_ref, prior_ref, w_ref, d_ref, e_ref,
                 o_ref, par_ref, states_ref, fitted_ref, u_ref, m_r, m_i, out_ref):
    fill_drive(w_ref, d_ref, u_ref)
    steps = u_ref.shape[0]
    half = u_ref.shape[2] // 2
    segs = tot_ref.shape[0]
    myseg = myseg_ref[0]
    zero = jnp.zeros(par_ref.shape[1:], jnp.float32)
    one = jnp.ones_like(zero)

    cr, ci = prior_ref[0], prior_ref[1]
    c_in = []
    c_my = [zero, zero]
    for s in range(segs):
        c_in.append((cr, ci))
        sel = myseg == s
        c_my = [jnp.where(sel, cr, c_my[0]), jnp.where(sel, ci, c_my[1])]
        Ar, Ai, Br, Bi = tot_ref[s, 0], tot_ref[s, 1], tot_ref[s, 2], tot_ref[s, 3]
        nr, ni = cmul(Ar, Ai, cr, ci)
        cr, ci = nr + Br, ni + Bi
    er, ei = zero, zero
    e_my = [zero, zero]
    for s in reversed(range(segs)):
        sel = myseg == s
        e_my = [jnp.where(sel, er, e_my[0]), jnp.where(sel, ei, e_my[1])]
        Gr, Gi = tot_ref[s, 4], tot_ref[s, 5]
        Pr, Pi = tot_ref[s, 6], tot_ref[s, 7]
        Kr, Ki = tot_ref[s, 8], tot_ref[s, 9]
        nr, ni = cmul(Gr, Gi, er, ei)
        xr, xi = cmul(Kr, Ki, c_in[s][0], c_in[s][1])
        er, ei = nr + Pr + xr, ni + Pi + xi
    nr, ni = cmul(mine_ref[0], mine_ref[1], c_my[0], c_my[1])
    cr, ci = nr + mine_ref[2], ni + mine_ref[3]
    nr, ni = cmul(mine_ref[4], mine_ref[5], e_my[0], e_my[1])
    xr, xi = cmul(mine_ref[8], mine_ref[9], c_my[0], c_my[1])
    er, ei = nr + mine_ref[6] + xr, ni + mine_ref[7] + xi

    lam_r, lam_i = par_ref[0], par_ref[1]
    bk_r, bk_i = par_ref[2], par_ref[3]
    w_plain, w_spike = par_ref[4], par_ref[5]
    scale = par_ref[6]

    def fwd(t, carry):
        mr, mi = carry
        f = factor_of(flags_ref[t])
        lr, li = f * lam_r, f * lam_i
        u = u_ref[t]
        mr, mi = lr * mr - li * mi + scale * u[:, :half], lr * mi + li * mr + scale * u[:, half:]
        m_r[t] = mr
        m_i[t] = mi
        return (mr, mi)

    lax.fori_loop(0, steps, fwd, (cr, ci), unroll=8)

    def bwd_step(t, carry, final):
        sr, si = carry
        flag = flags_ref[t]
        f = factor_of(flag)
        w = jnp.where(flag == 1, w_spike, w_plain)
        br, bi = f * bk_r, f * bk_i
        if final:
            last = last_ref[0] == 1
            w = jnp.where(last, one, w)
            br = jnp.where(last, zero, br)
            bi = jnp.where(last, zero, bi)
        nr, ni = cmul(br, bi, sr, si)
        sr, si = nr + w * m_r[t], ni + w * m_i[t]
        out_ref[t, :, :half] = sr
        out_ref[t, :, half:] = si
        return (sr, si)

    carry = bwd_step(steps - 1, (er, ei), True)
    lax.fori_loop(0, steps - 1, lambda j, c: bwd_step(steps - 2 - j, c, False), carry, unroll=8)

    contract = (((1,), (1,)), ((), ()))
    for a in range(e_ref.shape[0]):
        stacked = out_ref[:, a, :]
        states = lax.dot_general(e_ref[a], stacked, contract, precision=lax.Precision.HIGHEST,
                                 preferred_element_type=jnp.float32)
        states_ref[a] = states.astype(states_ref.dtype)
        seen = lax.dot_general(o_ref[a], stacked, contract, precision=lax.Precision.HIGHEST,
                               preferred_element_type=jnp.float32)
        fitted_ref[a] = (d_ref[a] - seen).astype(fitted_ref.dtype)


def gathered_over(spread, axis):
    return lax.all_to_all(spread, axis, 0, 0, tiled=False)


def on_device(
    sampled_data,
    update_weights,
    eigenbasis_columns,
    measuring_operator,
    eigen_damping,
    backward_damping,
    rotation_angle,
    switch_flags,
    prior_expectation,
):
    steps = sampled_data.shape[2]
    seg_index = lax.axis_index("seg")
    blk_index = lax.axis_index("blk")
    last = ((seg_index == lax.axis_size("seg") - 1) & (blk_index == lax.axis_size("blk") - 1))
    last = last.astype(jnp.int32).reshape(1)
    flags = switch_flags.astype(jnp.int32)

    forward_rate = eigen_damping[0]
    backward_rate = backward_damping[0]
    angle = rotation_angle[0]
    magnitude = jnp.exp(-forward_rate)
    smooth_magnitude = jnp.exp(-backward_rate)
    both = forward_rate + backward_rate
    params = jnp.stack(
        [
            magnitude * jnp.cos(angle),
            magnitude * jnp.sin(angle),
            smooth_magnitude * jnp.cos(angle),
            -(smooth_magnitude * jnp.sin(angle)),
            -jnp.expm1(-both),
            -jnp.expm1(jnp.float32(2.0 * math.log(spike_multiplier)) - both),
        ]
    )
    scaling = jnp.sqrt(-jnp.expm1(-2.0 * forward_rate))
    params = jnp.concatenate([params, scaling[None]], axis=0)
    u_shape = (steps, sampled_data.shape[0], sampled_data.shape[1])

    mode_shape = forward_rate.shape
    summary = pl.pallas_call(
        summary_kernel,
        out_shape=jax.ShapeDtypeStruct((lax.axis_size("blk"), 10) + mode_shape, jnp.float32),
        in_specs=[pl.BlockSpec(memory_space=SMEM)] * 2 + [pl.BlockSpec(memory_space=VMEM)] * 3,
        out_specs=pl.BlockSpec(memory_space=VMEM),
        scratch_shapes=[pltpu.VMEM(u_shape, jnp.float32)],
    )(flags, last, update_weights, sampled_data, params)

    gathered = gathered_over(summary, "blk")
    count = gathered.shape[0]
    tot, mine = pl.pallas_call(
        segment_kernel,
        out_shape=(
            jax.ShapeDtypeStruct((lax.axis_size("seg"), 10) + mode_shape, jnp.float32),
            jax.ShapeDtypeStruct((10,) + mode_shape, jnp.float32),
        ),
        in_specs=[pl.BlockSpec(memory_space=SMEM), pl.BlockSpec(memory_space=VMEM)],
        out_specs=(pl.BlockSpec(memory_space=VMEM), pl.BlockSpec(memory_space=VMEM)),
        scratch_shapes=[pltpu.VMEM((count,) + mode_shape, jnp.float32) for _ in range(4)],
    )(blk_index.astype(jnp.int32).reshape(1), gathered)

    seg_tot = gathered_over(tot, "seg")
    out_block = jax.ShapeDtypeStruct(sampled_data.shape, jnp.bfloat16)
    states, fitted = pl.pallas_call(
        final_kernel,
        out_shape=(out_block, out_block),
        in_specs=[pl.BlockSpec(memory_space=SMEM)] * 3 + [pl.BlockSpec(memory_space=VMEM)] * 8,
        out_specs=(pl.BlockSpec(memory_space=VMEM), pl.BlockSpec(memory_space=VMEM)),
        scratch_shapes=[pltpu.VMEM(u_shape, jnp.float32)]
        + [pltpu.VMEM((steps,) + mode_shape, jnp.float32) for _ in range(2)]
        + [pltpu.VMEM(u_shape, jnp.float32)],
    )(flags, last, seg_index.astype(jnp.int32).reshape(1), seg_tot, mine, prior_expectation,
      update_weights, sampled_data, eigenbasis_columns, measuring_operator, params)
    return (states, fitted)


def solution(mesh):
    placed = (
        P(None, None, ("seg", "blk")),
        P(),
        P(),
        P(),
        P(("seg", "blk"), None, None),
        P(("seg", "blk"), None, None),
        P(("seg", "blk"), None, None),
        P(("seg", "blk")),
        P(),
    )
    return jax.shard_map(
        on_device,
        mesh=mesh,
        in_specs=placed,
        out_specs=(P(None, None, ("seg", "blk")), P(None, None, ("seg", "blk"))),
        check_vma=False,
    )
```

```python
import math

import jax
import jax.numpy as jnp
from jax import lax
from jax.experimental import pallas as pl
from jax.experimental.pallas import tpu as pltpu
from jax.sharding import PartitionSpec as P

spike_multiplier = 0.7

VMEM = pltpu.VMEM
SMEM = pltpu.SMEM


def cmul(ar, ai, br, bi):
    return ar * br - ai * bi, ar * bi + ai * br


def factor_of(flag):
    return jnp.where(flag == 1, jnp.float32(spike_multiplier), jnp.float32(1.0))


def split_bf16(x):
    high = x.astype(jnp.bfloat16)
    low = (x - high.astype(jnp.float32)).astype(jnp.bfloat16)
    return high, low


def dot3(x, y, dims):
    xh, xl = split_bf16(x)
    yh, yl = split_bf16(y)

    def one(p, q):
        return lax.dot_general(p, q, dims, preferred_element_type=jnp.float32)

    return one(xh, yh) + (one(xh, yl) + one(xl, yh))


def fill_drive(w_ref, d_ref, u_ref):
    for a in range(w_ref.shape[0]):
        u_ref[:, a, :] = dot3(d_ref[a], w_ref[a], (((0,), (1,)), ((), ())))


def summary_kernel(flags_ref, last_ref, w_ref, d_ref, par_ref, out_ref, u_ref):
    fill_drive(w_ref, d_ref, u_ref)
    steps = u_ref.shape[0]
    half = u_ref.shape[2] // 2
    lam_r, lam_i = par_ref[0], par_ref[1]
    bk_r, bk_i = par_ref[2], par_ref[3]
    w_plain, w_spike = par_ref[4], par_ref[5]
    scale = par_ref[6]
    zero = jnp.zeros_like(lam_r)
    one = jnp.ones_like(lam_r)

    def step(t, carry, final):
        mr, mi, ar, ai, pr, pi, qr, qi, hr, hi = carry
        flag = flags_ref[t]
        f = factor_of(flag)
        lr, li = f * lam_r, f * lam_i
        u = u_ref[t]
        mr, mi = lr * mr - li * mi + scale * u[:, :half], lr * mi + li * mr + scale * u[:, half:]
        ar, ai = cmul(lr, li, ar, ai)
        w = jnp.where(flag == 1, w_spike, w_plain)
        br, bi = f * bk_r, f * bk_i
        if final:
            last = last_ref[0] == 1
            w = jnp.where(last, one, w)
            br = jnp.where(last, zero, br)
            bi = jnp.where(last, zero, bi)
        wmr, wmi = w * mr, w * mi
        war, wai = w * ar, w * ai
        tr, ti = cmul(hr, hi, wmr, wmi)
        pr, pi = pr + tr, pi + ti
        tr, ti = cmul(hr, hi, war, wai)
        qr, qi = qr + tr, qi + ti
        hr, hi = cmul(br, bi, hr, hi)
        return (mr, mi, ar, ai, pr, pi, qr, qi, hr, hi)

    carry = (zero, zero, one, zero, zero, zero, zero, zero, one, zero)
    carry = lax.fori_loop(0, steps - 1, lambda t, c: step(t, c, False), carry, unroll=8)
    carry = step(steps - 1, carry, True)
    mr, mi, ar, ai, pr, pi, qr, qi, hr, hi = carry
    for idx, v in enumerate((ar, ai, mr, mi, hr, hi, pr, pi, qr, qi)):
        for k in range(out_ref.shape[0]):
            out_ref[k, idx] = v


def segment_kernel(me_ref, g_ref, tot_ref, mine_ref, al_r, al_i, be_r, be_i):
    count = g_ref.shape[0]
    me = me_ref[0]
    zero = jnp.zeros(g_ref.shape[2:], jnp.float32)
    one = jnp.ones_like(zero)

    ar, ai, br, bi = one, zero, zero, zero
    rec = [one, zero, zero, zero]
    for k in range(count):
        sel = me == k
        rec = [jnp.where(sel, v, r) for v, r in zip((ar, ai, br, bi), rec)]
        al_r[k], al_i[k], be_r[k], be_i[k] = ar, ai, br, bi
        Ar, Ai, Br, Bi = g_ref[k, 0], g_ref[k, 1], g_ref[k, 2], g_ref[k, 3]
        ar, ai = cmul(Ar, Ai, ar, ai)
        nr, ni = cmul(Ar, Ai, br, bi)
        br, bi = nr + Br, ni + Bi
    fwd_tot = (ar, ai, br, bi)
    fwd_me = rec

    gr, gi, pr, pi, kr, ki = one, zero, zero, zero, zero, zero
    rec = [one, zero, zero, zero, zero, zero]
    for k in reversed(range(count)):
        sel = me == k
        rec = [jnp.where(sel, v, r) for v, r in zip((gr, gi, pr, pi, kr, ki), rec)]
        Gr, Gi = g_ref[k, 4], g_ref[k, 5]
        Pr, Pi = g_ref[k, 6], g_ref[k, 7]
        Qr, Qi = g_ref[k, 8], g_ref[k, 9]
        xr, xi = cmul(Qr, Qi, be_r[k], be_i[k])
        yr, yi = cmul(Qr, Qi, al_r[k], al_i[k])
        gr, gi = cmul(Gr, Gi, gr, gi)
        nr, ni = cmul(Gr, Gi, pr, pi)
        pr, pi = nr + Pr + xr, ni + Pi + xi
        nr, ni = cmul(Gr, Gi, kr, ki)
        kr, ki = nr + yr, ni + yi
    bwd_tot = (gr, gi, pr, pi, kr, ki)
    bwd_me = rec
    for idx, v in enumerate(fwd_tot + bwd_tot):
        for s in range(tot_ref.shape[0]):
            tot_ref[s, idx] = v
    for idx, v in enumerate(list(fwd_me) + list(bwd_me)):
        mine_ref[idx] = v


def final_kernel(flags_ref, last_ref, myseg_ref, tot_ref, mine_ref, prior_ref, w_ref, d_ref, e_hbm,
                 o_hbm, par_ref, states_ref, fitted_ref, u_ref, m_r, m_i, out_ref, e_ref, o_ref, sems):
    e_copy = pltpu.make_async_copy(e_hbm, e_ref, sems.at[0])
    o_copy = pltpu.make_async_copy(o_hbm, o_ref, sems.at[1])
    e_copy.start()
    o_copy.start()
    fill_drive(w_ref, d_ref, u_ref)
    steps = u_ref.shape[0]
    half = u_ref.shape[2] // 2
    segs = tot_ref.shape[0]
    myseg = myseg_ref[0]
    zero = jnp.zeros(par_ref.shape[1:], jnp.float32)
    one = jnp.ones_like(zero)

    cr, ci = prior_ref[0], prior_ref[1]
    c_in = []
    c_my = [zero, zero]
    for s in range(segs):
        c_in.append((cr, ci))
        sel = myseg == s
        c_my = [jnp.where(sel, cr, c_my[0]), jnp.where(sel, ci, c_my[1])]
        Ar, Ai, Br, Bi = tot_ref[s, 0], tot_ref[s, 1], tot_ref[s, 2], tot_ref[s, 3]
        nr, ni = cmul(Ar, Ai, cr, ci)
        cr, ci = nr + Br, ni + Bi
    er, ei = zero, zero
    e_my = [zero, zero]
    for s in reversed(range(segs)):
        sel = myseg == s
        e_my = [jnp.where(sel, er, e_my[0]), jnp.where(sel, ei, e_my[1])]
        Gr, Gi = tot_ref[s, 4], tot_ref[s, 5]
        Pr, Pi = tot_ref[s, 6], tot_ref[s, 7]
        Kr, Ki = tot_ref[s, 8], tot_ref[s, 9]
        nr, ni = cmul(Gr, Gi, er, ei)
        xr, xi = cmul(Kr, Ki, c_in[s][0], c_in[s][1])
        er, ei = nr + Pr + xr, ni + Pi + xi
    nr, ni = cmul(mine_ref[0], mine_ref[1], c_my[0], c_my[1])
    cr, ci = nr + mine_ref[2], ni + mine_ref[3]
    nr, ni = cmul(mine_ref[4], mine_ref[5], e_my[0], e_my[1])
    xr, xi = cmul(mine_ref[8], mine_ref[9], c_my[0], c_my[1])
    er, ei = nr + mine_ref[6] + xr, ni + mine_ref[7] + xi

    lam_r, lam_i = par_ref[0], par_ref[1]
    bk_r, bk_i = par_ref[2], par_ref[3]
    w_plain, w_spike = par_ref[4], par_ref[5]
    scale = par_ref[6]

    def fwd(t, carry):
        mr, mi = carry
        f = factor_of(flags_ref[t])
        lr, li = f * lam_r, f * lam_i
        u = u_ref[t]
        mr, mi = lr * mr - li * mi + scale * u[:, :half], lr * mi + li * mr + scale * u[:, half:]
        m_r[t] = mr
        m_i[t] = mi
        return (mr, mi)

    lax.fori_loop(0, steps, fwd, (cr, ci), unroll=8)

    def bwd_step(t, carry, final):
        sr, si = carry
        flag = flags_ref[t]
        f = factor_of(flag)
        w = jnp.where(flag == 1, w_spike, w_plain)
        br, bi = f * bk_r, f * bk_i
        if final:
            last = last_ref[0] == 1
            w = jnp.where(last, one, w)
            br = jnp.where(last, zero, br)
            bi = jnp.where(last, zero, bi)
        nr, ni = cmul(br, bi, sr, si)
        sr, si = nr + w * m_r[t], ni + w * m_i[t]
        out_ref[t, :, :half] = sr
        out_ref[t, :, half:] = si
        return (sr, si)

    carry = bwd_step(steps - 1, (er, ei), True)
    lax.fori_loop(0, steps - 1, lambda j, c: bwd_step(steps - 2 - j, c, False), carry, unroll=8)

    e_copy.wait()
    o_copy.wait()
    contract = (((1,), (1,)), ((), ()))
    for a in range(e_ref.shape[0]):
        stacked = out_ref[:, a, :]
        states = dot3(e_ref[a], stacked, contract)
        states_ref[a] = states.astype(states_ref.dtype)
        seen = dot3(o_ref[a], stacked, contract)
        fitted_ref[a] = (d_ref[a] - seen).astype(fitted_ref.dtype)


def gathered_over(spread, axis):
    return lax.all_to_all(spread, axis, 0, 0, tiled=False)


def on_device(
    sampled_data,
    update_weights,
    eigenbasis_columns,
    measuring_operator,
    eigen_damping,
    backward_damping,
    rotation_angle,
    switch_flags,
    prior_expectation,
):
    steps = sampled_data.shape[2]
    seg_index = lax.axis_index("seg")
    blk_index = lax.axis_index("blk")
    last = ((seg_index == lax.axis_size("seg") - 1) & (blk_index == lax.axis_size("blk") - 1))
    last = last.astype(jnp.int32).reshape(1)
    flags = switch_flags.astype(jnp.int32)

    forward_rate = eigen_damping[0]
    backward_rate = backward_damping[0]
    angle = rotation_angle[0]
    magnitude = jnp.exp(-forward_rate)
    smooth_magnitude = jnp.exp(-backward_rate)
    both = forward_rate + backward_rate
    params = jnp.stack(
        [
            magnitude * jnp.cos(angle),
            magnitude * jnp.sin(angle),
            smooth_magnitude * jnp.cos(angle),
            -(smooth_magnitude * jnp.sin(angle)),
            -jnp.expm1(-both),
            -jnp.expm1(jnp.float32(2.0 * math.log(spike_multiplier)) - both),
        ]
    )
    scaling = jnp.sqrt(-jnp.expm1(-2.0 * forward_rate))
    params = jnp.concatenate([params, scaling[None]], axis=0)
    u_shape = (steps, sampled_data.shape[0], sampled_data.shape[1])

    mode_shape = forward_rate.shape
    summary = pl.pallas_call(
        summary_kernel,
        out_shape=jax.ShapeDtypeStruct((lax.axis_size("blk"), 10) + mode_shape, jnp.float32),
        in_specs=[pl.BlockSpec(memory_space=SMEM)] * 2 + [pl.BlockSpec(memory_space=VMEM)] * 3,
        out_specs=pl.BlockSpec(memory_space=VMEM),
        scratch_shapes=[pltpu.VMEM(u_shape, jnp.float32)],
    )(flags, last, update_weights, sampled_data, params)

    gathered = gathered_over(summary, "blk")
    count = gathered.shape[0]
    tot, mine = pl.pallas_call(
        segment_kernel,
        out_shape=(
            jax.ShapeDtypeStruct((lax.axis_size("seg"), 10) + mode_shape, jnp.float32),
            jax.ShapeDtypeStruct((10,) + mode_shape, jnp.float32),
        ),
        in_specs=[pl.BlockSpec(memory_space=SMEM), pl.BlockSpec(memory_space=VMEM)],
        out_specs=(pl.BlockSpec(memory_space=VMEM), pl.BlockSpec(memory_space=VMEM)),
        scratch_shapes=[pltpu.VMEM((count,) + mode_shape, jnp.float32) for _ in range(4)],
    )(blk_index.astype(jnp.int32).reshape(1), gathered)

    seg_tot = gathered_over(tot, "seg")
    out_block = jax.ShapeDtypeStruct(sampled_data.shape, jnp.bfloat16)
    states, fitted = pl.pallas_call(
        final_kernel,
        out_shape=(out_block, out_block),
        in_specs=[pl.BlockSpec(memory_space=SMEM)] * 3 + [pl.BlockSpec(memory_space=VMEM)] * 5
        + [pl.BlockSpec(memory_space=pl.ANY)] * 2 + [pl.BlockSpec(memory_space=VMEM)],
        out_specs=(pl.BlockSpec(memory_space=VMEM), pl.BlockSpec(memory_space=VMEM)),
        scratch_shapes=[pltpu.VMEM(u_shape, jnp.float32)]
        + [pltpu.VMEM((steps,) + mode_shape, jnp.float32) for _ in range(2)]
        + [pltpu.VMEM(u_shape, jnp.float32)]
        + [pltpu.VMEM(eigenbasis_columns.shape, jnp.float32) for _ in range(2)]
        + [pltpu.SemaphoreType.DMA((2,))],
    )(flags, last, seg_index.astype(jnp.int32).reshape(1), seg_tot, mine, prior_expectation,
      update_weights, sampled_data, eigenbasis_columns, measuring_operator, params)
    return (states, fitted)


def solution(mesh):
    placed = (
        P(None, None, ("seg", "blk")),
        P(),
        P(),
        P(),
        P(("seg", "blk"), None, None),
        P(("seg", "blk"), None, None),
        P(("seg", "blk"), None, None),
        P(("seg", "blk")),
        P(),
    )
    return jax.shard_map(
        on_device,
        mesh=mesh,
        in_specs=placed,
        out_specs=(P(None, None, ("seg", "blk")), P(None, None, ("seg", "blk"))),
        check_vma=False,
    )
```

```python
import math

import jax
import jax.numpy as jnp
from jax import lax
from jax.experimental import pallas as pl
from jax.experimental.pallas import tpu as pltpu
from jax.sharding import PartitionSpec as P

spike_multiplier = 0.7

VMEM = pltpu.VMEM
SMEM = pltpu.SMEM
TUNED = pltpu.CompilerParams()


def cmul(ar, ai, br, bi):
    return ar * br - ai * bi, ar * bi + ai * br


def factor_of(flag):
    return jnp.where(flag == 1, jnp.float32(spike_multiplier), jnp.float32(1.0))


def split_bf16(x):
    high = x.astype(jnp.bfloat16)
    low = (x - high.astype(jnp.float32)).astype(jnp.bfloat16)
    return high, low


def dot3(x, y, dims):
    xh, xl = split_bf16(x)
    yh, yl = split_bf16(y)

    def one(p, q):
        return lax.dot_general(p, q, dims, preferred_element_type=jnp.float32)

    return one(xh, yh) + (one(xh, yl) + one(xl, yh))


def fill_drive(w_ref, d_ref, u_ref):
    for a in range(w_ref.shape[0]):
        u_ref[:, a, :] = dot3(d_ref[a], w_ref[a], (((0,), (1,)), ((), ())))


def summary_kernel(flags_ref, last_ref, w_ref, d_ref, par_ref, out_ref, u_ref):
    fill_drive(w_ref, d_ref, u_ref)
    steps = u_ref.shape[0]
    half = u_ref.shape[2] // 2
    lam_r, lam_i = par_ref[0], par_ref[1]
    bk_r, bk_i = par_ref[2], par_ref[3]
    w_plain, w_spike = par_ref[4], par_ref[5]
    scale = par_ref[6]
    zero = jnp.zeros_like(lam_r)
    one = jnp.ones_like(lam_r)

    def step(t, carry, final):
        mr, mi, ar, ai, pr, pi, qr, qi, hr, hi = carry
        flag = flags_ref[t]
        f = factor_of(flag)
        lr, li = f * lam_r, f * lam_i
        u = u_ref[t]
        mr, mi = lr * mr - li * mi + scale * u[:, :half], lr * mi + li * mr + scale * u[:, half:]
        ar, ai = cmul(lr, li, ar, ai)
        w = jnp.where(flag == 1, w_spike, w_plain)
        br, bi = f * bk_r, f * bk_i
        if final:
            last = last_ref[0] == 1
            w = jnp.where(last, one, w)
            br = jnp.where(last, zero, br)
            bi = jnp.where(last, zero, bi)
        wmr, wmi = w * mr, w * mi
        war, wai = w * ar, w * ai
        tr, ti = cmul(hr, hi, wmr, wmi)
        pr, pi = pr + tr, pi + ti
        tr, ti = cmul(hr, hi, war, wai)
        qr, qi = qr + tr, qi + ti
        hr, hi = cmul(br, bi, hr, hi)
        return (mr, mi, ar, ai, pr, pi, qr, qi, hr, hi)

    carry = (zero, zero, one, zero, zero, zero, zero, zero, one, zero)
    carry = lax.fori_loop(0, steps - 1, lambda t, c: step(t, c, False), carry, unroll=8)
    carry = step(steps - 1, carry, True)
    mr, mi, ar, ai, pr, pi, qr, qi, hr, hi = carry
    for idx, v in enumerate((ar, ai, mr, mi, hr, hi, pr, pi, qr, qi)):
        for k in range(out_ref.shape[0]):
            out_ref[k, idx] = v


def segment_kernel(me_ref, g_ref, tot_ref, mine_ref, al_r, al_i, be_r, be_i):
    count = g_ref.shape[0]
    me = me_ref[0]
    zero = jnp.zeros(g_ref.shape[2:], jnp.float32)
    one = jnp.ones_like(zero)

    ar, ai, br, bi = one, zero, zero, zero
    rec = [one, zero, zero, zero]
    for k in range(count):
        sel = me == k
        rec = [jnp.where(sel, v, r) for v, r in zip((ar, ai, br, bi), rec)]
        al_r[k], al_i[k], be_r[k], be_i[k] = ar, ai, br, bi
        Ar, Ai, Br, Bi = g_ref[k, 0], g_ref[k, 1], g_ref[k, 2], g_ref[k, 3]
        ar, ai = cmul(Ar, Ai, ar, ai)
        nr, ni = cmul(Ar, Ai, br, bi)
        br, bi = nr + Br, ni + Bi
    fwd_tot = (ar, ai, br, bi)
    fwd_me = rec

    gr, gi, pr, pi, kr, ki = one, zero, zero, zero, zero, zero
    rec = [one, zero, zero, zero, zero, zero]
    for k in reversed(range(count)):
        sel = me == k
        rec = [jnp.where(sel, v, r) for v, r in zip((gr, gi, pr, pi, kr, ki), rec)]
        Gr, Gi = g_ref[k, 4], g_ref[k, 5]
        Pr, Pi = g_ref[k, 6], g_ref[k, 7]
        Qr, Qi = g_ref[k, 8], g_ref[k, 9]
        xr, xi = cmul(Qr, Qi, be_r[k], be_i[k])
        yr, yi = cmul(Qr, Qi, al_r[k], al_i[k])
        gr, gi = cmul(Gr, Gi, gr, gi)
        nr, ni = cmul(Gr, Gi, pr, pi)
        pr, pi = nr + Pr + xr, ni + Pi + xi
        nr, ni = cmul(Gr, Gi, kr, ki)
        kr, ki = nr + yr, ni + yi
    bwd_tot = (gr, gi, pr, pi, kr, ki)
    bwd_me = rec
    for idx, v in enumerate(fwd_tot + bwd_tot):
        for s in range(tot_ref.shape[0]):
            tot_ref[s, idx] = v
    for idx, v in enumerate(list(fwd_me) + list(bwd_me)):
        mine_ref[idx] = v


def final_kernel(flags_ref, last_ref, myseg_ref, tot_ref, mine_ref, prior_ref, w_ref, d_ref, e_hbm,
                 o_hbm, par_ref, states_ref, fitted_ref, u_ref, m_r, m_i, out_ref, e_ref, o_ref, sems):
    e_copy = pltpu.make_async_copy(e_hbm, e_ref, sems.at[0])
    o_copy = pltpu.make_async_copy(o_hbm, o_ref, sems.at[1])
    e_copy.start()
    o_copy.start()
    fill_drive(w_ref, d_ref, u_ref)
    steps = u_ref.shape[0]
    half = u_ref.shape[2] // 2
    segs = tot_ref.shape[0]
    myseg = myseg_ref[0]
    zero = jnp.zeros(par_ref.shape[1:], jnp.float32)
    one = jnp.ones_like(zero)

    cr, ci = prior_ref[0], prior_ref[1]
    c_in = []
    c_my = [zero, zero]
    for s in range(segs):
        c_in.append((cr, ci))
        sel = myseg == s
        c_my = [jnp.where(sel, cr, c_my[0]), jnp.where(sel, ci, c_my[1])]
        Ar, Ai, Br, Bi = tot_ref[s, 0], tot_ref[s, 1], tot_ref[s, 2], tot_ref[s, 3]
        nr, ni = cmul(Ar, Ai, cr, ci)
        cr, ci = nr + Br, ni + Bi
    er, ei = zero, zero
    e_my = [zero, zero]
    for s in reversed(range(segs)):
        sel = myseg == s
        e_my = [jnp.where(sel, er, e_my[0]), jnp.where(sel, ei, e_my[1])]
        Gr, Gi = tot_ref[s, 4], tot_ref[s, 5]
        Pr, Pi = tot_ref[s, 6], tot_ref[s, 7]
        Kr, Ki = tot_ref[s, 8], tot_ref[s, 9]
        nr, ni = cmul(Gr, Gi, er, ei)
        xr, xi = cmul(Kr, Ki, c_in[s][0], c_in[s][1])
        er, ei = nr + Pr + xr, ni + Pi + xi
    nr, ni = cmul(mine_ref[0], mine_ref[1], c_my[0], c_my[1])
    cr, ci = nr + mine_ref[2], ni + mine_ref[3]
    nr, ni = cmul(mine_ref[4], mine_ref[5], e_my[0], e_my[1])
    xr, xi = cmul(mine_ref[8], mine_ref[9], c_my[0], c_my[1])
    er, ei = nr + mine_ref[6] + xr, ni + mine_ref[7] + xi

    lam_r, lam_i = par_ref[0], par_ref[1]
    bk_r, bk_i = par_ref[2], par_ref[3]
    w_plain, w_spike = par_ref[4], par_ref[5]
    scale = par_ref[6]

    def fwd(t, carry):
        mr, mi = carry
        f = factor_of(flags_ref[t])
        lr, li = f * lam_r, f * lam_i
        u = u_ref[t]
        mr, mi = lr * mr - li * mi + scale * u[:, :half], lr * mi + li * mr + scale * u[:, half:]
        m_r[t] = mr
        m_i[t] = mi
        return (mr, mi)

    lax.fori_loop(0, steps, fwd, (cr, ci), unroll=8)

    def bwd_step(t, carry, final):
        sr, si = carry
        flag = flags_ref[t]
        f = factor_of(flag)
        w = jnp.where(flag == 1, w_spike, w_plain)
        br, bi = f * bk_r, f * bk_i
        if final:
            last = last_ref[0] == 1
            w = jnp.where(last, one, w)
            br = jnp.where(last, zero, br)
            bi = jnp.where(last, zero, bi)
        nr, ni = cmul(br, bi, sr, si)
        sr, si = nr + w * m_r[t], ni + w * m_i[t]
        out_ref[t, :, :half] = sr
        out_ref[t, :, half:] = si
        return (sr, si)

    carry = bwd_step(steps - 1, (er, ei), True)
    lax.fori_loop(0, steps - 1, lambda j, c: bwd_step(steps - 2 - j, c, False), carry, unroll=8)

    e_copy.wait()
    o_copy.wait()
    contract = (((1,), (1,)), ((), ()))
    for a in range(e_ref.shape[0]):
        stacked = out_ref[:, a, :]
        states = dot3(e_ref[a], stacked, contract)
        states_ref[a] = states.astype(states_ref.dtype)
        seen = dot3(o_ref[a], stacked, contract)
        fitted_ref[a] = (d_ref[a] - seen).astype(fitted_ref.dtype)


def gathered_over(spread, axis):
    return lax.all_to_all(spread, axis, 0, 0, tiled=False)


def on_device(
    sampled_data,
    update_weights,
    eigenbasis_columns,
    measuring_operator,
    eigen_damping,
    backward_damping,
    rotation_angle,
    switch_flags,
    prior_expectation,
):
    steps = sampled_data.shape[2]
    seg_index = lax.axis_index("seg")
    blk_index = lax.axis_index("blk")
    last = ((seg_index == lax.axis_size("seg") - 1) & (blk_index == lax.axis_size("blk") - 1))
    last = last.astype(jnp.int32).reshape(1)
    flags = switch_flags.astype(jnp.int32)

    forward_rate = eigen_damping[0]
    backward_rate = backward_damping[0]
    angle = rotation_angle[0]
    magnitude = jnp.exp(-forward_rate)
    smooth_magnitude = jnp.exp(-backward_rate)
    both = forward_rate + backward_rate
    params = jnp.stack(
        [
            magnitude * jnp.cos(angle),
            magnitude * jnp.sin(angle),
            smooth_magnitude * jnp.cos(angle),
            -(smooth_magnitude * jnp.sin(angle)),
            -jnp.expm1(-both),
            -jnp.expm1(jnp.float32(2.0 * math.log(spike_multiplier)) - both),
        ]
    )
    scaling = jnp.sqrt(-jnp.expm1(-2.0 * forward_rate))
    params = jnp.concatenate([params, scaling[None]], axis=0)
    u_shape = (steps, sampled_data.shape[0], sampled_data.shape[1])

    mode_shape = forward_rate.shape
    summary = pl.pallas_call(
        summary_kernel,
        out_shape=jax.ShapeDtypeStruct((lax.axis_size("blk"), 10) + mode_shape, jnp.float32),
        in_specs=[pl.BlockSpec(memory_space=SMEM)] * 2 + [pl.BlockSpec(memory_space=VMEM)] * 3,
        out_specs=pl.BlockSpec(memory_space=VMEM),
        scratch_shapes=[pltpu.VMEM(u_shape, jnp.float32)],
        compiler_params=TUNED,
    )(flags, last, update_weights, sampled_data, params)

    gathered = gathered_over(summary, "blk")
    count = gathered.shape[0]
    tot, mine = pl.pallas_call(
        segment_kernel,
        out_shape=(
            jax.ShapeDtypeStruct((lax.axis_size("seg"), 10) + mode_shape, jnp.float32),
            jax.ShapeDtypeStruct((10,) + mode_shape, jnp.float32),
        ),
        in_specs=[pl.BlockSpec(memory_space=SMEM), pl.BlockSpec(memory_space=VMEM)],
        out_specs=(pl.BlockSpec(memory_space=VMEM), pl.BlockSpec(memory_space=VMEM)),
        scratch_shapes=[pltpu.VMEM((count,) + mode_shape, jnp.float32) for _ in range(4)],
        compiler_params=TUNED,
    )(blk_index.astype(jnp.int32).reshape(1), gathered)

    seg_tot = gathered_over(tot, "seg")
    out_block = jax.ShapeDtypeStruct(sampled_data.shape, jnp.bfloat16)
    states, fitted = pl.pallas_call(
        final_kernel,
        out_shape=(out_block, out_block),
        in_specs=[pl.BlockSpec(memory_space=SMEM)] * 3 + [pl.BlockSpec(memory_space=VMEM)] * 5
        + [pl.BlockSpec(memory_space=pl.ANY)] * 2 + [pl.BlockSpec(memory_space=VMEM)],
        out_specs=(pl.BlockSpec(memory_space=VMEM), pl.BlockSpec(memory_space=VMEM)),
        scratch_shapes=[pltpu.VMEM(u_shape, jnp.float32)]
        + [pltpu.VMEM((steps,) + mode_shape, jnp.float32) for _ in range(2)]
        + [pltpu.VMEM(u_shape, jnp.float32)]
        + [pltpu.VMEM(eigenbasis_columns.shape, jnp.float32) for _ in range(2)]
        + [pltpu.SemaphoreType.DMA((2,))],
        compiler_params=TUNED,
    )(flags, last, seg_index.astype(jnp.int32).reshape(1), seg_tot, mine, prior_expectation,
      update_weights, sampled_data, eigenbasis_columns, measuring_operator, params)
    return (states, fitted)


def solution(mesh):
    placed = (
        P(None, None, ("seg", "blk")),
        P(),
        P(),
        P(),
        P(("seg", "blk"), None, None),
        P(("seg", "blk"), None, None),
        P(("seg", "blk"), None, None),
        P(("seg", "blk")),
        P(),
    )
    return jax.shard_map(
        on_device,
        mesh=mesh,
        in_specs=placed,
        out_specs=(P(None, None, ("seg", "blk")), P(None, None, ("seg", "blk"))),
        check_vma=False,
    )
```

```python
import math

import jax
import jax.numpy as jnp
from jax import lax
from jax.experimental import pallas as pl
from jax.experimental.pallas import tpu as pltpu
from jax.sharding import PartitionSpec as P

spike_multiplier = 0.7

VMEM = pltpu.VMEM
SMEM = pltpu.SMEM


def cmul(ar, ai, br, bi):
    return ar * br - ai * bi, ar * bi + ai * br


def factor_of(flag):
    return jnp.where(flag == 1, jnp.float32(spike_multiplier), jnp.float32(1.0))


LOG_SPIKE_TWICE = 2.0 * math.log(spike_multiplier)


def expm1(x):
    small = jnp.abs(x) < 0.5
    xs = jnp.where(small, x, 0.0)
    p = jnp.ones_like(x)
    for k in range(12, 1, -1):
        p = 1.0 + (xs * jnp.float32(1.0 / k)) * p
    return jnp.where(small, xs * p, jnp.exp(x) - 1.0)


def mode_params(fd, bd, th):
    mag = jnp.exp(-fd)
    smag = jnp.exp(-bd)
    cos, sin = jnp.cos(th), jnp.sin(th)
    both = fd + bd
    return (
        mag * cos,
        mag * sin,
        smag * cos,
        -(smag * sin),
        -expm1(-both),
        -expm1(jnp.float32(LOG_SPIKE_TWICE) - both),
        jnp.sqrt(-expm1(-2.0 * fd)),
    )


def start_rate_copies(rate_hbm, rate_ref, sems, first):
    copies = [pltpu.make_async_copy(rate_hbm[i], rate_ref.at[i], sems.at[first + i]) for i in range(3)]
    for c in copies:
        c.start()
    return copies


def split_bf16(x):
    high = x.astype(jnp.bfloat16)
    low = (x - high.astype(jnp.float32)).astype(jnp.bfloat16)
    return high, low


def dot3(x, y, dims):
    xh, xl = split_bf16(x)
    yh, yl = split_bf16(y)

    def one(p, q):
        return lax.dot_general(p, q, dims, preferred_element_type=jnp.float32)

    return one(xh, yh) + (one(xh, yl) + one(xl, yh))


def fill_drive(w_ref, d_ref, u_ref):
    for a in range(w_ref.shape[0]):
        u_ref[:, a, :] = dot3(d_ref[a], w_ref[a], (((0,), (1,)), ((), ())))


def summary_kernel(flags_ref, last_ref, w_ref, d_ref, fd_hbm, bd_hbm, th_hbm, out_ref, u_ref,
                   rate_ref, sems):
    copies = start_rate_copies((fd_hbm, bd_hbm, th_hbm), rate_ref, sems, 0)
    fill_drive(w_ref, d_ref, u_ref)
    for c in copies:
        c.wait()
    steps = u_ref.shape[0]
    half = u_ref.shape[2] // 2
    lam_r, lam_i, bk_r, bk_i, w_plain, w_spike, scale = mode_params(
        rate_ref[0, 0], rate_ref[1, 0], rate_ref[2, 0])
    zero = jnp.zeros_like(lam_r)
    one = jnp.ones_like(lam_r)

    def step(t, carry, final):
        mr, mi, ar, ai, pr, pi, qr, qi, hr, hi = carry
        flag = flags_ref[t]
        f = factor_of(flag)
        lr, li = f * lam_r, f * lam_i
        u = u_ref[t]
        mr, mi = lr * mr - li * mi + scale * u[:, :half], lr * mi + li * mr + scale * u[:, half:]
        ar, ai = cmul(lr, li, ar, ai)
        w = jnp.where(flag == 1, w_spike, w_plain)
        br, bi = f * bk_r, f * bk_i
        if final:
            last = last_ref[0] == 1
            w = jnp.where(last, one, w)
            br = jnp.where(last, zero, br)
            bi = jnp.where(last, zero, bi)
        wmr, wmi = w * mr, w * mi
        war, wai = w * ar, w * ai
        tr, ti = cmul(hr, hi, wmr, wmi)
        pr, pi = pr + tr, pi + ti
        tr, ti = cmul(hr, hi, war, wai)
        qr, qi = qr + tr, qi + ti
        hr, hi = cmul(br, bi, hr, hi)
        return (mr, mi, ar, ai, pr, pi, qr, qi, hr, hi)

    carry = (zero, zero, one, zero, zero, zero, zero, zero, one, zero)
    carry = lax.fori_loop(0, steps - 1, lambda t, c: step(t, c, False), carry, unroll=8)
    carry = step(steps - 1, carry, True)
    mr, mi, ar, ai, pr, pi, qr, qi, hr, hi = carry
    for idx, v in enumerate((ar, ai, mr, mi, hr, hi, pr, pi, qr, qi)):
        for k in range(out_ref.shape[0]):
            out_ref[k, idx] = v


def segment_kernel(me_ref, g_ref, tot_ref, mine_ref, al_r, al_i, be_r, be_i):
    count = g_ref.shape[0]
    me = me_ref[0]
    zero = jnp.zeros(g_ref.shape[2:], jnp.float32)
    one = jnp.ones_like(zero)

    ar, ai, br, bi = one, zero, zero, zero
    rec = [one, zero, zero, zero]
    for k in range(count):
        sel = me == k
        rec = [jnp.where(sel, v, r) for v, r in zip((ar, ai, br, bi), rec)]
        al_r[k], al_i[k], be_r[k], be_i[k] = ar, ai, br, bi
        Ar, Ai, Br, Bi = g_ref[k, 0], g_ref[k, 1], g_ref[k, 2], g_ref[k, 3]
        ar, ai = cmul(Ar, Ai, ar, ai)
        nr, ni = cmul(Ar, Ai, br, bi)
        br, bi = nr + Br, ni + Bi
    fwd_tot = (ar, ai, br, bi)
    fwd_me = rec

    gr, gi, pr, pi, kr, ki = one, zero, zero, zero, zero, zero
    rec = [one, zero, zero, zero, zero, zero]
    for k in reversed(range(count)):
        sel = me == k
        rec = [jnp.where(sel, v, r) for v, r in zip((gr, gi, pr, pi, kr, ki), rec)]
        Gr, Gi = g_ref[k, 4], g_ref[k, 5]
        Pr, Pi = g_ref[k, 6], g_ref[k, 7]
        Qr, Qi = g_ref[k, 8], g_ref[k, 9]
        xr, xi = cmul(Qr, Qi, be_r[k], be_i[k])
        yr, yi = cmul(Qr, Qi, al_r[k], al_i[k])
        gr, gi = cmul(Gr, Gi, gr, gi)
        nr, ni = cmul(Gr, Gi, pr, pi)
        pr, pi = nr + Pr + xr, ni + Pi + xi
        nr, ni = cmul(Gr, Gi, kr, ki)
        kr, ki = nr + yr, ni + yi
    bwd_tot = (gr, gi, pr, pi, kr, ki)
    bwd_me = rec
    for idx, v in enumerate(fwd_tot + bwd_tot):
        for s in range(tot_ref.shape[0]):
            tot_ref[s, idx] = v
    for idx, v in enumerate(list(fwd_me) + list(bwd_me)):
        mine_ref[idx] = v


def final_kernel(flags_ref, last_ref, myseg_ref, tot_ref, mine_ref, prior_ref, w_ref, d_ref, e_hbm,
                 o_hbm, fd_hbm, bd_hbm, th_hbm, states_ref, fitted_ref, u_ref, m_r, m_i, out_ref, e_ref,
                 o_ref, rate_ref, sems):
    e_copy = pltpu.make_async_copy(e_hbm, e_ref, sems.at[0])
    o_copy = pltpu.make_async_copy(o_hbm, o_ref, sems.at[1])
    e_copy.start()
    o_copy.start()
    copies = start_rate_copies((fd_hbm, bd_hbm, th_hbm), rate_ref, sems, 2)
    fill_drive(w_ref, d_ref, u_ref)
    steps = u_ref.shape[0]
    half = u_ref.shape[2] // 2
    segs = tot_ref.shape[0]
    myseg = myseg_ref[0]
    zero = jnp.zeros(prior_ref.shape[1:], jnp.float32)
    one = jnp.ones_like(zero)

    cr, ci = prior_ref[0], prior_ref[1]
    c_in = []
    c_my = [zero, zero]
    for s in range(segs):
        c_in.append((cr, ci))
        sel = myseg == s
        c_my = [jnp.where(sel, cr, c_my[0]), jnp.where(sel, ci, c_my[1])]
        Ar, Ai, Br, Bi = tot_ref[s, 0], tot_ref[s, 1], tot_ref[s, 2], tot_ref[s, 3]
        nr, ni = cmul(Ar, Ai, cr, ci)
        cr, ci = nr + Br, ni + Bi
    er, ei = zero, zero
    e_my = [zero, zero]
    for s in reversed(range(segs)):
        sel = myseg == s
        e_my = [jnp.where(sel, er, e_my[0]), jnp.where(sel, ei, e_my[1])]
        Gr, Gi = tot_ref[s, 4], tot_ref[s, 5]
        Pr, Pi = tot_ref[s, 6], tot_ref[s, 7]
        Kr, Ki = tot_ref[s, 8], tot_ref[s, 9]
        nr, ni = cmul(Gr, Gi, er, ei)
        xr, xi = cmul(Kr, Ki, c_in[s][0], c_in[s][1])
        er, ei = nr + Pr + xr, ni + Pi + xi
    nr, ni = cmul(mine_ref[0], mine_ref[1], c_my[0], c_my[1])
    cr, ci = nr + mine_ref[2], ni + mine_ref[3]
    nr, ni = cmul(mine_ref[4], mine_ref[5], e_my[0], e_my[1])
    xr, xi = cmul(mine_ref[8], mine_ref[9], c_my[0], c_my[1])
    er, ei = nr + mine_ref[6] + xr, ni + mine_ref[7] + xi

    for c in copies:
        c.wait()
    lam_r, lam_i, bk_r, bk_i, w_plain, w_spike, scale = mode_params(
        rate_ref[0, 0], rate_ref[1, 0], rate_ref[2, 0])

    def fwd(t, carry):
        mr, mi = carry
        f = factor_of(flags_ref[t])
        lr, li = f * lam_r, f * lam_i
        u = u_ref[t]
        mr, mi = lr * mr - li * mi + scale * u[:, :half], lr * mi + li * mr + scale * u[:, half:]
        m_r[t] = mr
        m_i[t] = mi
        return (mr, mi)

    lax.fori_loop(0, steps, fwd, (cr, ci), unroll=8)

    def bwd_step(t, carry, final):
        sr, si = carry
        flag = flags_ref[t]
        f = factor_of(flag)
        w = jnp.where(flag == 1, w_spike, w_plain)
        br, bi = f * bk_r, f * bk_i
        if final:
            last = last_ref[0] == 1
            w = jnp.where(last, one, w)
            br = jnp.where(last, zero, br)
            bi = jnp.where(last, zero, bi)
        nr, ni = cmul(br, bi, sr, si)
        sr, si = nr + w * m_r[t], ni + w * m_i[t]
        out_ref[t, :, :half] = sr
        out_ref[t, :, half:] = si
        return (sr, si)

    carry = bwd_step(steps - 1, (er, ei), True)
    lax.fori_loop(0, steps - 1, lambda j, c: bwd_step(steps - 2 - j, c, False), carry, unroll=8)

    e_copy.wait()
    o_copy.wait()
    contract = (((1,), (1,)), ((), ()))
    for a in range(e_ref.shape[0]):
        stacked = out_ref[:, a, :]
        states = dot3(e_ref[a], stacked, contract)
        states_ref[a] = states.astype(states_ref.dtype)
        seen = dot3(o_ref[a], stacked, contract)
        fitted_ref[a] = (d_ref[a] - seen).astype(fitted_ref.dtype)


def gathered_over(spread, axis):
    return lax.all_to_all(spread, axis, 0, 0, tiled=False)


def on_device(
    sampled_data,
    update_weights,
    eigenbasis_columns,
    measuring_operator,
    eigen_damping,
    backward_damping,
    rotation_angle,
    switch_flags,
    prior_expectation,
):
    steps = sampled_data.shape[2]
    seg_index = lax.axis_index("seg")
    blk_index = lax.axis_index("blk")
    last = ((seg_index == lax.axis_size("seg") - 1) & (blk_index == lax.axis_size("blk") - 1))
    last = last.astype(jnp.int32).reshape(1)
    flags = switch_flags.astype(jnp.int32)

    u_shape = (steps, sampled_data.shape[0], sampled_data.shape[1])
    rates = (eigen_damping, backward_damping, rotation_angle)
    rate_scratch = pltpu.VMEM((3,) + eigen_damping.shape, jnp.float32)

    mode_shape = eigen_damping.shape[1:]
    summary = pl.pallas_call(
        summary_kernel,
        out_shape=jax.ShapeDtypeStruct((lax.axis_size("blk"), 10) + mode_shape, jnp.float32),
        in_specs=[pl.BlockSpec(memory_space=SMEM)] * 2 + [pl.BlockSpec(memory_space=VMEM)] * 2
        + [pl.BlockSpec(memory_space=pl.ANY)] * 3,
        out_specs=pl.BlockSpec(memory_space=VMEM),
        scratch_shapes=[pltpu.VMEM(u_shape, jnp.float32), rate_scratch, pltpu.SemaphoreType.DMA((3,))],
    )(flags, last, update_weights, sampled_data, *rates)

    gathered = gathered_over(summary, "blk")
    count = gathered.shape[0]
    tot, mine = pl.pallas_call(
        segment_kernel,
        out_shape=(
            jax.ShapeDtypeStruct((lax.axis_size("seg"), 10) + mode_shape, jnp.float32),
            jax.ShapeDtypeStruct((10,) + mode_shape, jnp.float32),
        ),
        in_specs=[pl.BlockSpec(memory_space=SMEM), pl.BlockSpec(memory_space=VMEM)],
        out_specs=(pl.BlockSpec(memory_space=VMEM), pl.BlockSpec(memory_space=VMEM)),
        scratch_shapes=[pltpu.VMEM((count,) + mode_shape, jnp.float32) for _ in range(4)],
    )(blk_index.astype(jnp.int32).reshape(1), gathered)

    seg_tot = gathered_over(tot, "seg")
    out_block = jax.ShapeDtypeStruct(sampled_data.shape, jnp.bfloat16)
    states, fitted = pl.pallas_call(
        final_kernel,
        out_shape=(out_block, out_block),
        in_specs=[pl.BlockSpec(memory_space=SMEM)] * 3 + [pl.BlockSpec(memory_space=VMEM)] * 5
        + [pl.BlockSpec(memory_space=pl.ANY)] * 5,
        out_specs=(pl.BlockSpec(memory_space=VMEM), pl.BlockSpec(memory_space=VMEM)),
        scratch_shapes=[pltpu.VMEM(u_shape, jnp.float32)]
        + [pltpu.VMEM((steps,) + mode_shape, jnp.float32) for _ in range(2)]
        + [pltpu.VMEM(u_shape, jnp.float32)]
        + [pltpu.VMEM(eigenbasis_columns.shape, jnp.float32) for _ in range(2)]
        + [rate_scratch, pltpu.SemaphoreType.DMA((5,))],
    )(flags, last, seg_index.astype(jnp.int32).reshape(1), seg_tot, mine, prior_expectation,
      update_weights, sampled_data, eigenbasis_columns, measuring_operator, *rates)
    return (states, fitted)


def solution(mesh):
    placed = (
        P(None, None, ("seg", "blk")),
        P(),
        P(),
        P(),
        P(("seg", "blk"), None, None),
        P(("seg", "blk"), None, None),
        P(("seg", "blk"), None, None),
        P(("seg", "blk")),
        P(),
    )
    return jax.shard_map(
        on_device,
        mesh=mesh,
        in_specs=placed,
        out_specs=(P(None, None, ("seg", "blk")), P(None, None, ("seg", "blk"))),
        check_vma=False,
    )
```

```python
import math

import jax
import jax.numpy as jnp
from jax import lax
from jax.experimental import pallas as pl
from jax.experimental.pallas import tpu as pltpu
from jax.sharding import PartitionSpec as P

spike_multiplier = 0.7

VMEM = pltpu.VMEM
SMEM = pltpu.SMEM


def cmul(ar, ai, br, bi):
    return ar * br - ai * bi, ar * bi + ai * br


def factor_of(flag):
    return jnp.where(flag == 1, jnp.float32(spike_multiplier), jnp.float32(1.0))


LOG_SPIKE_TWICE = 2.0 * math.log(spike_multiplier)


def expm1(x):
    small = jnp.abs(x) < 0.5
    xs = jnp.where(small, x, 0.0)
    p = jnp.ones_like(x)
    for k in range(12, 1, -1):
        p = 1.0 + (xs * jnp.float32(1.0 / k)) * p
    return jnp.where(small, xs * p, jnp.exp(x) - 1.0)


def mode_params(fd, bd, th):
    mag = jnp.exp(-fd)
    smag = jnp.exp(-bd)
    cos, sin = jnp.cos(th), jnp.sin(th)
    both = fd + bd
    return (
        mag * cos,
        mag * sin,
        smag * cos,
        -(smag * sin),
        -expm1(-both),
        -expm1(jnp.float32(LOG_SPIKE_TWICE) - both),
        jnp.sqrt(-expm1(-2.0 * fd)),
    )


def start_rate_copies(rate_hbm, rate_ref, sems, first):
    copies = [pltpu.make_async_copy(rate_hbm[i], rate_ref.at[i], sems.at[first + i]) for i in range(3)]
    for c in copies:
        c.start()
    return copies


def split_bf16(x):
    high = x.astype(jnp.bfloat16)
    low = (x - high.astype(jnp.float32)).astype(jnp.bfloat16)
    return high, low


def dot3(x, y, dims):
    xh, xl = split_bf16(x)
    yh, yl = split_bf16(y)

    def one(p, q):
        return lax.dot_general(p, q, dims, preferred_element_type=jnp.float32)

    return one(xh, yh) + (one(xh, yl) + one(xl, yh))


def start_input_copies(w_hbm, d_hbm, w_ref, d_ref, sems, first):
    copies = []
    for a in range(w_ref.shape[0]):
        pair = (pltpu.make_async_copy(w_hbm.at[a], w_ref.at[a], sems.at[first + 2 * a]),
                pltpu.make_async_copy(d_hbm.at[a], d_ref.at[a], sems.at[first + 2 * a + 1]))
        for c in pair:
            c.start()
        copies.append(pair)
    return copies


def fill_drive(w_ref, d_ref, u_ref, copies):
    for a in range(w_ref.shape[0]):
        for c in copies[a]:
            c.wait()
        u_ref[:, a, :] = dot3(d_ref[a], w_ref[a], (((0,), (1,)), ((), ())))


def summary_kernel(flags_ref, last_ref, w_hbm, d_hbm, fd_hbm, bd_hbm, th_hbm, out_ref, u_ref,
                   rate_ref, w_ref, d_ref, sems):
    inputs = start_input_copies(w_hbm, d_hbm, w_ref, d_ref, sems, 3)
    copies = start_rate_copies((fd_hbm, bd_hbm, th_hbm), rate_ref, sems, 0)
    fill_drive(w_ref, d_ref, u_ref, inputs)
    for c in copies:
        c.wait()
    steps = u_ref.shape[0]
    half = u_ref.shape[2] // 2
    lam_r, lam_i, bk_r, bk_i, w_plain, w_spike, scale = mode_params(
        rate_ref[0, 0], rate_ref[1, 0], rate_ref[2, 0])
    zero = jnp.zeros_like(lam_r)
    one = jnp.ones_like(lam_r)

    def step(t, carry, final):
        mr, mi, ar, ai, pr, pi, qr, qi, hr, hi = carry
        flag = flags_ref[t]
        f = factor_of(flag)
        lr, li = f * lam_r, f * lam_i
        u = u_ref[t]
        mr, mi = lr * mr - li * mi + scale * u[:, :half], lr * mi + li * mr + scale * u[:, half:]
        ar, ai = cmul(lr, li, ar, ai)
        w = jnp.where(flag == 1, w_spike, w_plain)
        br, bi = f * bk_r, f * bk_i
        if final:
            last = last_ref[0] == 1
            w = jnp.where(last, one, w)
            br = jnp.where(last, zero, br)
            bi = jnp.where(last, zero, bi)
        wmr, wmi = w * mr, w * mi
        war, wai = w * ar, w * ai
        tr, ti = cmul(hr, hi, wmr, wmi)
        pr, pi = pr + tr, pi + ti
        tr, ti = cmul(hr, hi, war, wai)
        qr, qi = qr + tr, qi + ti
        hr, hi = cmul(br, bi, hr, hi)
        return (mr, mi, ar, ai, pr, pi, qr, qi, hr, hi)

    carry = (zero, zero, one, zero, zero, zero, zero, zero, one, zero)
    carry = lax.fori_loop(0, steps - 1, lambda t, c: step(t, c, False), carry, unroll=8)
    carry = step(steps - 1, carry, True)
    mr, mi, ar, ai, pr, pi, qr, qi, hr, hi = carry
    for idx, v in enumerate((ar, ai, mr, mi, hr, hi, pr, pi, qr, qi)):
        for k in range(out_ref.shape[0]):
            out_ref[k, idx] = v


def segment_kernel(me_ref, g_ref, tot_ref, mine_ref, al_r, al_i, be_r, be_i):
    count = g_ref.shape[0]
    me = me_ref[0]
    zero = jnp.zeros(g_ref.shape[2:], jnp.float32)
    one = jnp.ones_like(zero)

    ar, ai, br, bi = one, zero, zero, zero
    rec = [one, zero, zero, zero]
    for k in range(count):
        sel = me == k
        rec = [jnp.where(sel, v, r) for v, r in zip((ar, ai, br, bi), rec)]
        al_r[k], al_i[k], be_r[k], be_i[k] = ar, ai, br, bi
        Ar, Ai, Br, Bi = g_ref[k, 0], g_ref[k, 1], g_ref[k, 2], g_ref[k, 3]
        ar, ai = cmul(Ar, Ai, ar, ai)
        nr, ni = cmul(Ar, Ai, br, bi)
        br, bi = nr + Br, ni + Bi
    fwd_tot = (ar, ai, br, bi)
    fwd_me = rec

    gr, gi, pr, pi, kr, ki = one, zero, zero, zero, zero, zero
    rec = [one, zero, zero, zero, zero, zero]
    for k in reversed(range(count)):
        sel = me == k
        rec = [jnp.where(sel, v, r) for v, r in zip((gr, gi, pr, pi, kr, ki), rec)]
        Gr, Gi = g_ref[k, 4], g_ref[k, 5]
        Pr, Pi = g_ref[k, 6], g_ref[k, 7]
        Qr, Qi = g_ref[k, 8], g_ref[k, 9]
        xr, xi = cmul(Qr, Qi, be_r[k], be_i[k])
        yr, yi = cmul(Qr, Qi, al_r[k], al_i[k])
        gr, gi = cmul(Gr, Gi, gr, gi)
        nr, ni = cmul(Gr, Gi, pr, pi)
        pr, pi = nr + Pr + xr, ni + Pi + xi
        nr, ni = cmul(Gr, Gi, kr, ki)
        kr, ki = nr + yr, ni + yi
    bwd_tot = (gr, gi, pr, pi, kr, ki)
    bwd_me = rec
    for idx, v in enumerate(fwd_tot + bwd_tot):
        for s in range(tot_ref.shape[0]):
            tot_ref[s, idx] = v
    for idx, v in enumerate(list(fwd_me) + list(bwd_me)):
        mine_ref[idx] = v


def final_kernel(flags_ref, last_ref, myseg_ref, tot_ref, mine_ref, prior_ref, w_hbm, d_hbm, e_hbm,
                 o_hbm, fd_hbm, bd_hbm, th_hbm, states_ref, fitted_ref, u_ref, m_r, m_i, out_ref, e_ref,
                 o_ref, rate_ref, w_ref, d_ref, sems):
    inputs = start_input_copies(w_hbm, d_hbm, w_ref, d_ref, sems, 5)
    e_copy = pltpu.make_async_copy(e_hbm, e_ref, sems.at[0])
    o_copy = pltpu.make_async_copy(o_hbm, o_ref, sems.at[1])
    e_copy.start()
    o_copy.start()
    copies = start_rate_copies((fd_hbm, bd_hbm, th_hbm), rate_ref, sems, 2)
    fill_drive(w_ref, d_ref, u_ref, inputs)
    steps = u_ref.shape[0]
    half = u_ref.shape[2] // 2
    segs = tot_ref.shape[0]
    myseg = myseg_ref[0]
    zero = jnp.zeros(prior_ref.shape[1:], jnp.float32)
    one = jnp.ones_like(zero)

    cr, ci = prior_ref[0], prior_ref[1]
    c_in = []
    c_my = [zero, zero]
    for s in range(segs):
        c_in.append((cr, ci))
        sel = myseg == s
        c_my = [jnp.where(sel, cr, c_my[0]), jnp.where(sel, ci, c_my[1])]
        Ar, Ai, Br, Bi = tot_ref[s, 0], tot_ref[s, 1], tot_ref[s, 2], tot_ref[s, 3]
        nr, ni = cmul(Ar, Ai, cr, ci)
        cr, ci = nr + Br, ni + Bi
    er, ei = zero, zero
    e_my = [zero, zero]
    for s in reversed(range(segs)):
        sel = myseg == s
        e_my = [jnp.where(sel, er, e_my[0]), jnp.where(sel, ei, e_my[1])]
        Gr, Gi = tot_ref[s, 4], tot_ref[s, 5]
        Pr, Pi = tot_ref[s, 6], tot_ref[s, 7]
        Kr, Ki = tot_ref[s, 8], tot_ref[s, 9]
        nr, ni = cmul(Gr, Gi, er, ei)
        xr, xi = cmul(Kr, Ki, c_in[s][0], c_in[s][1])
        er, ei = nr + Pr + xr, ni + Pi + xi
    nr, ni = cmul(mine_ref[0], mine_ref[1], c_my[0], c_my[1])
    cr, ci = nr + mine_ref[2], ni + mine_ref[3]
    nr, ni = cmul(mine_ref[4], mine_ref[5], e_my[0], e_my[1])
    xr, xi = cmul(mine_ref[8], mine_ref[9], c_my[0], c_my[1])
    er, ei = nr + mine_ref[6] + xr, ni + mine_ref[7] + xi

    for c in copies:
        c.wait()
    lam_r, lam_i, bk_r, bk_i, w_plain, w_spike, scale = mode_params(
        rate_ref[0, 0], rate_ref[1, 0], rate_ref[2, 0])

    def fwd(t, carry):
        mr, mi = carry
        f = factor_of(flags_ref[t])
        lr, li = f * lam_r, f * lam_i
        u = u_ref[t]
        mr, mi = lr * mr - li * mi + scale * u[:, :half], lr * mi + li * mr + scale * u[:, half:]
        m_r[t] = mr
        m_i[t] = mi
        return (mr, mi)

    lax.fori_loop(0, steps, fwd, (cr, ci), unroll=8)

    def bwd_step(t, carry, final):
        sr, si = carry
        flag = flags_ref[t]
        f = factor_of(flag)
        w = jnp.where(flag == 1, w_spike, w_plain)
        br, bi = f * bk_r, f * bk_i
        if final:
            last = last_ref[0] == 1
            w = jnp.where(last, one, w)
            br = jnp.where(last, zero, br)
            bi = jnp.where(last, zero, bi)
        nr, ni = cmul(br, bi, sr, si)
        sr, si = nr + w * m_r[t], ni + w * m_i[t]
        out_ref[t, :, :half] = sr
        out_ref[t, :, half:] = si
        return (sr, si)

    carry = bwd_step(steps - 1, (er, ei), True)
    lax.fori_loop(0, steps - 1, lambda j, c: bwd_step(steps - 2 - j, c, False), carry, unroll=8)

    e_copy.wait()
    o_copy.wait()
    contract = (((1,), (1,)), ((), ()))
    for a in range(e_ref.shape[0]):
        stacked = out_ref[:, a, :]
        states = dot3(e_ref[a], stacked, contract)
        states_ref[a] = states.astype(states_ref.dtype)
        seen = dot3(o_ref[a], stacked, contract)
        fitted_ref[a] = (d_ref[a] - seen).astype(fitted_ref.dtype)


def gathered_over(spread, axis):
    return lax.all_to_all(spread, axis, 0, 0, tiled=False)


def on_device(
    sampled_data,
    update_weights,
    eigenbasis_columns,
    measuring_operator,
    eigen_damping,
    backward_damping,
    rotation_angle,
    switch_flags,
    prior_expectation,
):
    steps = sampled_data.shape[2]
    seg_index = lax.axis_index("seg")
    blk_index = lax.axis_index("blk")
    last = ((seg_index == lax.axis_size("seg") - 1) & (blk_index == lax.axis_size("blk") - 1))
    last = last.astype(jnp.int32).reshape(1)
    flags = switch_flags.astype(jnp.int32)

    u_shape = (steps, sampled_data.shape[0], sampled_data.shape[1])
    rates = (eigen_damping, backward_damping, rotation_angle)
    rate_scratch = pltpu.VMEM((3,) + eigen_damping.shape, jnp.float32)

    mode_shape = eigen_damping.shape[1:]
    summary = pl.pallas_call(
        summary_kernel,
        out_shape=jax.ShapeDtypeStruct((lax.axis_size("blk"), 10) + mode_shape, jnp.float32),
        in_specs=[pl.BlockSpec(memory_space=SMEM)] * 2 + [pl.BlockSpec(memory_space=pl.ANY)] * 5,
        out_specs=pl.BlockSpec(memory_space=VMEM),
        scratch_shapes=[pltpu.VMEM(u_shape, jnp.float32), rate_scratch]
        + [pltpu.VMEM(update_weights.shape, jnp.float32), pltpu.VMEM(sampled_data.shape, jnp.float32)]
        + [pltpu.SemaphoreType.DMA((11,))],
    )(flags, last, update_weights, sampled_data, *rates)

    gathered = gathered_over(summary, "blk")
    count = gathered.shape[0]
    tot, mine = pl.pallas_call(
        segment_kernel,
        out_shape=(
            jax.ShapeDtypeStruct((lax.axis_size("seg"), 10) + mode_shape, jnp.float32),
            jax.ShapeDtypeStruct((10,) + mode_shape, jnp.float32),
        ),
        in_specs=[pl.BlockSpec(memory_space=SMEM), pl.BlockSpec(memory_space=VMEM)],
        out_specs=(pl.BlockSpec(memory_space=VMEM), pl.BlockSpec(memory_space=VMEM)),
        scratch_shapes=[pltpu.VMEM((count,) + mode_shape, jnp.float32) for _ in range(4)],
    )(blk_index.astype(jnp.int32).reshape(1), gathered)

    seg_tot = gathered_over(tot, "seg")
    out_block = jax.ShapeDtypeStruct(sampled_data.shape, jnp.bfloat16)
    states, fitted = pl.pallas_call(
        final_kernel,
        out_shape=(out_block, out_block),
        in_specs=[pl.BlockSpec(memory_space=SMEM)] * 3 + [pl.BlockSpec(memory_space=VMEM)] * 3
        + [pl.BlockSpec(memory_space=pl.ANY)] * 7,
        out_specs=(pl.BlockSpec(memory_space=VMEM), pl.BlockSpec(memory_space=VMEM)),
        scratch_shapes=[pltpu.VMEM(u_shape, jnp.float32)]
        + [pltpu.VMEM((steps,) + mode_shape, jnp.float32) for _ in range(2)]
        + [pltpu.VMEM(u_shape, jnp.float32)]
        + [pltpu.VMEM(eigenbasis_columns.shape, jnp.float32) for _ in range(2)]
        + [rate_scratch]
        + [pltpu.VMEM(update_weights.shape, jnp.float32), pltpu.VMEM(sampled_data.shape, jnp.float32)]
        + [pltpu.SemaphoreType.DMA((13,))],
    )(flags, last, seg_index.astype(jnp.int32).reshape(1), seg_tot, mine, prior_expectation,
      update_weights, sampled_data, eigenbasis_columns, measuring_operator, *rates)
    return (states, fitted)


def solution(mesh):
    placed = (
        P(None, None, ("seg", "blk")),
        P(),
        P(),
        P(),
        P(("seg", "blk"), None, None),
        P(("seg", "blk"), None, None),
        P(("seg", "blk"), None, None),
        P(("seg", "blk")),
        P(),
    )
    return jax.shard_map(
        on_device,
        mesh=mesh,
        in_specs=placed,
        out_specs=(P(None, None, ("seg", "blk")), P(None, None, ("seg", "blk"))),
        check_vma=False,
    )
```

```python
import math

import jax
import jax.numpy as jnp
from jax import lax
from jax.experimental import pallas as pl
from jax.experimental.pallas import tpu as pltpu
from jax.sharding import PartitionSpec as P

spike_multiplier = 0.7

VMEM = pltpu.VMEM
SMEM = pltpu.SMEM


def cmul(ar, ai, br, bi):
    return ar * br - ai * bi, ar * bi + ai * br


def factor_of(flag):
    return jnp.where(flag == 1, jnp.float32(spike_multiplier), jnp.float32(1.0))


LOG_SPIKE_TWICE = 2.0 * math.log(spike_multiplier)


def expm1(x):
    small = jnp.abs(x) < 0.5
    xs = jnp.where(small, x, 0.0)
    p = jnp.ones_like(x)
    for k in range(12, 1, -1):
        p = 1.0 + (xs * jnp.float32(1.0 / k)) * p
    return jnp.where(small, xs * p, jnp.exp(x) - 1.0)


def mode_params(fd, bd, th):
    mag = jnp.exp(-fd)
    smag = jnp.exp(-bd)
    cos, sin = jnp.cos(th), jnp.sin(th)
    both = fd + bd
    return (
        mag * cos,
        mag * sin,
        smag * cos,
        -(smag * sin),
        -expm1(-both),
        -expm1(jnp.float32(LOG_SPIKE_TWICE) - both),
        jnp.sqrt(-expm1(-2.0 * fd)),
    )


def start_rate_copies(rate_hbm, rate_ref, sems, first):
    copies = [pltpu.make_async_copy(rate_hbm[i], rate_ref.at[i], sems.at[first + i]) for i in range(3)]
    for c in copies:
        c.start()
    return copies


def split_bf16(x):
    high = x.astype(jnp.bfloat16)
    low = (x - high.astype(jnp.float32)).astype(jnp.bfloat16)
    return high, low


def dot3(x, y, dims):
    xh, xl = split_bf16(x)
    yh, yl = split_bf16(y)

    def one(p, q):
        return lax.dot_general(p, q, dims, preferred_element_type=jnp.float32)

    return one(xh, yh) + (one(xh, yl) + one(xl, yh))


def fill_drive(w_ref, d_ref, u_ref):
    for a in range(w_ref.shape[0]):
        u_ref[:, a, :] = dot3(d_ref[a], w_ref[a], (((0,), (1,)), ((), ())))


def summary_kernel(flags_ref, last_ref, w_ref, d_ref, fd_hbm, bd_hbm, th_hbm, out_ref, u_ref,
                   rate_ref, sems):
    copies = start_rate_copies((fd_hbm, bd_hbm, th_hbm), rate_ref, sems, 0)
    fill_drive(w_ref, d_ref, u_ref)
    for c in copies:
        c.wait()
    steps = u_ref.shape[0]
    half = u_ref.shape[2] // 2
    lam_r, lam_i, bk_r, bk_i, w_plain, w_spike, scale = mode_params(
        rate_ref[0, 0], rate_ref[1, 0], rate_ref[2, 0])
    zero = jnp.zeros_like(lam_r)
    one = jnp.ones_like(lam_r)

    def step(t, carry, final):
        mr, mi, ar, ai, pr, pi, qr, qi, hr, hi = carry
        flag = flags_ref[t]
        f = factor_of(flag)
        lr, li = f * lam_r, f * lam_i
        u = u_ref[t]
        mr, mi = lr * mr - li * mi + scale * u[:, :half], lr * mi + li * mr + scale * u[:, half:]
        ar, ai = cmul(lr, li, ar, ai)
        w = jnp.where(flag == 1, w_spike, w_plain)
        br, bi = f * bk_r, f * bk_i
        if final:
            last = last_ref[0] == 1
            w = jnp.where(last, one, w)
            br = jnp.where(last, zero, br)
            bi = jnp.where(last, zero, bi)
        wmr, wmi = w * mr, w * mi
        war, wai = w * ar, w * ai
        tr, ti = cmul(hr, hi, wmr, wmi)
        pr, pi = pr + tr, pi + ti
        tr, ti = cmul(hr, hi, war, wai)
        qr, qi = qr + tr, qi + ti
        hr, hi = cmul(br, bi, hr, hi)
        return (mr, mi, ar, ai, pr, pi, qr, qi, hr, hi)

    carry = (zero, zero, one, zero, zero, zero, zero, zero, one, zero)
    carry = lax.fori_loop(0, steps - 1, lambda t, c: step(t, c, False), carry, unroll=32)
    carry = step(steps - 1, carry, True)
    mr, mi, ar, ai, pr, pi, qr, qi, hr, hi = carry
    for idx, v in enumerate((ar, ai, mr, mi, hr, hi, pr, pi, qr, qi)):
        for k in range(out_ref.shape[0]):
            out_ref[k, idx] = v


def segment_kernel(me_ref, g_ref, tot_ref, mine_ref, al_r, al_i, be_r, be_i):
    count = g_ref.shape[0]
    me = me_ref[0]
    zero = jnp.zeros(g_ref.shape[2:], jnp.float32)
    one = jnp.ones_like(zero)

    ar, ai, br, bi = one, zero, zero, zero
    rec = [one, zero, zero, zero]
    for k in range(count):
        sel = me == k
        rec = [jnp.where(sel, v, r) for v, r in zip((ar, ai, br, bi), rec)]
        al_r[k], al_i[k], be_r[k], be_i[k] = ar, ai, br, bi
        Ar, Ai, Br, Bi = g_ref[k, 0], g_ref[k, 1], g_ref[k, 2], g_ref[k, 3]
        ar, ai = cmul(Ar, Ai, ar, ai)
        nr, ni = cmul(Ar, Ai, br, bi)
        br, bi = nr + Br, ni + Bi
    fwd_tot = (ar, ai, br, bi)
    fwd_me = rec

    gr, gi, pr, pi, kr, ki = one, zero, zero, zero, zero, zero
    rec = [one, zero, zero, zero, zero, zero]
    for k in reversed(range(count)):
        sel = me == k
        rec = [jnp.where(sel, v, r) for v, r in zip((gr, gi, pr, pi, kr, ki), rec)]
        Gr, Gi = g_ref[k, 4], g_ref[k, 5]
        Pr, Pi = g_ref[k, 6], g_ref[k, 7]
        Qr, Qi = g_ref[k, 8], g_ref[k, 9]
        xr, xi = cmul(Qr, Qi, be_r[k], be_i[k])
        yr, yi = cmul(Qr, Qi, al_r[k], al_i[k])
        gr, gi = cmul(Gr, Gi, gr, gi)
        nr, ni = cmul(Gr, Gi, pr, pi)
        pr, pi = nr + Pr + xr, ni + Pi + xi
        nr, ni = cmul(Gr, Gi, kr, ki)
        kr, ki = nr + yr, ni + yi
    bwd_tot = (gr, gi, pr, pi, kr, ki)
    bwd_me = rec
    for idx, v in enumerate(fwd_tot + bwd_tot):
        for s in range(tot_ref.shape[0]):
            tot_ref[s, idx] = v
    for idx, v in enumerate(list(fwd_me) + list(bwd_me)):
        mine_ref[idx] = v


def final_kernel(flags_ref, last_ref, myseg_ref, tot_ref, mine_ref, prior_ref, w_ref, d_ref, e_hbm,
                 o_hbm, fd_hbm, bd_hbm, th_hbm, states_ref, fitted_ref, u_ref, m_r, m_i, out_ref, e_ref,
                 o_ref, rate_ref, sems):
    e_copy = pltpu.make_async_copy(e_hbm, e_ref, sems.at[0])
    o_copy = pltpu.make_async_copy(o_hbm, o_ref, sems.at[1])
    e_copy.start()
    o_copy.start()
    copies = start_rate_copies((fd_hbm, bd_hbm, th_hbm), rate_ref, sems, 2)
    fill_drive(w_ref, d_ref, u_ref)
    steps = u_ref.shape[0]
    half = u_ref.shape[2] // 2
    segs = tot_ref.shape[0]
    myseg = myseg_ref[0]
    zero = jnp.zeros(prior_ref.shape[1:], jnp.float32)
    one = jnp.ones_like(zero)

    cr, ci = prior_ref[0], prior_ref[1]
    c_in = []
    c_my = [zero, zero]
    for s in range(segs):
        c_in.append((cr, ci))
        sel = myseg == s
        c_my = [jnp.where(sel, cr, c_my[0]), jnp.where(sel, ci, c_my[1])]
        Ar, Ai, Br, Bi = tot_ref[s, 0], tot_ref[s, 1], tot_ref[s, 2], tot_ref[s, 3]
        nr, ni = cmul(Ar, Ai, cr, ci)
        cr, ci = nr + Br, ni + Bi
    er, ei = zero, zero
    e_my = [zero, zero]
    for s in reversed(range(segs)):
        sel = myseg == s
        e_my = [jnp.where(sel, er, e_my[0]), jnp.where(sel, ei, e_my[1])]
        Gr, Gi = tot_ref[s, 4], tot_ref[s, 5]
        Pr, Pi = tot_ref[s, 6], tot_ref[s, 7]
        Kr, Ki = tot_ref[s, 8], tot_ref[s, 9]
        nr, ni = cmul(Gr, Gi, er, ei)
        xr, xi = cmul(Kr, Ki, c_in[s][0], c_in[s][1])
        er, ei = nr + Pr + xr, ni + Pi + xi
    nr, ni = cmul(mine_ref[0], mine_ref[1], c_my[0], c_my[1])
    cr, ci = nr + mine_ref[2], ni + mine_ref[3]
    nr, ni = cmul(mine_ref[4], mine_ref[5], e_my[0], e_my[1])
    xr, xi = cmul(mine_ref[8], mine_ref[9], c_my[0], c_my[1])
    er, ei = nr + mine_ref[6] + xr, ni + mine_ref[7] + xi

    for c in copies:
        c.wait()
    lam_r, lam_i, bk_r, bk_i, w_plain, w_spike, scale = mode_params(
        rate_ref[0, 0], rate_ref[1, 0], rate_ref[2, 0])

    def fwd(t, carry):
        mr, mi = carry
        f = factor_of(flags_ref[t])
        lr, li = f * lam_r, f * lam_i
        u = u_ref[t]
        mr, mi = lr * mr - li * mi + scale * u[:, :half], lr * mi + li * mr + scale * u[:, half:]
        m_r[t] = mr
        m_i[t] = mi
        return (mr, mi)

    lax.fori_loop(0, steps, fwd, (cr, ci), unroll=32)

    def bwd_step(t, carry, final):
        sr, si = carry
        flag = flags_ref[t]
        f = factor_of(flag)
        w = jnp.where(flag == 1, w_spike, w_plain)
        br, bi = f * bk_r, f * bk_i
        if final:
            last = last_ref[0] == 1
            w = jnp.where(last, one, w)
            br = jnp.where(last, zero, br)
            bi = jnp.where(last, zero, bi)
        nr, ni = cmul(br, bi, sr, si)
        sr, si = nr + w * m_r[t], ni + w * m_i[t]
        out_ref[t, :, :half] = sr
        out_ref[t, :, half:] = si
        return (sr, si)

    carry = bwd_step(steps - 1, (er, ei), True)
    lax.fori_loop(0, steps - 1, lambda j, c: bwd_step(steps - 2 - j, c, False), carry, unroll=32)

    e_copy.wait()
    o_copy.wait()
    contract = (((1,), (1,)), ((), ()))
    for a in range(e_ref.shape[0]):
        stacked = out_ref[:, a, :]
        states = dot3(e_ref[a], stacked, contract)
        states_ref[a] = states.astype(states_ref.dtype)
        seen = dot3(o_ref[a], stacked, contract)
        fitted_ref[a] = (d_ref[a] - seen).astype(fitted_ref.dtype)


def gathered_over(spread, axis):
    return lax.all_to_all(spread, axis, 0, 0, tiled=False)


def on_device(
    sampled_data,
    update_weights,
    eigenbasis_columns,
    measuring_operator,
    eigen_damping,
    backward_damping,
    rotation_angle,
    switch_flags,
    prior_expectation,
):
    steps = sampled_data.shape[2]
    seg_index = lax.axis_index("seg")
    blk_index = lax.axis_index("blk")
    last = ((seg_index == lax.axis_size("seg") - 1) & (blk_index == lax.axis_size("blk") - 1))
    last = last.astype(jnp.int32).reshape(1)
    flags = switch_flags.astype(jnp.int32)

    u_shape = (steps, sampled_data.shape[0], sampled_data.shape[1])
    rates = (eigen_damping, backward_damping, rotation_angle)
    rate_scratch = pltpu.VMEM((3,) + eigen_damping.shape, jnp.float32)

    mode_shape = eigen_damping.shape[1:]
    summary = pl.pallas_call(
        summary_kernel,
        out_shape=jax.ShapeDtypeStruct((lax.axis_size("blk"), 10) + mode_shape, jnp.float32),
        in_specs=[pl.BlockSpec(memory_space=SMEM)] * 2 + [pl.BlockSpec(memory_space=VMEM)] * 2
        + [pl.BlockSpec(memory_space=pl.ANY)] * 3,
        out_specs=pl.BlockSpec(memory_space=VMEM),
        scratch_shapes=[pltpu.VMEM(u_shape, jnp.float32), rate_scratch, pltpu.SemaphoreType.DMA((3,))],
    )(flags, last, update_weights, sampled_data, *rates)

    gathered = gathered_over(summary, "blk")
    count = gathered.shape[0]
    tot, mine = pl.pallas_call(
        segment_kernel,
        out_shape=(
            jax.ShapeDtypeStruct((lax.axis_size("seg"), 10) + mode_shape, jnp.float32),
            jax.ShapeDtypeStruct((10,) + mode_shape, jnp.float32),
        ),
        in_specs=[pl.BlockSpec(memory_space=SMEM), pl.BlockSpec(memory_space=VMEM)],
        out_specs=(pl.BlockSpec(memory_space=VMEM), pl.BlockSpec(memory_space=VMEM)),
        scratch_shapes=[pltpu.VMEM((count,) + mode_shape, jnp.float32) for _ in range(4)],
    )(blk_index.astype(jnp.int32).reshape(1), gathered)

    seg_tot = gathered_over(tot, "seg")
    out_block = jax.ShapeDtypeStruct(sampled_data.shape, jnp.bfloat16)
    states, fitted = pl.pallas_call(
        final_kernel,
        out_shape=(out_block, out_block),
        in_specs=[pl.BlockSpec(memory_space=SMEM)] * 3 + [pl.BlockSpec(memory_space=VMEM)] * 5
        + [pl.BlockSpec(memory_space=pl.ANY)] * 5,
        out_specs=(pl.BlockSpec(memory_space=VMEM), pl.BlockSpec(memory_space=VMEM)),
        scratch_shapes=[pltpu.VMEM(u_shape, jnp.float32)]
        + [pltpu.VMEM((steps,) + mode_shape, jnp.float32) for _ in range(2)]
        + [pltpu.VMEM(u_shape, jnp.float32)]
        + [pltpu.VMEM(eigenbasis_columns.shape, jnp.float32) for _ in range(2)]
        + [rate_scratch, pltpu.SemaphoreType.DMA((5,))],
    )(flags, last, seg_index.astype(jnp.int32).reshape(1), seg_tot, mine, prior_expectation,
      update_weights, sampled_data, eigenbasis_columns, measuring_operator, *rates)
    return (states, fitted)


def solution(mesh):
    placed = (
        P(None, None, ("seg", "blk")),
        P(),
        P(),
        P(),
        P(("seg", "blk"), None, None),
        P(("seg", "blk"), None, None),
        P(("seg", "blk"), None, None),
        P(("seg", "blk")),
        P(),
    )
    return jax.shard_map(
        on_device,
        mesh=mesh,
        in_specs=placed,
        out_specs=(P(None, None, ("seg", "blk")), P(None, None, ("seg", "blk"))),
        check_vma=False,
    )
```

```python
import math

import jax
import jax.numpy as jnp
from jax import lax
from jax.experimental import pallas as pl
from jax.experimental.pallas import tpu as pltpu
from jax.sharding import PartitionSpec as P

spike_multiplier = 0.7

VMEM = pltpu.VMEM
SMEM = pltpu.SMEM


def cmul(ar, ai, br, bi):
    return ar * br - ai * bi, ar * bi + ai * br


def factor_of(flag):
    return jnp.where(flag == 1, jnp.float32(spike_multiplier), jnp.float32(1.0))


LOG_SPIKE_TWICE = 2.0 * math.log(spike_multiplier)


def expm1(x):
    small = jnp.abs(x) < 0.5
    xs = jnp.where(small, x, 0.0)
    p = jnp.ones_like(x)
    for k in range(12, 1, -1):
        p = 1.0 + (xs * jnp.float32(1.0 / k)) * p
    return jnp.where(small, xs * p, jnp.exp(x) - 1.0)


def mode_params(fd, bd, th):
    mag = jnp.exp(-fd)
    smag = jnp.exp(-bd)
    cos, sin = jnp.cos(th), jnp.sin(th)
    both = fd + bd
    return (
        mag * cos,
        mag * sin,
        smag * cos,
        -(smag * sin),
        -expm1(-both),
        -expm1(jnp.float32(LOG_SPIKE_TWICE) - both),
        jnp.sqrt(-expm1(-2.0 * fd)),
    )


def start_rate_copies(rate_hbm, rate_ref, sems, first):
    copies = [pltpu.make_async_copy(rate_hbm[i], rate_ref.at[i], sems.at[first + i]) for i in range(3)]
    for c in copies:
        c.start()
    return copies


def split_bf16(x):
    high = x.astype(jnp.bfloat16)
    low = (x - high.astype(jnp.float32)).astype(jnp.bfloat16)
    return high, low


def dot3(x, y, dims):
    xh, xl = split_bf16(x)
    yh, yl = split_bf16(y)

    def one(p, q):
        return lax.dot_general(p, q, dims, preferred_element_type=jnp.float32)

    return one(xh, yh) + (one(xh, yl) + one(xl, yh))


def fill_drive(w_ref, d_ref, u_ref):
    for a in range(w_ref.shape[0]):
        u_ref[:, a, :] = dot3(d_ref[a], w_ref[a], (((0,), (1,)), ((), ())))


def summary_kernel(flags_ref, last_ref, w_ref, d_ref, fd_hbm, bd_hbm, th_hbm, out_ref, b_ref, a_ref,
                   u_ref, rate_ref, sems):
    copies = start_rate_copies((fd_hbm, bd_hbm, th_hbm), rate_ref, sems, 0)
    fill_drive(w_ref, d_ref, u_ref)
    for c in copies:
        c.wait()
    steps = u_ref.shape[0]
    half = u_ref.shape[2] // 2
    lam_r, lam_i, bk_r, bk_i, w_plain, w_spike, scale = mode_params(
        rate_ref[0, 0], rate_ref[1, 0], rate_ref[2, 0])
    zero = jnp.zeros_like(lam_r)
    one = jnp.ones_like(lam_r)

    def step(t, carry, final):
        mr, mi, ar, ai, pr, pi, qr, qi, hr, hi = carry
        flag = flags_ref[t]
        f = factor_of(flag)
        lr, li = f * lam_r, f * lam_i
        u = u_ref[t]
        mr, mi = lr * mr - li * mi + scale * u[:, :half], lr * mi + li * mr + scale * u[:, half:]
        ar, ai = cmul(lr, li, ar, ai)
        b_ref[t, :, :half] = mr
        b_ref[t, :, half:] = mi
        a_ref[t, :, :half] = ar
        a_ref[t, :, half:] = ai
        w = jnp.where(flag == 1, w_spike, w_plain)
        br, bi = f * bk_r, f * bk_i
        if final:
            last = last_ref[0] == 1
            w = jnp.where(last, one, w)
            br = jnp.where(last, zero, br)
            bi = jnp.where(last, zero, bi)
        wmr, wmi = w * mr, w * mi
        war, wai = w * ar, w * ai
        tr, ti = cmul(hr, hi, wmr, wmi)
        pr, pi = pr + tr, pi + ti
        tr, ti = cmul(hr, hi, war, wai)
        qr, qi = qr + tr, qi + ti
        hr, hi = cmul(br, bi, hr, hi)
        return (mr, mi, ar, ai, pr, pi, qr, qi, hr, hi)

    carry = (zero, zero, one, zero, zero, zero, zero, zero, one, zero)
    carry = lax.fori_loop(0, steps - 1, lambda t, c: step(t, c, False), carry, unroll=8)
    carry = step(steps - 1, carry, True)
    mr, mi, ar, ai, pr, pi, qr, qi, hr, hi = carry
    for idx, v in enumerate((ar, ai, mr, mi, hr, hi, pr, pi, qr, qi)):
        for k in range(out_ref.shape[0]):
            out_ref[k, idx] = v


def segment_kernel(me_ref, g_ref, tot_ref, mine_ref, al_r, al_i, be_r, be_i):
    count = g_ref.shape[0]
    me = me_ref[0]
    zero = jnp.zeros(g_ref.shape[2:], jnp.float32)
    one = jnp.ones_like(zero)

    ar, ai, br, bi = one, zero, zero, zero
    rec = [one, zero, zero, zero]
    for k in range(count):
        sel = me == k
        rec = [jnp.where(sel, v, r) for v, r in zip((ar, ai, br, bi), rec)]
        al_r[k], al_i[k], be_r[k], be_i[k] = ar, ai, br, bi
        Ar, Ai, Br, Bi = g_ref[k, 0], g_ref[k, 1], g_ref[k, 2], g_ref[k, 3]
        ar, ai = cmul(Ar, Ai, ar, ai)
        nr, ni = cmul(Ar, Ai, br, bi)
        br, bi = nr + Br, ni + Bi
    fwd_tot = (ar, ai, br, bi)
    fwd_me = rec

    gr, gi, pr, pi, kr, ki = one, zero, zero, zero, zero, zero
    rec = [one, zero, zero, zero, zero, zero]
    for k in reversed(range(count)):
        sel = me == k
        rec = [jnp.where(sel, v, r) for v, r in zip((gr, gi, pr, pi, kr, ki), rec)]
        Gr, Gi = g_ref[k, 4], g_ref[k, 5]
        Pr, Pi = g_ref[k, 6], g_ref[k, 7]
        Qr, Qi = g_ref[k, 8], g_ref[k, 9]
        xr, xi = cmul(Qr, Qi, be_r[k], be_i[k])
        yr, yi = cmul(Qr, Qi, al_r[k], al_i[k])
        gr, gi = cmul(Gr, Gi, gr, gi)
        nr, ni = cmul(Gr, Gi, pr, pi)
        pr, pi = nr + Pr + xr, ni + Pi + xi
        nr, ni = cmul(Gr, Gi, kr, ki)
        kr, ki = nr + yr, ni + yi
    bwd_tot = (gr, gi, pr, pi, kr, ki)
    bwd_me = rec
    for idx, v in enumerate(fwd_tot + bwd_tot):
        for s in range(tot_ref.shape[0]):
            tot_ref[s, idx] = v
    for idx, v in enumerate(list(fwd_me) + list(bwd_me)):
        mine_ref[idx] = v


def final_kernel(flags_ref, last_ref, myseg_ref, tot_ref, mine_ref, prior_ref, b_ref, a_ref, d_hbm,
                 e_hbm, o_hbm, fd_hbm, bd_hbm, th_hbm, states_ref, fitted_ref, out_ref, d_ref, e_ref,
                 o_ref, rate_ref, sems):
    e_copy = pltpu.make_async_copy(e_hbm, e_ref, sems.at[0])
    o_copy = pltpu.make_async_copy(o_hbm, o_ref, sems.at[1])
    d_copy = pltpu.make_async_copy(d_hbm, d_ref, sems.at[5])
    e_copy.start()
    o_copy.start()
    d_copy.start()
    copies = start_rate_copies((fd_hbm, bd_hbm, th_hbm), rate_ref, sems, 2)
    steps = b_ref.shape[0]
    half = b_ref.shape[2] // 2
    segs = tot_ref.shape[0]
    myseg = myseg_ref[0]
    zero = jnp.zeros(prior_ref.shape[1:], jnp.float32)
    one = jnp.ones_like(zero)

    cr, ci = prior_ref[0], prior_ref[1]
    c_in = []
    c_my = [zero, zero]
    for s in range(segs):
        c_in.append((cr, ci))
        sel = myseg == s
        c_my = [jnp.where(sel, cr, c_my[0]), jnp.where(sel, ci, c_my[1])]
        Ar, Ai, Br, Bi = tot_ref[s, 0], tot_ref[s, 1], tot_ref[s, 2], tot_ref[s, 3]
        nr, ni = cmul(Ar, Ai, cr, ci)
        cr, ci = nr + Br, ni + Bi
    er, ei = zero, zero
    e_my = [zero, zero]
    for s in reversed(range(segs)):
        sel = myseg == s
        e_my = [jnp.where(sel, er, e_my[0]), jnp.where(sel, ei, e_my[1])]
        Gr, Gi = tot_ref[s, 4], tot_ref[s, 5]
        Pr, Pi = tot_ref[s, 6], tot_ref[s, 7]
        Kr, Ki = tot_ref[s, 8], tot_ref[s, 9]
        nr, ni = cmul(Gr, Gi, er, ei)
        xr, xi = cmul(Kr, Ki, c_in[s][0], c_in[s][1])
        er, ei = nr + Pr + xr, ni + Pi + xi
    nr, ni = cmul(mine_ref[0], mine_ref[1], c_my[0], c_my[1])
    cr, ci = nr + mine_ref[2], ni + mine_ref[3]
    nr, ni = cmul(mine_ref[4], mine_ref[5], e_my[0], e_my[1])
    xr, xi = cmul(mine_ref[8], mine_ref[9], c_my[0], c_my[1])
    er, ei = nr + mine_ref[6] + xr, ni + mine_ref[7] + xi

    for c in copies:
        c.wait()
    lam_r, lam_i, bk_r, bk_i, w_plain, w_spike, scale = mode_params(
        rate_ref[0, 0], rate_ref[1, 0], rate_ref[2, 0])

    def bwd_step(t, carry, final):
        sr, si = carry
        flag = flags_ref[t]
        f = factor_of(flag)
        w = jnp.where(flag == 1, w_spike, w_plain)
        br, bi = f * bk_r, f * bk_i
        if final:
            last = last_ref[0] == 1
            w = jnp.where(last, one, w)
            br = jnp.where(last, zero, br)
            bi = jnp.where(last, zero, bi)
        b = b_ref[t]
        a = a_ref[t]
        xr, xi = cmul(a[:, :half], a[:, half:], cr, ci)
        nr, ni = cmul(br, bi, sr, si)
        sr, si = nr + w * (b[:, :half] + xr), ni + w * (b[:, half:] + xi)
        out_ref[t, :, :half] = sr
        out_ref[t, :, half:] = si
        return (sr, si)

    carry = bwd_step(steps - 1, (er, ei), True)
    lax.fori_loop(0, steps - 1, lambda j, c: bwd_step(steps - 2 - j, c, False), carry, unroll=8)

    e_copy.wait()
    o_copy.wait()
    d_copy.wait()
    contract = (((1,), (1,)), ((), ()))
    for a in range(e_ref.shape[0]):
        stacked = out_ref[:, a, :]
        states = dot3(e_ref[a], stacked, contract)
        states_ref[a] = states.astype(states_ref.dtype)
        seen = dot3(o_ref[a], stacked, contract)
        fitted_ref[a] = (d_ref[a] - seen).astype(fitted_ref.dtype)


def gathered_over(spread, axis):
    return lax.all_to_all(spread, axis, 0, 0, tiled=False)


def on_device(
    sampled_data,
    update_weights,
    eigenbasis_columns,
    measuring_operator,
    eigen_damping,
    backward_damping,
    rotation_angle,
    switch_flags,
    prior_expectation,
):
    steps = sampled_data.shape[2]
    seg_index = lax.axis_index("seg")
    blk_index = lax.axis_index("blk")
    last = ((seg_index == lax.axis_size("seg") - 1) & (blk_index == lax.axis_size("blk") - 1))
    last = last.astype(jnp.int32).reshape(1)
    flags = switch_flags.astype(jnp.int32)

    u_shape = (steps, sampled_data.shape[0], sampled_data.shape[1])
    rates = (eigen_damping, backward_damping, rotation_angle)
    rate_scratch = pltpu.VMEM((3,) + eigen_damping.shape, jnp.float32)

    mode_shape = eigen_damping.shape[1:]
    runs = jax.ShapeDtypeStruct(u_shape, jnp.float32)
    summary, forward_zero, growth = pl.pallas_call(
        summary_kernel,
        out_shape=(jax.ShapeDtypeStruct((lax.axis_size("blk"), 10) + mode_shape, jnp.float32), runs, runs),
        in_specs=[pl.BlockSpec(memory_space=SMEM)] * 2 + [pl.BlockSpec(memory_space=VMEM)] * 2
        + [pl.BlockSpec(memory_space=pl.ANY)] * 3,
        out_specs=(pl.BlockSpec(memory_space=VMEM),) * 3,
        scratch_shapes=[pltpu.VMEM(u_shape, jnp.float32), rate_scratch, pltpu.SemaphoreType.DMA((3,))],
    )(flags, last, update_weights, sampled_data, *rates)

    gathered = gathered_over(summary, "blk")
    count = gathered.shape[0]
    tot, mine = pl.pallas_call(
        segment_kernel,
        out_shape=(
            jax.ShapeDtypeStruct((lax.axis_size("seg"), 10) + mode_shape, jnp.float32),
            jax.ShapeDtypeStruct((10,) + mode_shape, jnp.float32),
        ),
        in_specs=[pl.BlockSpec(memory_space=SMEM), pl.BlockSpec(memory_space=VMEM)],
        out_specs=(pl.BlockSpec(memory_space=VMEM), pl.BlockSpec(memory_space=VMEM)),
        scratch_shapes=[pltpu.VMEM((count,) + mode_shape, jnp.float32) for _ in range(4)],
    )(blk_index.astype(jnp.int32).reshape(1), gathered)

    seg_tot = gathered_over(tot, "seg")
    out_block = jax.ShapeDtypeStruct(sampled_data.shape, jnp.bfloat16)
    states, fitted = pl.pallas_call(
        final_kernel,
        out_shape=(out_block, out_block),
        in_specs=[pl.BlockSpec(memory_space=SMEM)] * 3 + [pl.BlockSpec(memory_space=VMEM)] * 5
        + [pl.BlockSpec(memory_space=pl.ANY)] * 6,
        out_specs=(pl.BlockSpec(memory_space=VMEM), pl.BlockSpec(memory_space=VMEM)),
        scratch_shapes=[pltpu.VMEM(u_shape, jnp.float32)]
        + [pltpu.VMEM(sampled_data.shape, jnp.float32)]
        + [pltpu.VMEM(eigenbasis_columns.shape, jnp.float32) for _ in range(2)]
        + [rate_scratch, pltpu.SemaphoreType.DMA((6,))],
    )(flags, last, seg_index.astype(jnp.int32).reshape(1), seg_tot, mine, prior_expectation,
      forward_zero, growth, sampled_data, eigenbasis_columns, measuring_operator, *rates)
    return (states, fitted)


def solution(mesh):
    placed = (
        P(None, None, ("seg", "blk")),
        P(),
        P(),
        P(),
        P(("seg", "blk"), None, None),
        P(("seg", "blk"), None, None),
        P(("seg", "blk"), None, None),
        P(("seg", "blk")),
        P(),
    )
    return jax.shard_map(
        on_device,
        mesh=mesh,
        in_specs=placed,
        out_specs=(P(None, None, ("seg", "blk")), P(None, None, ("seg", "blk"))),
        check_vma=False,
    )
```

```python
import math

import jax
import jax.numpy as jnp
from jax import lax
from jax.experimental import pallas as pl
from jax.experimental.pallas import tpu as pltpu
from jax.sharding import PartitionSpec as P

spike_multiplier = 0.7

VMEM = pltpu.VMEM
SMEM = pltpu.SMEM


def cmul(ar, ai, br, bi):
    return ar * br - ai * bi, ar * bi + ai * br


def factor_of(flag):
    return jnp.where(flag == 1, jnp.float32(spike_multiplier), jnp.float32(1.0))


LOG_SPIKE_TWICE = 2.0 * math.log(spike_multiplier)


def expm1(x):
    small = jnp.abs(x) < 0.5
    xs = jnp.where(small, x, 0.0)
    p = jnp.ones_like(x)
    for k in range(12, 1, -1):
        p = 1.0 + (xs * jnp.float32(1.0 / k)) * p
    return jnp.where(small, xs * p, jnp.exp(x) - 1.0)


def mode_params(fd, bd, th):
    mag = jnp.exp(-fd)
    smag = jnp.exp(-bd)
    cos, sin = jnp.cos(th), jnp.sin(th)
    both = fd + bd
    return (
        mag * cos,
        mag * sin,
        smag * cos,
        -(smag * sin),
        -expm1(-both),
        -expm1(jnp.float32(LOG_SPIKE_TWICE) - both),
        jnp.sqrt(-expm1(-2.0 * fd)),
    )


def start_rate_copies(rate_hbm, rate_ref, sems, first):
    copies = [pltpu.make_async_copy(rate_hbm[i], rate_ref.at[i], sems.at[first + i]) for i in range(3)]
    for c in copies:
        c.start()
    return copies


def split_bf16(x):
    high = x.astype(jnp.bfloat16)
    low = (x - high.astype(jnp.float32)).astype(jnp.bfloat16)
    return high, low


def dot3(x, y, dims):
    xh, xl = split_bf16(x)
    yh, yl = split_bf16(y)

    def one(p, q):
        return lax.dot_general(p, q, dims, preferred_element_type=jnp.float32)

    return one(xh, yh) + (one(xh, yl) + one(xl, yh))


def fill_drive(w_ref, d_ref, u_ref):
    for a in range(w_ref.shape[0]):
        u_ref[:, a, :] = dot3(d_ref[a], w_ref[a], (((0,), (1,)), ((), ())))


def summary_kernel(flags_ref, last_ref, w_ref, d_ref, fd_hbm, bd_hbm, th_hbm, out_ref, u_ref,
                   rate_ref, sems):
    copies = start_rate_copies((fd_hbm, bd_hbm, th_hbm), rate_ref, sems, 0)
    fill_drive(w_ref, d_ref, u_ref)
    for c in copies:
        c.wait()
    steps = u_ref.shape[0]
    half = u_ref.shape[2] // 2
    lam_r, lam_i, bk_r, bk_i, w_plain, w_spike, scale = mode_params(
        rate_ref[0, 0], rate_ref[1, 0], rate_ref[2, 0])
    zero = jnp.zeros_like(lam_r)
    one = jnp.ones_like(lam_r)

    def step(t, carry, final):
        mr, mi, ar, ai, pr, pi, qr, qi, hr, hi = carry
        flag = flags_ref[t]
        f = factor_of(flag)
        lr, li = f * lam_r, f * lam_i
        u = u_ref[t]
        mr, mi = lr * mr - li * mi + scale * u[:, :half], lr * mi + li * mr + scale * u[:, half:]
        ar, ai = cmul(lr, li, ar, ai)
        w = jnp.where(flag == 1, w_spike, w_plain)
        br, bi = f * bk_r, f * bk_i
        if final:
            last = last_ref[0] == 1
            w = jnp.where(last, one, w)
            br = jnp.where(last, zero, br)
            bi = jnp.where(last, zero, bi)
        wmr, wmi = w * mr, w * mi
        war, wai = w * ar, w * ai
        tr, ti = cmul(hr, hi, wmr, wmi)
        pr, pi = pr + tr, pi + ti
        tr, ti = cmul(hr, hi, war, wai)
        qr, qi = qr + tr, qi + ti
        hr, hi = cmul(br, bi, hr, hi)
        return (mr, mi, ar, ai, pr, pi, qr, qi, hr, hi)

    carry = (zero, zero, one, zero, zero, zero, zero, zero, one, zero)
    carry = lax.fori_loop(0, steps - 1, lambda t, c: step(t, c, False), carry, unroll=8)
    carry = step(steps - 1, carry, True)
    mr, mi, ar, ai, pr, pi, qr, qi, hr, hi = carry
    for idx, v in enumerate((ar, ai, mr, mi, hr, hi, pr, pi, qr, qi)):
        for k in range(out_ref.shape[0]):
            out_ref[k, idx] = v


def segment_kernel(me_ref, g_ref, tot_ref, mine_ref, al_r, al_i, be_r, be_i):
    count = g_ref.shape[0]
    me = me_ref[0]
    zero = jnp.zeros(g_ref.shape[2:], jnp.float32)
    one = jnp.ones_like(zero)

    ar, ai, br, bi = one, zero, zero, zero
    rec = [one, zero, zero, zero]
    for k in range(count):
        sel = me == k
        rec = [jnp.where(sel, v, r) for v, r in zip((ar, ai, br, bi), rec)]
        al_r[k], al_i[k], be_r[k], be_i[k] = ar, ai, br, bi
        Ar, Ai, Br, Bi = g_ref[k, 0], g_ref[k, 1], g_ref[k, 2], g_ref[k, 3]
        ar, ai = cmul(Ar, Ai, ar, ai)
        nr, ni = cmul(Ar, Ai, br, bi)
        br, bi = nr + Br, ni + Bi
    fwd_tot = (ar, ai, br, bi)
    fwd_me = rec

    gr, gi, pr, pi, kr, ki = one, zero, zero, zero, zero, zero
    rec = [one, zero, zero, zero, zero, zero]
    for k in reversed(range(count)):
        sel = me == k
        rec = [jnp.where(sel, v, r) for v, r in zip((gr, gi, pr, pi, kr, ki), rec)]
        Gr, Gi = g_ref[k, 4], g_ref[k, 5]
        Pr, Pi = g_ref[k, 6], g_ref[k, 7]
        Qr, Qi = g_ref[k, 8], g_ref[k, 9]
        xr, xi = cmul(Qr, Qi, be_r[k], be_i[k])
        yr, yi = cmul(Qr, Qi, al_r[k], al_i[k])
        gr, gi = cmul(Gr, Gi, gr, gi)
        nr, ni = cmul(Gr, Gi, pr, pi)
        pr, pi = nr + Pr + xr, ni + Pi + xi
        nr, ni = cmul(Gr, Gi, kr, ki)
        kr, ki = nr + yr, ni + yi
    bwd_tot = (gr, gi, pr, pi, kr, ki)
    bwd_me = rec
    for idx, v in enumerate(fwd_tot + bwd_tot):
        for s in range(tot_ref.shape[0]):
            tot_ref[s, idx] = v
    for idx, v in enumerate(list(fwd_me) + list(bwd_me)):
        mine_ref[idx] = v


def drive_kernel(w_ref, d_ref, u_ref):
    fill_drive(w_ref, d_ref, u_ref)


def final_kernel(flags_ref, last_ref, myseg_ref, tot_ref, mine_ref, prior_ref, u_ref, d_ref, e_hbm,
                 o_hbm, fd_hbm, bd_hbm, th_hbm, states_ref, fitted_ref, m_r, m_i, out_ref, e_ref,
                 o_ref, rate_ref, sems):
    e_copy = pltpu.make_async_copy(e_hbm, e_ref, sems.at[0])
    o_copy = pltpu.make_async_copy(o_hbm, o_ref, sems.at[1])
    e_copy.start()
    o_copy.start()
    copies = start_rate_copies((fd_hbm, bd_hbm, th_hbm), rate_ref, sems, 2)
    steps = u_ref.shape[0]
    half = u_ref.shape[2] // 2
    segs = tot_ref.shape[0]
    myseg = myseg_ref[0]
    zero = jnp.zeros(prior_ref.shape[1:], jnp.float32)
    one = jnp.ones_like(zero)

    cr, ci = prior_ref[0], prior_ref[1]
    c_in = []
    c_my = [zero, zero]
    for s in range(segs):
        c_in.append((cr, ci))
        sel = myseg == s
        c_my = [jnp.where(sel, cr, c_my[0]), jnp.where(sel, ci, c_my[1])]
        Ar, Ai, Br, Bi = tot_ref[s, 0], tot_ref[s, 1], tot_ref[s, 2], tot_ref[s, 3]
        nr, ni = cmul(Ar, Ai, cr, ci)
        cr, ci = nr + Br, ni + Bi
    er, ei = zero, zero
    e_my = [zero, zero]
    for s in reversed(range(segs)):
        sel = myseg == s
        e_my = [jnp.where(sel, er, e_my[0]), jnp.where(sel, ei, e_my[1])]
        Gr, Gi = tot_ref[s, 4], tot_ref[s, 5]
        Pr, Pi = tot_ref[s, 6], tot_ref[s, 7]
        Kr, Ki = tot_ref[s, 8], tot_ref[s, 9]
        nr, ni = cmul(Gr, Gi, er, ei)
        xr, xi = cmul(Kr, Ki, c_in[s][0], c_in[s][1])
        er, ei = nr + Pr + xr, ni + Pi + xi
    nr, ni = cmul(mine_ref[0], mine_ref[1], c_my[0], c_my[1])
    cr, ci = nr + mine_ref[2], ni + mine_ref[3]
    nr, ni = cmul(mine_ref[4], mine_ref[5], e_my[0], e_my[1])
    xr, xi = cmul(mine_ref[8], mine_ref[9], c_my[0], c_my[1])
    er, ei = nr + mine_ref[6] + xr, ni + mine_ref[7] + xi

    for c in copies:
        c.wait()
    lam_r, lam_i, bk_r, bk_i, w_plain, w_spike, scale = mode_params(
        rate_ref[0, 0], rate_ref[1, 0], rate_ref[2, 0])

    def fwd(t, carry):
        mr, mi = carry
        f = factor_of(flags_ref[t])
        lr, li = f * lam_r, f * lam_i
        u = u_ref[t]
        mr, mi = lr * mr - li * mi + scale * u[:, :half], lr * mi + li * mr + scale * u[:, half:]
        m_r[t] = mr
        m_i[t] = mi
        return (mr, mi)

    lax.fori_loop(0, steps, fwd, (cr, ci), unroll=8)

    def bwd_step(t, carry, final):
        sr, si = carry
        flag = flags_ref[t]
        f = factor_of(flag)
        w = jnp.where(flag == 1, w_spike, w_plain)
        br, bi = f * bk_r, f * bk_i
        if final:
            last = last_ref[0] == 1
            w = jnp.where(last, one, w)
            br = jnp.where(last, zero, br)
            bi = jnp.where(last, zero, bi)
        nr, ni = cmul(br, bi, sr, si)
        sr, si = nr + w * m_r[t], ni + w * m_i[t]
        out_ref[t, :, :half] = sr
        out_ref[t, :, half:] = si
        return (sr, si)

    carry = bwd_step(steps - 1, (er, ei), True)
    lax.fori_loop(0, steps - 1, lambda j, c: bwd_step(steps - 2 - j, c, False), carry, unroll=8)

    e_copy.wait()
    o_copy.wait()
    contract = (((1,), (1,)), ((), ()))
    for a in range(e_ref.shape[0]):
        stacked = out_ref[:, a, :]
        states = dot3(e_ref[a], stacked, contract)
        states_ref[a] = states.astype(states_ref.dtype)
        seen = dot3(o_ref[a], stacked, contract)
        fitted_ref[a] = (d_ref[a] - seen).astype(fitted_ref.dtype)


def gathered_over(spread, axis):
    return lax.all_to_all(spread, axis, 0, 0, tiled=False)


def on_device(
    sampled_data,
    update_weights,
    eigenbasis_columns,
    measuring_operator,
    eigen_damping,
    backward_damping,
    rotation_angle,
    switch_flags,
    prior_expectation,
):
    steps = sampled_data.shape[2]
    seg_index = lax.axis_index("seg")
    blk_index = lax.axis_index("blk")
    last = ((seg_index == lax.axis_size("seg") - 1) & (blk_index == lax.axis_size("blk") - 1))
    last = last.astype(jnp.int32).reshape(1)
    flags = switch_flags.astype(jnp.int32)

    u_shape = (steps, sampled_data.shape[0], sampled_data.shape[1])
    rates = (eigen_damping, backward_damping, rotation_angle)
    rate_scratch = pltpu.VMEM((3,) + eigen_damping.shape, jnp.float32)

    mode_shape = eigen_damping.shape[1:]
    summary = pl.pallas_call(
        summary_kernel,
        out_shape=jax.ShapeDtypeStruct((lax.axis_size("blk"), 10) + mode_shape, jnp.float32),
        in_specs=[pl.BlockSpec(memory_space=SMEM)] * 2 + [pl.BlockSpec(memory_space=VMEM)] * 2
        + [pl.BlockSpec(memory_space=pl.ANY)] * 3,
        out_specs=pl.BlockSpec(memory_space=VMEM),
        scratch_shapes=[pltpu.VMEM(u_shape, jnp.float32), rate_scratch, pltpu.SemaphoreType.DMA((3,))],
    )(flags, last, update_weights, sampled_data, *rates)

    gathered = gathered_over(summary, "blk")
    count = gathered.shape[0]
    tot, mine = pl.pallas_call(
        segment_kernel,
        out_shape=(
            jax.ShapeDtypeStruct((lax.axis_size("seg"), 10) + mode_shape, jnp.float32),
            jax.ShapeDtypeStruct((10,) + mode_shape, jnp.float32),
        ),
        in_specs=[pl.BlockSpec(memory_space=SMEM), pl.BlockSpec(memory_space=VMEM)],
        out_specs=(pl.BlockSpec(memory_space=VMEM), pl.BlockSpec(memory_space=VMEM)),
        scratch_shapes=[pltpu.VMEM((count,) + mode_shape, jnp.float32) for _ in range(4)],
    )(blk_index.astype(jnp.int32).reshape(1), gathered)

    drive = pl.pallas_call(
        drive_kernel,
        out_shape=jax.ShapeDtypeStruct(u_shape, jnp.float32),
        in_specs=[pl.BlockSpec(memory_space=VMEM)] * 2,
        out_specs=pl.BlockSpec(memory_space=VMEM),
        cost_estimate=pl.CostEstimate(flops=3 * 2 * int(math.prod(sampled_data.shape)) * sampled_data.shape[1],
                                      bytes_accessed=4 * 4 * int(math.prod(sampled_data.shape)),
                                      transcendentals=0),
    )(update_weights, sampled_data)
    seg_tot = gathered_over(tot, "seg")
    out_block = jax.ShapeDtypeStruct(sampled_data.shape, jnp.bfloat16)
    states, fitted = pl.pallas_call(
        final_kernel,
        out_shape=(out_block, out_block),
        in_specs=[pl.BlockSpec(memory_space=SMEM)] * 3 + [pl.BlockSpec(memory_space=VMEM)] * 5
        + [pl.BlockSpec(memory_space=pl.ANY)] * 5,
        out_specs=(pl.BlockSpec(memory_space=VMEM), pl.BlockSpec(memory_space=VMEM)),
        scratch_shapes=[pltpu.VMEM((steps,) + mode_shape, jnp.float32) for _ in range(2)]
        + [pltpu.VMEM(u_shape, jnp.float32)]
        + [pltpu.VMEM(eigenbasis_columns.shape, jnp.float32) for _ in range(2)]
        + [rate_scratch, pltpu.SemaphoreType.DMA((5,))],
    )(flags, last, seg_index.astype(jnp.int32).reshape(1), seg_tot, mine, prior_expectation,
      drive, sampled_data, eigenbasis_columns, measuring_operator, *rates)
    return (states, fitted)


def solution(mesh):
    placed = (
        P(None, None, ("seg", "blk")),
        P(),
        P(),
        P(),
        P(("seg", "blk"), None, None),
        P(("seg", "blk"), None, None),
        P(("seg", "blk"), None, None),
        P(("seg", "blk")),
        P(),
    )
    return jax.shard_map(
        on_device,
        mesh=mesh,
        in_specs=placed,
        out_specs=(P(None, None, ("seg", "blk")), P(None, None, ("seg", "blk"))),
        check_vma=False,
    )
```

```python
import math

import jax
import jax.numpy as jnp
from jax import lax
from jax.experimental import pallas as pl
from jax.experimental.pallas import tpu as pltpu
from jax.sharding import PartitionSpec as P

spike_multiplier = 0.7

VMEM = pltpu.VMEM
SMEM = pltpu.SMEM


def cmul(ar, ai, br, bi):
    return ar * br - ai * bi, ar * bi + ai * br


def factor_of(flag):
    return jnp.where(flag == 1, jnp.float32(spike_multiplier), jnp.float32(1.0))


LOG_SPIKE_TWICE = 2.0 * math.log(spike_multiplier)


def expm1(x):
    small = jnp.abs(x) < 0.5
    xs = jnp.where(small, x, 0.0)
    p = jnp.ones_like(x)
    for k in range(12, 1, -1):
        p = 1.0 + (xs * jnp.float32(1.0 / k)) * p
    return jnp.where(small, xs * p, jnp.exp(x) - 1.0)


def mode_params(fd, bd, th):
    mag = jnp.exp(-fd)
    smag = jnp.exp(-bd)
    cos, sin = jnp.cos(th), jnp.sin(th)
    both = fd + bd
    return (
        mag * cos,
        mag * sin,
        smag * cos,
        -(smag * sin),
        -expm1(-both),
        -expm1(jnp.float32(LOG_SPIKE_TWICE) - both),
        jnp.sqrt(-expm1(-2.0 * fd)),
    )


def start_rate_copies(rate_hbm, rate_ref, sems, first):
    copies = [pltpu.make_async_copy(rate_hbm[i], rate_ref.at[i], sems.at[first + i]) for i in range(3)]
    for c in copies:
        c.start()
    return copies


def split_bf16(x):
    high = x.astype(jnp.bfloat16)
    low = (x - high.astype(jnp.float32)).astype(jnp.bfloat16)
    return high, low


def dot3(x, y, dims):
    xh, xl = split_bf16(x)
    yh, yl = split_bf16(y)

    def one(p, q):
        return lax.dot_general(p, q, dims, preferred_element_type=jnp.float32)

    return one(xh, yh) + (one(xh, yl) + one(xl, yh))


def fill_drive(w_ref, d_ref, u_ref):
    for a in range(w_ref.shape[0]):
        u_ref[:, a, :] = dot3(d_ref[a], w_ref[a], (((0,), (1,)), ((), ())))


def summary_kernel(flags_ref, last_ref, w_ref, d_ref, fd_hbm, bd_hbm, th_hbm, out_ref, u_ref,
                   rate_ref, sems):
    copies = start_rate_copies((fd_hbm, bd_hbm, th_hbm), rate_ref, sems, 0)
    fill_drive(w_ref, d_ref, u_ref)
    for c in copies:
        c.wait()
    steps = u_ref.shape[0]
    half = u_ref.shape[2] // 2
    lam_r, lam_i, bk_r, bk_i, w_plain, w_spike, scale = mode_params(
        rate_ref[0, 0], rate_ref[1, 0], rate_ref[2, 0])
    zero = jnp.zeros_like(lam_r)
    one = jnp.ones_like(lam_r)

    def step(t, carry, final):
        mr, mi, ar, ai, pr, pi, qr, qi, hr, hi = carry
        flag = flags_ref[t]
        f = factor_of(flag)
        lr, li = f * lam_r, f * lam_i
        u = u_ref[t]
        mr, mi = lr * mr - li * mi + scale * u[:, :half], lr * mi + li * mr + scale * u[:, half:]
        ar, ai = cmul(lr, li, ar, ai)
        w = jnp.where(flag == 1, w_spike, w_plain)
        br, bi = f * bk_r, f * bk_i
        if final:
            last = last_ref[0] == 1
            w = jnp.where(last, one, w)
            br = jnp.where(last, zero, br)
            bi = jnp.where(last, zero, bi)
        wmr, wmi = w * mr, w * mi
        war, wai = w * ar, w * ai
        tr, ti = cmul(hr, hi, wmr, wmi)
        pr, pi = pr + tr, pi + ti
        tr, ti = cmul(hr, hi, war, wai)
        qr, qi = qr + tr, qi + ti
        hr, hi = cmul(br, bi, hr, hi)
        return (mr, mi, ar, ai, pr, pi, qr, qi, hr, hi)

    carry = (zero, zero, one, zero, zero, zero, zero, zero, one, zero)
    carry = lax.fori_loop(0, steps - 1, lambda t, c: step(t, c, False), carry, unroll=8)
    carry = step(steps - 1, carry, True)
    mr, mi, ar, ai, pr, pi, qr, qi, hr, hi = carry
    for idx, v in enumerate((ar, ai, mr, mi, hr, hi, pr, pi, qr, qi)):
        for k in range(out_ref.shape[0]):
            out_ref[k, idx] = v


def segment_kernel(me_ref, g_ref, tot_ref, mine_ref, al_r, al_i, be_r, be_i, back_ref):
    count = g_ref.shape[0]
    me = me_ref[0]
    zero = jnp.zeros(g_ref.shape[2:], jnp.float32)
    one = jnp.ones_like(zero)

    ar, ai, br, bi = one, zero, zero, zero
    for k in range(count):
        al_r[k], al_i[k], be_r[k], be_i[k] = ar, ai, br, bi
        Ar, Ai, Br, Bi = g_ref[k, 0], g_ref[k, 1], g_ref[k, 2], g_ref[k, 3]
        ar, ai = cmul(Ar, Ai, ar, ai)
        nr, ni = cmul(Ar, Ai, br, bi)
        br, bi = nr + Br, ni + Bi
    fwd_tot = (ar, ai, br, bi)
    fwd_me = [al_r[me], al_i[me], be_r[me], be_i[me]]

    gr, gi, pr, pi, kr, ki = one, zero, zero, zero, zero, zero
    for k in reversed(range(count)):
        for idx, v in enumerate((gr, gi, pr, pi, kr, ki)):
            back_ref[k, idx] = v
        Gr, Gi = g_ref[k, 4], g_ref[k, 5]
        Pr, Pi = g_ref[k, 6], g_ref[k, 7]
        Qr, Qi = g_ref[k, 8], g_ref[k, 9]
        xr, xi = cmul(Qr, Qi, be_r[k], be_i[k])
        yr, yi = cmul(Qr, Qi, al_r[k], al_i[k])
        gr, gi = cmul(Gr, Gi, gr, gi)
        nr, ni = cmul(Gr, Gi, pr, pi)
        pr, pi = nr + Pr + xr, ni + Pi + xi
        nr, ni = cmul(Gr, Gi, kr, ki)
        kr, ki = nr + yr, ni + yi
    bwd_tot = (gr, gi, pr, pi, kr, ki)
    mine_back = back_ref[me]
    bwd_me = [mine_back[idx] for idx in range(6)]
    for idx, v in enumerate(fwd_tot + bwd_tot):
        for s in range(tot_ref.shape[0]):
            tot_ref[s, idx] = v
    for idx, v in enumerate(list(fwd_me) + list(bwd_me)):
        mine_ref[idx] = v


def final_kernel(flags_ref, last_ref, myseg_ref, tot_ref, mine_ref, prior_ref, w_ref, d_ref, e_hbm,
                 o_hbm, fd_hbm, bd_hbm, th_hbm, states_ref, fitted_ref, u_ref, m_r, m_i, out_ref, e_ref,
                 o_ref, rate_ref, sems):
    e_copy = pltpu.make_async_copy(e_hbm, e_ref, sems.at[0])
    o_copy = pltpu.make_async_copy(o_hbm, o_ref, sems.at[1])
    e_copy.start()
    o_copy.start()
    copies = start_rate_copies((fd_hbm, bd_hbm, th_hbm), rate_ref, sems, 2)
    fill_drive(w_ref, d_ref, u_ref)
    steps = u_ref.shape[0]
    half = u_ref.shape[2] // 2
    segs = tot_ref.shape[0]
    myseg = myseg_ref[0]
    zero = jnp.zeros(prior_ref.shape[1:], jnp.float32)
    one = jnp.ones_like(zero)

    cr, ci = prior_ref[0], prior_ref[1]
    c_in = []
    c_my = [zero, zero]
    for s in range(segs):
        c_in.append((cr, ci))
        sel = myseg == s
        c_my = [jnp.where(sel, cr, c_my[0]), jnp.where(sel, ci, c_my[1])]
        Ar, Ai, Br, Bi = tot_ref[s, 0], tot_ref[s, 1], tot_ref[s, 2], tot_ref[s, 3]
        nr, ni = cmul(Ar, Ai, cr, ci)
        cr, ci = nr + Br, ni + Bi
    er, ei = zero, zero
    e_my = [zero, zero]
    for s in reversed(range(segs)):
        sel = myseg == s
        e_my = [jnp.where(sel, er, e_my[0]), jnp.where(sel, ei, e_my[1])]
        Gr, Gi = tot_ref[s, 4], tot_ref[s, 5]
        Pr, Pi = tot_ref[s, 6], tot_ref[s, 7]
        Kr, Ki = tot_ref[s, 8], tot_ref[s, 9]
        nr, ni = cmul(Gr, Gi, er, ei)
        xr, xi = cmul(Kr, Ki, c_in[s][0], c_in[s][1])
        er, ei = nr + Pr + xr, ni + Pi + xi
    nr, ni = cmul(mine_ref[0], mine_ref[1], c_my[0], c_my[1])
    cr, ci = nr + mine_ref[2], ni + mine_ref[3]
    nr, ni = cmul(mine_ref[4], mine_ref[5], e_my[0], e_my[1])
    xr, xi = cmul(mine_ref[8], mine_ref[9], c_my[0], c_my[1])
    er, ei = nr + mine_ref[6] + xr, ni + mine_ref[7] + xi

    for c in copies:
        c.wait()
    lam_r, lam_i, bk_r, bk_i, w_plain, w_spike, scale = mode_params(
        rate_ref[0, 0], rate_ref[1, 0], rate_ref[2, 0])

    def fwd(t, carry):
        mr, mi = carry
        f = factor_of(flags_ref[t])
        lr, li = f * lam_r, f * lam_i
        u = u_ref[t]
        mr, mi = lr * mr - li * mi + scale * u[:, :half], lr * mi + li * mr + scale * u[:, half:]
        m_r[t] = mr
        m_i[t] = mi
        return (mr, mi)

    lax.fori_loop(0, steps, fwd, (cr, ci), unroll=8)

    def bwd_step(t, carry, final):
        sr, si = carry
        flag = flags_ref[t]
        f = factor_of(flag)
        w = jnp.where(flag == 1, w_spike, w_plain)
        br, bi = f * bk_r, f * bk_i
        if final:
            last = last_ref[0] == 1
            w = jnp.where(last, one, w)
            br = jnp.where(last, zero, br)
            bi = jnp.where(last, zero, bi)
        nr, ni = cmul(br, bi, sr, si)
        sr, si = nr + w * m_r[t], ni + w * m_i[t]
        out_ref[t, :, :half] = sr
        out_ref[t, :, half:] = si
        return (sr, si)

    carry = bwd_step(steps - 1, (er, ei), True)
    lax.fori_loop(0, steps - 1, lambda j, c: bwd_step(steps - 2 - j, c, False), carry, unroll=8)

    e_copy.wait()
    o_copy.wait()
    contract = (((1,), (1,)), ((), ()))
    for a in range(e_ref.shape[0]):
        stacked = out_ref[:, a, :]
        states = dot3(e_ref[a], stacked, contract)
        states_ref[a] = states.astype(states_ref.dtype)
        seen = dot3(o_ref[a], stacked, contract)
        fitted_ref[a] = (d_ref[a] - seen).astype(fitted_ref.dtype)


def gathered_over(spread, axis):
    return lax.all_to_all(spread, axis, 0, 0, tiled=False)


def on_device(
    sampled_data,
    update_weights,
    eigenbasis_columns,
    measuring_operator,
    eigen_damping,
    backward_damping,
    rotation_angle,
    switch_flags,
    prior_expectation,
):
    steps = sampled_data.shape[2]
    seg_index = lax.axis_index("seg")
    blk_index = lax.axis_index("blk")
    last = ((seg_index == lax.axis_size("seg") - 1) & (blk_index == lax.axis_size("blk") - 1))
    last = last.astype(jnp.int32).reshape(1)
    flags = switch_flags.astype(jnp.int32)

    u_shape = (steps, sampled_data.shape[0], sampled_data.shape[1])
    rates = (eigen_damping, backward_damping, rotation_angle)
    rate_scratch = pltpu.VMEM((3,) + eigen_damping.shape, jnp.float32)

    mode_shape = eigen_damping.shape[1:]
    summary = pl.pallas_call(
        summary_kernel,
        out_shape=jax.ShapeDtypeStruct((lax.axis_size("blk"), 10) + mode_shape, jnp.float32),
        in_specs=[pl.BlockSpec(memory_space=SMEM)] * 2 + [pl.BlockSpec(memory_space=VMEM)] * 2
        + [pl.BlockSpec(memory_space=pl.ANY)] * 3,
        out_specs=pl.BlockSpec(memory_space=VMEM),
        scratch_shapes=[pltpu.VMEM(u_shape, jnp.float32), rate_scratch, pltpu.SemaphoreType.DMA((3,))],
    )(flags, last, update_weights, sampled_data, *rates)

    gathered = gathered_over(summary, "blk")
    count = gathered.shape[0]
    tot, mine = pl.pallas_call(
        segment_kernel,
        out_shape=(
            jax.ShapeDtypeStruct((lax.axis_size("seg"), 10) + mode_shape, jnp.float32),
            jax.ShapeDtypeStruct((10,) + mode_shape, jnp.float32),
        ),
        in_specs=[pl.BlockSpec(memory_space=SMEM), pl.BlockSpec(memory_space=VMEM)],
        out_specs=(pl.BlockSpec(memory_space=VMEM), pl.BlockSpec(memory_space=VMEM)),
        scratch_shapes=[pltpu.VMEM((count,) + mode_shape, jnp.float32) for _ in range(4)]
        + [pltpu.VMEM((count, 6) + mode_shape, jnp.float32)],
    )(blk_index.astype(jnp.int32).reshape(1), gathered)

    seg_tot = gathered_over(tot, "seg")
    out_block = jax.ShapeDtypeStruct(sampled_data.shape, jnp.bfloat16)
    states, fitted = pl.pallas_call(
        final_kernel,
        out_shape=(out_block, out_block),
        in_specs=[pl.BlockSpec(memory_space=SMEM)] * 3 + [pl.BlockSpec(memory_space=VMEM)] * 5
        + [pl.BlockSpec(memory_space=pl.ANY)] * 5,
        out_specs=(pl.BlockSpec(memory_space=VMEM), pl.BlockSpec(memory_space=VMEM)),
        scratch_shapes=[pltpu.VMEM(u_shape, jnp.float32)]
        + [pltpu.VMEM((steps,) + mode_shape, jnp.float32) for _ in range(2)]
        + [pltpu.VMEM(u_shape, jnp.float32)]
        + [pltpu.VMEM(eigenbasis_columns.shape, jnp.float32) for _ in range(2)]
        + [rate_scratch, pltpu.SemaphoreType.DMA((5,))],
    )(flags, last, seg_index.astype(jnp.int32).reshape(1), seg_tot, mine, prior_expectation,
      update_weights, sampled_data, eigenbasis_columns, measuring_operator, *rates)
    return (states, fitted)


def solution(mesh):
    placed = (
        P(None, None, ("seg", "blk")),
        P(),
        P(),
        P(),
        P(("seg", "blk"), None, None),
        P(("seg", "blk"), None, None),
        P(("seg", "blk"), None, None),
        P(("seg", "blk")),
        P(),
    )
    return jax.shard_map(
        on_device,
        mesh=mesh,
        in_specs=placed,
        out_specs=(P(None, None, ("seg", "blk")), P(None, None, ("seg", "blk"))),
        check_vma=False,
    )
```

```python
import math

import jax
import jax.numpy as jnp
from jax import lax
from jax.experimental import pallas as pl
from jax.experimental.pallas import tpu as pltpu
from jax.sharding import PartitionSpec as P

spike_multiplier = 0.7

VMEM = pltpu.VMEM
SMEM = pltpu.SMEM


def cmul(ar, ai, br, bi):
    return ar * br - ai * bi, ar * bi + ai * br


def factor_of(flag):
    return jnp.where(flag == 1, jnp.float32(spike_multiplier), jnp.float32(1.0))


LOG_SPIKE_TWICE = 2.0 * math.log(spike_multiplier)


def expm1(x):
    small = jnp.abs(x) < 0.5
    xs = jnp.where(small, x, 0.0)
    p = jnp.ones_like(x)
    for k in range(12, 1, -1):
        p = 1.0 + (xs * jnp.float32(1.0 / k)) * p
    return jnp.where(small, xs * p, jnp.exp(x) - 1.0)


def mode_params(fd, bd, th):
    mag = jnp.exp(-fd)
    smag = jnp.exp(-bd)
    cos, sin = jnp.cos(th), jnp.sin(th)
    both = fd + bd
    return (
        mag * cos,
        mag * sin,
        smag * cos,
        -(smag * sin),
        -expm1(-both),
        -expm1(jnp.float32(LOG_SPIKE_TWICE) - both),
        jnp.sqrt(-expm1(-2.0 * fd)),
    )


def start_rate_copies(rate_hbm, rate_ref, sems, first):
    copies = [pltpu.make_async_copy(rate_hbm[i], rate_ref.at[i], sems.at[first + i]) for i in range(3)]
    for c in copies:
        c.start()
    return copies


def split_bf16(x):
    high = x.astype(jnp.bfloat16)
    low = (x - high.astype(jnp.float32)).astype(jnp.bfloat16)
    return high, low


def dot3(x, y, dims):
    xh, xl = split_bf16(x)
    yh, yl = split_bf16(y)

    def one(p, q):
        return lax.dot_general(p, q, dims, preferred_element_type=jnp.float32)

    return one(xh, yh) + (one(xh, yl) + one(xl, yh))


def fill_drive(w_ref, d_ref, u_ref):
    for a in range(w_ref.shape[0]):
        u_ref[:, a, :] = dot3(d_ref[a], w_ref[a], (((0,), (1,)), ((), ())))


def summary_kernel(flags_ref, last_ref, w_ref, d_ref, fd_hbm, bd_hbm, th_hbm, out_ref, u_ref,
                   rate_ref, sems):
    copies = start_rate_copies((fd_hbm, bd_hbm, th_hbm), rate_ref, sems, 0)
    fill_drive(w_ref, d_ref, u_ref)
    for c in copies:
        c.wait()
    steps = u_ref.shape[0]
    half = u_ref.shape[2] // 2
    lam_r, lam_i, bk_r, bk_i, w_plain, w_spike, scale = mode_params(
        rate_ref[0, 0], rate_ref[1, 0], rate_ref[2, 0])
    zero = jnp.zeros_like(lam_r)
    one = jnp.ones_like(lam_r)

    def step(t, carry, final):
        mr, mi, ar, ai, pr, pi, qr, qi, hr, hi = carry
        flag = flags_ref[t]
        f = factor_of(flag)
        lr, li = f * lam_r, f * lam_i
        u = u_ref[t]
        mr, mi = lr * mr - li * mi + scale * u[:, :half], lr * mi + li * mr + scale * u[:, half:]
        ar, ai = cmul(lr, li, ar, ai)
        w = jnp.where(flag == 1, w_spike, w_plain)
        br, bi = f * bk_r, f * bk_i
        if final:
            last = last_ref[0] == 1
            w = jnp.where(last, one, w)
            br = jnp.where(last, zero, br)
            bi = jnp.where(last, zero, bi)
        wmr, wmi = w * mr, w * mi
        war, wai = w * ar, w * ai
        tr, ti = cmul(hr, hi, wmr, wmi)
        pr, pi = pr + tr, pi + ti
        tr, ti = cmul(hr, hi, war, wai)
        qr, qi = qr + tr, qi + ti
        hr, hi = cmul(br, bi, hr, hi)
        return (mr, mi, ar, ai, pr, pi, qr, qi, hr, hi)

    carry = (zero, zero, one, zero, zero, zero, zero, zero, one, zero)
    carry = lax.fori_loop(0, steps - 1, lambda t, c: step(t, c, False), carry, unroll=8)
    carry = step(steps - 1, carry, True)
    mr, mi, ar, ai, pr, pi, qr, qi, hr, hi = carry
    for idx, v in enumerate((ar, ai, mr, mi, hr, hi, pr, pi, qr, qi)):
        for k in range(out_ref.shape[0]):
            out_ref[k, idx] = v


def segment_kernel(me_ref, g_ref, tot_ref, mine_ref, al_r, al_i, be_r, be_i):
    count = g_ref.shape[0]
    me = me_ref[0]
    zero = jnp.zeros(g_ref.shape[2:], jnp.float32)
    one = jnp.ones_like(zero)

    ar, ai, br, bi = one, zero, zero, zero
    rec = [one, zero, zero, zero]
    for k in range(count):
        sel = me == k
        rec = [jnp.where(sel, v, r) for v, r in zip((ar, ai, br, bi), rec)]
        al_r[k], al_i[k], be_r[k], be_i[k] = ar, ai, br, bi
        Ar, Ai, Br, Bi = g_ref[k, 0], g_ref[k, 1], g_ref[k, 2], g_ref[k, 3]
        ar, ai = cmul(Ar, Ai, ar, ai)
        nr, ni = cmul(Ar, Ai, br, bi)
        br, bi = nr + Br, ni + Bi
    fwd_tot = (ar, ai, br, bi)
    fwd_me = rec

    gr, gi, pr, pi, kr, ki = one, zero, zero, zero, zero, zero
    rec = [one, zero, zero, zero, zero, zero]
    for k in reversed(range(count)):
        sel = me == k
        rec = [jnp.where(sel, v, r) for v, r in zip((gr, gi, pr, pi, kr, ki), rec)]
        Gr, Gi = g_ref[k, 4], g_ref[k, 5]
        Pr, Pi = g_ref[k, 6], g_ref[k, 7]
        Qr, Qi = g_ref[k, 8], g_ref[k, 9]
        xr, xi = cmul(Qr, Qi, be_r[k], be_i[k])
        yr, yi = cmul(Qr, Qi, al_r[k], al_i[k])
        gr, gi = cmul(Gr, Gi, gr, gi)
        nr, ni = cmul(Gr, Gi, pr, pi)
        pr, pi = nr + Pr + xr, ni + Pi + xi
        nr, ni = cmul(Gr, Gi, kr, ki)
        kr, ki = nr + yr, ni + yi
    bwd_tot = (gr, gi, pr, pi, kr, ki)
    bwd_me = rec
    for idx, v in enumerate(fwd_tot + bwd_tot):
        for s in range(tot_ref.shape[0]):
            tot_ref[s, idx] = v
    for idx, v in enumerate(list(fwd_me) + list(bwd_me)):
        mine_ref[idx] = v


def final_kernel(flags_ref, last_ref, myseg_ref, tot_ref, mine_ref, prior_ref, w_ref, d_ref, e_hbm,
                 o_hbm, fd_hbm, bd_hbm, th_hbm, states_hbm, fitted_hbm, u_ref, m_r, m_i, out_ref, e_ref,
                 o_ref, rate_ref, states_ref, fitted_ref, sems):
    e_copy = pltpu.make_async_copy(e_hbm, e_ref, sems.at[0])
    o_copy = pltpu.make_async_copy(o_hbm, o_ref, sems.at[1])
    e_copy.start()
    o_copy.start()
    copies = start_rate_copies((fd_hbm, bd_hbm, th_hbm), rate_ref, sems, 2)
    fill_drive(w_ref, d_ref, u_ref)
    steps = u_ref.shape[0]
    half = u_ref.shape[2] // 2
    segs = tot_ref.shape[0]
    myseg = myseg_ref[0]
    zero = jnp.zeros(prior_ref.shape[1:], jnp.float32)
    one = jnp.ones_like(zero)

    cr, ci = prior_ref[0], prior_ref[1]
    c_in = []
    c_my = [zero, zero]
    for s in range(segs):
        c_in.append((cr, ci))
        sel = myseg == s
        c_my = [jnp.where(sel, cr, c_my[0]), jnp.where(sel, ci, c_my[1])]
        Ar, Ai, Br, Bi = tot_ref[s, 0], tot_ref[s, 1], tot_ref[s, 2], tot_ref[s, 3]
        nr, ni = cmul(Ar, Ai, cr, ci)
        cr, ci = nr + Br, ni + Bi
    er, ei = zero, zero
    e_my = [zero, zero]
    for s in reversed(range(segs)):
        sel = myseg == s
        e_my = [jnp.where(sel, er, e_my[0]), jnp.where(sel, ei, e_my[1])]
        Gr, Gi = tot_ref[s, 4], tot_ref[s, 5]
        Pr, Pi = tot_ref[s, 6], tot_ref[s, 7]
        Kr, Ki = tot_ref[s, 8], tot_ref[s, 9]
        nr, ni = cmul(Gr, Gi, er, ei)
        xr, xi = cmul(Kr, Ki, c_in[s][0], c_in[s][1])
        er, ei = nr + Pr + xr, ni + Pi + xi
    nr, ni = cmul(mine_ref[0], mine_ref[1], c_my[0], c_my[1])
    cr, ci = nr + mine_ref[2], ni + mine_ref[3]
    nr, ni = cmul(mine_ref[4], mine_ref[5], e_my[0], e_my[1])
    xr, xi = cmul(mine_ref[8], mine_ref[9], c_my[0], c_my[1])
    er, ei = nr + mine_ref[6] + xr, ni + mine_ref[7] + xi

    for c in copies:
        c.wait()
    lam_r, lam_i, bk_r, bk_i, w_plain, w_spike, scale = mode_params(
        rate_ref[0, 0], rate_ref[1, 0], rate_ref[2, 0])

    def fwd(t, carry):
        mr, mi = carry
        f = factor_of(flags_ref[t])
        lr, li = f * lam_r, f * lam_i
        u = u_ref[t]
        mr, mi = lr * mr - li * mi + scale * u[:, :half], lr * mi + li * mr + scale * u[:, half:]
        m_r[t] = mr
        m_i[t] = mi
        return (mr, mi)

    lax.fori_loop(0, steps, fwd, (cr, ci), unroll=8)

    def bwd_step(t, carry, final):
        sr, si = carry
        flag = flags_ref[t]
        f = factor_of(flag)
        w = jnp.where(flag == 1, w_spike, w_plain)
        br, bi = f * bk_r, f * bk_i
        if final:
            last = last_ref[0] == 1
            w = jnp.where(last, one, w)
            br = jnp.where(last, zero, br)
            bi = jnp.where(last, zero, bi)
        nr, ni = cmul(br, bi, sr, si)
        sr, si = nr + w * m_r[t], ni + w * m_i[t]
        out_ref[t, :, :half] = sr
        out_ref[t, :, half:] = si
        return (sr, si)

    carry = bwd_step(steps - 1, (er, ei), True)
    lax.fori_loop(0, steps - 1, lambda j, c: bwd_step(steps - 2 - j, c, False), carry, unroll=8)

    e_copy.wait()
    o_copy.wait()
    contract = (((1,), (1,)), ((), ()))
    written = []
    for a in range(e_ref.shape[0]):
        stacked = out_ref[:, a, :]
        states = dot3(e_ref[a], stacked, contract)
        states_ref[a] = states.astype(states_ref.dtype)
        seen = dot3(o_ref[a], stacked, contract)
        fitted_ref[a] = (d_ref[a] - seen).astype(fitted_ref.dtype)
        for c in (pltpu.make_async_copy(states_ref.at[a], states_hbm.at[a], sems.at[5 + 2 * a]),
                  pltpu.make_async_copy(fitted_ref.at[a], fitted_hbm.at[a], sems.at[6 + 2 * a])):
            c.start()
            written.append(c)
    for c in written:
        c.wait()


def gathered_over(spread, axis):
    return lax.all_to_all(spread, axis, 0, 0, tiled=False)


def on_device(
    sampled_data,
    update_weights,
    eigenbasis_columns,
    measuring_operator,
    eigen_damping,
    backward_damping,
    rotation_angle,
    switch_flags,
    prior_expectation,
):
    steps = sampled_data.shape[2]
    seg_index = lax.axis_index("seg")
    blk_index = lax.axis_index("blk")
    last = ((seg_index == lax.axis_size("seg") - 1) & (blk_index == lax.axis_size("blk") - 1))
    last = last.astype(jnp.int32).reshape(1)
    flags = switch_flags.astype(jnp.int32)

    u_shape = (steps, sampled_data.shape[0], sampled_data.shape[1])
    rates = (eigen_damping, backward_damping, rotation_angle)
    rate_scratch = pltpu.VMEM((3,) + eigen_damping.shape, jnp.float32)

    mode_shape = eigen_damping.shape[1:]
    summary = pl.pallas_call(
        summary_kernel,
        out_shape=jax.ShapeDtypeStruct((lax.axis_size("blk"), 10) + mode_shape, jnp.float32),
        in_specs=[pl.BlockSpec(memory_space=SMEM)] * 2 + [pl.BlockSpec(memory_space=VMEM)] * 2
        + [pl.BlockSpec(memory_space=pl.ANY)] * 3,
        out_specs=pl.BlockSpec(memory_space=VMEM),
        scratch_shapes=[pltpu.VMEM(u_shape, jnp.float32), rate_scratch, pltpu.SemaphoreType.DMA((3,))],
    )(flags, last, update_weights, sampled_data, *rates)

    gathered = gathered_over(summary, "blk")
    count = gathered.shape[0]
    tot, mine = pl.pallas_call(
        segment_kernel,
        out_shape=(
            jax.ShapeDtypeStruct((lax.axis_size("seg"), 10) + mode_shape, jnp.float32),
            jax.ShapeDtypeStruct((10,) + mode_shape, jnp.float32),
        ),
        in_specs=[pl.BlockSpec(memory_space=SMEM), pl.BlockSpec(memory_space=VMEM)],
        out_specs=(pl.BlockSpec(memory_space=VMEM), pl.BlockSpec(memory_space=VMEM)),
        scratch_shapes=[pltpu.VMEM((count,) + mode_shape, jnp.float32) for _ in range(4)],
    )(blk_index.astype(jnp.int32).reshape(1), gathered)

    seg_tot = gathered_over(tot, "seg")
    out_block = jax.ShapeDtypeStruct(sampled_data.shape, jnp.bfloat16)
    states, fitted = pl.pallas_call(
        final_kernel,
        out_shape=(out_block, out_block),
        in_specs=[pl.BlockSpec(memory_space=SMEM)] * 3 + [pl.BlockSpec(memory_space=VMEM)] * 5
        + [pl.BlockSpec(memory_space=pl.ANY)] * 5,
        out_specs=(pl.BlockSpec(memory_space=pl.ANY), pl.BlockSpec(memory_space=pl.ANY)),
        scratch_shapes=[pltpu.VMEM(u_shape, jnp.float32)]
        + [pltpu.VMEM((steps,) + mode_shape, jnp.float32) for _ in range(2)]
        + [pltpu.VMEM(u_shape, jnp.float32)]
        + [pltpu.VMEM(eigenbasis_columns.shape, jnp.float32) for _ in range(2)]
        + [rate_scratch]
        + [pltpu.VMEM(sampled_data.shape, jnp.bfloat16) for _ in range(2)]
        + [pltpu.SemaphoreType.DMA((13,))],
    )(flags, last, seg_index.astype(jnp.int32).reshape(1), seg_tot, mine, prior_expectation,
      update_weights, sampled_data, eigenbasis_columns, measuring_operator, *rates)
    return (states, fitted)


def solution(mesh):
    placed = (
        P(None, None, ("seg", "blk")),
        P(),
        P(),
        P(),
        P(("seg", "blk"), None, None),
        P(("seg", "blk"), None, None),
        P(("seg", "blk"), None, None),
        P(("seg", "blk")),
        P(),
    )
    return jax.shard_map(
        on_device,
        mesh=mesh,
        in_specs=placed,
        out_specs=(P(None, None, ("seg", "blk")), P(None, None, ("seg", "blk"))),
        check_vma=False,
    )
```

```python
import math

import jax
import jax.numpy as jnp
from jax import lax
from jax.experimental import pallas as pl
from jax.experimental.pallas import tpu as pltpu
from jax.sharding import PartitionSpec as P

spike_multiplier = 0.7

VMEM = pltpu.VMEM
SMEM = pltpu.SMEM


def cmul(ar, ai, br, bi):
    return ar * br - ai * bi, ar * bi + ai * br


def factor_of(flag):
    return jnp.where(flag == 1, jnp.float32(spike_multiplier), jnp.float32(1.0))


LOG_SPIKE_TWICE = 2.0 * math.log(spike_multiplier)


def expm1(x):
    small = jnp.abs(x) < 0.5
    xs = jnp.where(small, x, 0.0)
    p = jnp.ones_like(x)
    for k in range(12, 1, -1):
        p = 1.0 + (xs * jnp.float32(1.0 / k)) * p
    return jnp.where(small, xs * p, jnp.exp(x) - 1.0)


def mode_params(fd, bd, th):
    mag = jnp.exp(-fd)
    smag = jnp.exp(-bd)
    cos, sin = jnp.cos(th), jnp.sin(th)
    both = fd + bd
    return (
        mag * cos,
        mag * sin,
        smag * cos,
        -(smag * sin),
        -expm1(-both),
        -expm1(jnp.float32(LOG_SPIKE_TWICE) - both),
        jnp.sqrt(-expm1(-2.0 * fd)),
    )


def start_rate_copies(rate_hbm, rate_ref, sems, first):
    copies = [pltpu.make_async_copy(rate_hbm[i], rate_ref.at[i], sems.at[first + i]) for i in range(3)]
    for c in copies:
        c.start()
    return copies


def split_bf16(x):
    high = x.astype(jnp.bfloat16)
    low = (x - high.astype(jnp.float32)).astype(jnp.bfloat16)
    return high, low


def dot3(x, y, dims):
    xh, xl = split_bf16(x)
    yh, yl = split_bf16(y)

    def one(p, q):
        return lax.dot_general(p, q, dims, preferred_element_type=jnp.float32)

    return one(xh, yh) + (one(xh, yl) + one(xl, yh))


def fill_drive(w_ref, d_ref, u_ref):
    for a in range(w_ref.shape[0]):
        u_ref[:, a, :] = dot3(d_ref[a], w_ref[a], (((0,), (1,)), ((), ())))


def summary_kernel(flags_ref, last_ref, w_ref, d_ref, fd_hbm, bd_hbm, th_hbm, out_ref, u_ref,
                   rate_ref, sems):
    copies = start_rate_copies((fd_hbm, bd_hbm, th_hbm), rate_ref, sems, 0)
    fill_drive(w_ref, d_ref, u_ref)
    for c in copies:
        c.wait()
    steps = u_ref.shape[0]
    half = u_ref.shape[2] // 2
    lam_r, lam_i, bk_r, bk_i, w_plain, w_spike, scale = mode_params(
        rate_ref[0, 0], rate_ref[1, 0], rate_ref[2, 0])
    zero = jnp.zeros_like(lam_r)
    one = jnp.ones_like(lam_r)

    def step(t, carry, final):
        mr, mi, ar, ai, pr, pi, qr, qi, hr, hi = carry
        flag = flags_ref[t]
        f = factor_of(flag)
        lr, li = f * lam_r, f * lam_i
        u = u_ref[t]
        mr, mi = lr * mr - li * mi + scale * u[:, :half], lr * mi + li * mr + scale * u[:, half:]
        ar, ai = cmul(lr, li, ar, ai)
        w = jnp.where(flag == 1, w_spike, w_plain)
        br, bi = f * bk_r, f * bk_i
        if final:
            last = last_ref[0] == 1
            w = jnp.where(last, one, w)
            br = jnp.where(last, zero, br)
            bi = jnp.where(last, zero, bi)
        wmr, wmi = w * mr, w * mi
        war, wai = w * ar, w * ai
        tr, ti = cmul(hr, hi, wmr, wmi)
        pr, pi = pr + tr, pi + ti
        tr, ti = cmul(hr, hi, war, wai)
        qr, qi = qr + tr, qi + ti
        hr, hi = cmul(br, bi, hr, hi)
        return (mr, mi, ar, ai, pr, pi, qr, qi, hr, hi)

    carry = (zero, zero, one, zero, zero, zero, zero, zero, one, zero)
    carry = lax.fori_loop(0, steps - 1, lambda t, c: step(t, c, False), carry, unroll=8)
    carry = step(steps - 1, carry, True)
    mr, mi, ar, ai, pr, pi, qr, qi, hr, hi = carry
    for idx, v in enumerate((ar, ai, mr, mi, hr, hi, pr, pi, qr, qi)):
        for k in range(out_ref.shape[0]):
            out_ref[k, idx] = v


def segment_kernel(me_ref, g_ref, tot_ref, mine_ref, al_r, al_i, be_r, be_i, back_ref):
    count = g_ref.shape[0]
    me = me_ref[0]
    zero = jnp.zeros(g_ref.shape[2:], jnp.float32)
    one = jnp.ones_like(zero)

    ar, ai, br, bi = one, zero, zero, zero
    for k in range(count):
        al_r[k], al_i[k], be_r[k], be_i[k] = ar, ai, br, bi
        Ar, Ai, Br, Bi = g_ref[k, 0], g_ref[k, 1], g_ref[k, 2], g_ref[k, 3]
        ar, ai = cmul(Ar, Ai, ar, ai)
        nr, ni = cmul(Ar, Ai, br, bi)
        br, bi = nr + Br, ni + Bi
    fwd_tot = (ar, ai, br, bi)
    fwd_me = [al_r[me], al_i[me], be_r[me], be_i[me]]

    gr, gi, pr, pi, kr, ki = one, zero, zero, zero, zero, zero
    for k in reversed(range(count)):
        for idx, v in enumerate((gr, gi, pr, pi, kr, ki)):
            back_ref[k, idx] = v
        Gr, Gi = g_ref[k, 4], g_ref[k, 5]
        Pr, Pi = g_ref[k, 6], g_ref[k, 7]
        Qr, Qi = g_ref[k, 8], g_ref[k, 9]
        xr, xi = cmul(Qr, Qi, be_r[k], be_i[k])
        yr, yi = cmul(Qr, Qi, al_r[k], al_i[k])
        gr, gi = cmul(Gr, Gi, gr, gi)
        nr, ni = cmul(Gr, Gi, pr, pi)
        pr, pi = nr + Pr + xr, ni + Pi + xi
        nr, ni = cmul(Gr, Gi, kr, ki)
        kr, ki = nr + yr, ni + yi
    bwd_tot = (gr, gi, pr, pi, kr, ki)
    mine_back = back_ref[me]
    bwd_me = [mine_back[idx] for idx in range(6)]
    for idx, v in enumerate(fwd_tot + bwd_tot):
        for s in range(tot_ref.shape[0]):
            tot_ref[s, idx] = v
    for idx, v in enumerate(list(fwd_me) + list(bwd_me)):
        mine_ref[idx] = v


def final_kernel(flags_ref, last_ref, myseg_ref, tot_ref, mine_ref, prior_ref, w_ref, d_ref, e_hbm,
                 o_hbm, fd_hbm, bd_hbm, th_hbm, states_hbm, fitted_hbm, u_ref, m_r, m_i, out_ref, e_ref,
                 o_ref, rate_ref, states_ref, fitted_ref, sems):
    e_copy = pltpu.make_async_copy(e_hbm, e_ref, sems.at[0])
    o_copy = pltpu.make_async_copy(o_hbm, o_ref, sems.at[1])
    e_copy.start()
    o_copy.start()
    copies = start_rate_copies((fd_hbm, bd_hbm, th_hbm), rate_ref, sems, 2)
    fill_drive(w_ref, d_ref, u_ref)
    steps = u_ref.shape[0]
    half = u_ref.shape[2] // 2
    segs = tot_ref.shape[0]
    myseg = myseg_ref[0]
    zero = jnp.zeros(prior_ref.shape[1:], jnp.float32)
    one = jnp.ones_like(zero)

    cr, ci = prior_ref[0], prior_ref[1]
    c_in = []
    c_my = [zero, zero]
    for s in range(segs):
        c_in.append((cr, ci))
        sel = myseg == s
        c_my = [jnp.where(sel, cr, c_my[0]), jnp.where(sel, ci, c_my[1])]
        Ar, Ai, Br, Bi = tot_ref[s, 0], tot_ref[s, 1], tot_ref[s, 2], tot_ref[s, 3]
        nr, ni = cmul(Ar, Ai, cr, ci)
        cr, ci = nr + Br, ni + Bi
    er, ei = zero, zero
    e_my = [zero, zero]
    for s in reversed(range(segs)):
        sel = myseg == s
        e_my = [jnp.where(sel, er, e_my[0]), jnp.where(sel, ei, e_my[1])]
        Gr, Gi = tot_ref[s, 4], tot_ref[s, 5]
        Pr, Pi = tot_ref[s, 6], tot_ref[s, 7]
        Kr, Ki = tot_ref[s, 8], tot_ref[s, 9]
        nr, ni = cmul(Gr, Gi, er, ei)
        xr, xi = cmul(Kr, Ki, c_in[s][0], c_in[s][1])
        er, ei = nr + Pr + xr, ni + Pi + xi
    nr, ni = cmul(mine_ref[0], mine_ref[1], c_my[0], c_my[1])
    cr, ci = nr + mine_ref[2], ni + mine_ref[3]
    nr, ni = cmul(mine_ref[4], mine_ref[5], e_my[0], e_my[1])
    xr, xi = cmul(mine_ref[8], mine_ref[9], c_my[0], c_my[1])
    er, ei = nr + mine_ref[6] + xr, ni + mine_ref[7] + xi

    for c in copies:
        c.wait()
    lam_r, lam_i, bk_r, bk_i, w_plain, w_spike, scale = mode_params(
        rate_ref[0, 0], rate_ref[1, 0], rate_ref[2, 0])

    def fwd(t, carry):
        mr, mi = carry
        f = factor_of(flags_ref[t])
        lr, li = f * lam_r, f * lam_i
        u = u_ref[t]
        mr, mi = lr * mr - li * mi + scale * u[:, :half], lr * mi + li * mr + scale * u[:, half:]
        m_r[t] = mr
        m_i[t] = mi
        return (mr, mi)

    lax.fori_loop(0, steps, fwd, (cr, ci), unroll=8)

    def bwd_step(t, carry, final):
        sr, si = carry
        flag = flags_ref[t]
        f = factor_of(flag)
        w = jnp.where(flag == 1, w_spike, w_plain)
        br, bi = f * bk_r, f * bk_i
        if final:
            last = last_ref[0] == 1
            w = jnp.where(last, one, w)
            br = jnp.where(last, zero, br)
            bi = jnp.where(last, zero, bi)
        nr, ni = cmul(br, bi, sr, si)
        sr, si = nr + w * m_r[t], ni + w * m_i[t]
        out_ref[t, :, :half] = sr
        out_ref[t, :, half:] = si
        return (sr, si)

    carry = bwd_step(steps - 1, (er, ei), True)
    lax.fori_loop(0, steps - 1, lambda j, c: bwd_step(steps - 2 - j, c, False), carry, unroll=8)

    e_copy.wait()
    o_copy.wait()
    contract = (((1,), (1,)), ((), ()))
    written = []
    for a in range(e_ref.shape[0]):
        stacked = out_ref[:, a, :]
        states = dot3(e_ref[a], stacked, contract)
        states_ref[a] = states.astype(states_ref.dtype)
        seen = dot3(o_ref[a], stacked, contract)
        fitted_ref[a] = (d_ref[a] - seen).astype(fitted_ref.dtype)
        for c in (pltpu.make_async_copy(states_ref.at[a], states_hbm.at[a], sems.at[5 + 2 * a]),
                  pltpu.make_async_copy(fitted_ref.at[a], fitted_hbm.at[a], sems.at[6 + 2 * a])):
            c.start()
            written.append(c)
    for c in written:
        c.wait()


def gathered_over(spread, axis):
    return lax.all_to_all(spread, axis, 0, 0, tiled=False)


def on_device(
    sampled_data,
    update_weights,
    eigenbasis_columns,
    measuring_operator,
    eigen_damping,
    backward_damping,
    rotation_angle,
    switch_flags,
    prior_expectation,
):
    steps = sampled_data.shape[2]
    seg_index = lax.axis_index("seg")
    blk_index = lax.axis_index("blk")
    last = ((seg_index == lax.axis_size("seg") - 1) & (blk_index == lax.axis_size("blk") - 1))
    last = last.astype(jnp.int32).reshape(1)
    flags = switch_flags.astype(jnp.int32)

    u_shape = (steps, sampled_data.shape[0], sampled_data.shape[1])
    rates = (eigen_damping, backward_damping, rotation_angle)
    rate_scratch = pltpu.VMEM((3,) + eigen_damping.shape, jnp.float32)

    mode_shape = eigen_damping.shape[1:]
    summary = pl.pallas_call(
        summary_kernel,
        out_shape=jax.ShapeDtypeStruct((lax.axis_size("blk"), 10) + mode_shape, jnp.float32),
        in_specs=[pl.BlockSpec(memory_space=SMEM)] * 2 + [pl.BlockSpec(memory_space=VMEM)] * 2
        + [pl.BlockSpec(memory_space=pl.ANY)] * 3,
        out_specs=pl.BlockSpec(memory_space=VMEM),
        scratch_shapes=[pltpu.VMEM(u_shape, jnp.float32), rate_scratch, pltpu.SemaphoreType.DMA((3,))],
    )(flags, last, update_weights, sampled_data, *rates)

    gathered = gathered_over(summary, "blk")
    count = gathered.shape[0]
    tot, mine = pl.pallas_call(
        segment_kernel,
        out_shape=(
            jax.ShapeDtypeStruct((lax.axis_size("seg"), 10) + mode_shape, jnp.float32),
            jax.ShapeDtypeStruct((10,) + mode_shape, jnp.float32),
        ),
        in_specs=[pl.BlockSpec(memory_space=SMEM), pl.BlockSpec(memory_space=VMEM)],
        out_specs=(pl.BlockSpec(memory_space=VMEM), pl.BlockSpec(memory_space=VMEM)),
        scratch_shapes=[pltpu.VMEM((count,) + mode_shape, jnp.float32) for _ in range(4)]
        + [pltpu.VMEM((count, 6) + mode_shape, jnp.float32)],
    )(blk_index.astype(jnp.int32).reshape(1), gathered)

    seg_tot = gathered_over(tot, "seg")
    out_block = jax.ShapeDtypeStruct(sampled_data.shape, jnp.bfloat16)
    states, fitted = pl.pallas_call(
        final_kernel,
        out_shape=(out_block, out_block),
        in_specs=[pl.BlockSpec(memory_space=SMEM)] * 3 + [pl.BlockSpec(memory_space=VMEM)] * 5
        + [pl.BlockSpec(memory_space=pl.ANY)] * 5,
        out_specs=(pl.BlockSpec(memory_space=pl.ANY), pl.BlockSpec(memory_space=pl.ANY)),
        scratch_shapes=[pltpu.VMEM(u_shape, jnp.float32)]
        + [pltpu.VMEM((steps,) + mode_shape, jnp.float32) for _ in range(2)]
        + [pltpu.VMEM(u_shape, jnp.float32)]
        + [pltpu.VMEM(eigenbasis_columns.shape, jnp.float32) for _ in range(2)]
        + [rate_scratch]
        + [pltpu.VMEM(sampled_data.shape, jnp.bfloat16) for _ in range(2)]
        + [pltpu.SemaphoreType.DMA((13,))],
    )(flags, last, seg_index.astype(jnp.int32).reshape(1), seg_tot, mine, prior_expectation,
      update_weights, sampled_data, eigenbasis_columns, measuring_operator, *rates)
    return (states, fitted)


def solution(mesh):
    placed = (
        P(None, None, ("seg", "blk")),
        P(),
        P(),
        P(),
        P(("seg", "blk"), None, None),
        P(("seg", "blk"), None, None),
        P(("seg", "blk"), None, None),
        P(("seg", "blk")),
        P(),
    )
    return jax.shard_map(
        on_device,
        mesh=mesh,
        in_specs=placed,
        out_specs=(P(None, None, ("seg", "blk")), P(None, None, ("seg", "blk"))),
        check_vma=False,
    )
```
